128 devices in a mesh: face: 2 (over core), elem: 64 (over y, z, x).
Axes of the slice: x: 4, y: 4, z: 4, core: 2. Of those that a mesh axis runs over, the one named last changes fastest.
Arguments:
- state: float32 [432, 32, 8192], P(None, 'face', 'elem'), may hold values from -6 to 6
- speed_x: float32 [432], replicated, may hold values from -0.25 to 0.25
- speed_y: float32 [432], replicated, may hold values from -0.25 to 0.25
- w_in: bfloat16 [512, 432], replicated, may hold values from -0.3125 to 0.3125
- b_in: float32 [512], replicated, may hold values from -1.8 to 1.8
- w_mid: bfloat16 [512, 512], replicated, may hold values from -0.25 to 0.25
- b_mid: float32 [512], replicated, may hold values from -1.8 to 1.8
- w_top: bfloat16 [512, 512], replicated, may hold values from -0.25 to 0.25
- b_top: float32 [512], replicated, may hold values from -1.8 to 1.8
- w_out: bfloat16 [360, 512], replicated, may hold values from -0.25 to 0.25
- b_out: float32 [360], replicated, may hold values from -1.8 to 1.8
- span_of: int32 [2, 64, 2048, 1], P('face', 'elem'), may hold values from 0 to 127; in each aligned block of 2048 rows (0 to 2047, 2048 to 4095, ..., all dimensions but the last counted through in order) at most 32 rows name the same one
Outputs:
- final_state: float32 [432, 32, 8192], P(None, 'face', 'elem')
- tendencies: bfloat16 [360, 32, 8192], P(None, 'face', 'elem')
- span_heating: float32 [128], P(('face', 'elem'))
The draws below stay inside these ranges and needn't reach their ends.
Inputs may be any that keep to these rules, and one draw needn't show every extreme that they name: `span_of`: among the columns of one device, no span is named more than 32 times, a bound that some block reaches; every span is named by some column.
All inputs are finite; a program needn't handle non-finite values.
Results may differ from the reference program's by a relative error of at most 0.0095.
Values may be sent and summed in bfloat16 or wider, within the bound.
No kernel may reach another device: no remote copies, remote signals or barrier semaphores. Data moves between devices by JAX's collectives and lax.ppermute only.
A program may use at most 128 MiB of HBM per device.

```python
import math
import jax
import jax.numpy as jnp
import numpy as np
from jax import lax

NP = 4
LEV = 72
HID = 512
F_IN = 432
F_OUT = 360
PX = 128
PY = 16
NPX = 8192
NPY = 32
COLS_DEV = 2048
CAP = 32
N_FACE = 2
N_ELEM = 64
DEVICES = 128


def block_levels(rng, shape, cuts, low, high):
    def one(axis_at, blocks):
        steps = jax.random.uniform(jax.random.fold_in(jax.random.fold_in(rng, 6), axis_at), (blocks,), jnp.float32, low / len(cuts), high / len(cuts))
        return jnp.repeat(jnp.exp(steps), shape[axis_at] // blocks).reshape((-1,) + (1,) * (len(shape) - axis_at - 1))

    level = one(*cuts[0])
    for cut in cuts[1:]:
        level = level * one(*cut)
    return level


def deal_out(own_key, own, number, rows, amount, top, reach, lean):
    ranking = jax.random.permutation(own_key, amount)
    packed, usual = shares(amount, rows * top, reach, lean, True), shares(amount, rows * top, reach, lean, False)
    places = jnp.arange(amount)

    def named(lengths, turn):
        used = int((lengths > 0).sum())
        fixed = max(1, used // 4)
        moved = fixed + (places - fixed + turn * (used - fixed)) % max(1, amount - fixed)
        return jnp.zeros((amount,), jnp.int32).at[ranking[jnp.where(places < fixed, places, moved)]].set(jnp.asarray(lengths, jnp.int32))

    lengths = jnp.where(number % 4 == 0, named(packed, number // 4), named(usual, number - number // 4 - 1))
    mixed = jax.random.permutation(jax.random.fold_in(own, 3), amount)
    giver, sink = mixed[0:amount // 2 * 2:2], mixed[1:amount // 2 * 2:2]
    slack = jnp.minimum(lengths[giver] - 1, reach - lengths[sink]) // 2
    slack = jnp.where((giver == ranking[0]) | (sink == ranking[0]) | (lengths[sink] == 0), 0, jnp.maximum(slack, 0))
    moved = jax.random.randint(jax.random.fold_in(own, 4), (amount // 2,), 0, 1 << 20) % (slack + 1)
    lengths = lengths.at[giver].add(-moved).at[sink].add(moved)
    items = jnp.searchsorted(jnp.cumsum(lengths), jnp.arange(rows * top), side="right").astype(jnp.int32)
    table = items.reshape(top, rows).T
    table = table[jax.random.permutation(jax.random.fold_in(own, 1), rows)]
    turn = jax.random.randint(jax.random.fold_in(own, 2), (rows, 1), 0, top)
    return jnp.take_along_axis(table, (jnp.arange(top)[None, :] + turn) % top, axis=1)


def shares(amount, total, limit, lean, full):
    portions = [(1 << 20) // math.isqrt(grade ** lean) + 1 for grade in range(1, amount + 1)]
    largest = limit if full else min(limit, max(-(-total // amount), total * portions[0] // sum(portions)))
    least = 1 if total - largest >= amount - 1 else 0
    holding, rest = [largest] + [least] * (amount - 1), total - largest - least * (amount - 1)
    while rest > 0:
        free = [i for i in range(1, amount) if holding[i] < largest] or [i for i in range(1, amount) if holding[i] < limit]
        mass, budget = sum([portions[i] for i in free]), rest
        for i in free:
            extra = min(limit - holding[i], max(1, budget * portions[i] // mass), rest)
            holding[i] = holding[i] + extra
            rest = rest - extra
    return np.array(holding)


def gaussian(own_key, shape, deviation, most, shards=(), dtype=jnp.bfloat16):
    factor_of = block_levels(own_key, shape, shards, -0.22, 0.18) if shards else 1.0
    entries = jax.random.normal(own_key, shape, jnp.float32) * deviation * factor_of
    return jnp.minimum(jnp.maximum(entries, -most), most).astype(dtype)


def setup_inputs(seed: int = 0) -> dict:
    key_list = jax.random.split(jax.random.key(seed), 13)
    state = gaussian(key_list[0], (F_IN, NPY, NPX), 1.0, 6.0, ((1, 2), (2, 64)), jnp.float32)
    speed_x = jnp.clip(jax.random.uniform(key_list[1], (F_IN,), jnp.float32, -0.25, 0.25), -0.25, 0.25)
    speed_y = jnp.clip(jax.random.uniform(key_list[2], (F_IN,), jnp.float32, -0.25, 0.25), -0.25, 0.25)
    w_in = gaussian(key_list[3], (HID, F_IN), F_IN ** -0.5, 0.3125)
    b_in = gaussian(key_list[4], (HID,), 0.3, 1.8, (), jnp.float32)
    w_mid = gaussian(key_list[5], (HID, HID), HID ** -0.5, 0.25)
    b_mid = gaussian(key_list[6], (HID,), 0.3, 1.8, (), jnp.float32)
    w_top = gaussian(key_list[7], (HID, HID), HID ** -0.5, 0.25)
    b_top = gaussian(key_list[8], (HID,), 0.3, 1.8, (), jnp.float32)
    w_out = gaussian(key_list[9], (F_OUT, HID), HID ** -0.5, 0.25)
    b_out = gaussian(key_list[10], (F_OUT,), 0.3, 1.8, (), jnp.float32)
    span_of_keys = jax.random.split(jax.random.fold_in(key_list[11], 1), N_FACE * N_ELEM * COLS_DEV // COLS_DEV)
    span_of_turns = jax.random.permutation(jax.random.fold_in(key_list[11], 3), N_FACE * N_ELEM * COLS_DEV // COLS_DEV)
    span_of = jax.vmap(lambda own, number: deal_out(jax.random.fold_in(key_list[11], 2), own, number, COLS_DEV, DEVICES, 1, CAP, 2))(span_of_keys, span_of_turns).reshape((N_FACE, N_ELEM, COLS_DEV, 1))
    return {"state": state, "speed_x": speed_x, "speed_y": speed_y, "w_in": w_in, "b_in": b_in, "w_mid": w_mid, "b_mid": b_mid, "w_top": w_top, "b_top": b_top, "w_out": w_out, "b_out": b_out, "span_of": span_of}


def gll_matrix():
    inner_node = 1.0 / math.sqrt(5.0)
    gll_nodes = np.array([-1.0, -inner_node, inner_node, 1.0])
    weights = np.array([1.0 / np.prod([gll_nodes[outer] - gll_nodes[other] for other in range(4) if other != outer]) for outer in range(4)])
    matrix = np.zeros((4, 4))
    for outer in range(4):
        for inner in range(4):
            if inner != outer:
                matrix[outer, inner] = weights[inner] / weights[outer] / (gll_nodes[outer] - gll_nodes[inner])
    for outer in range(4):
        matrix[outer, outer] = -np.sum(matrix[outer])
    return matrix.astype(np.float32)

def stiff_x(tendency):
    feats, height, breadth = tendency.shape
    blocks = tendency.reshape(feats, height, breadth // NP, NP)
    first_pts = blocks[..., 0]
    last_pts = blocks[..., NP - 1]
    new_last = 0.5 * (last_pts + jnp.roll(first_pts, -1, axis=2))
    new_first = jnp.roll(new_last, 1, axis=2)
    blocks = blocks.at[..., 0].set(new_first).at[..., NP - 1].set(new_last)
    return blocks.reshape(tendency.shape)

def stiff_y(tendency):
    feats, height, breadth = tendency.shape
    blocks = tendency.reshape(feats, height // NP, NP, breadth)
    first_pts = blocks[:, :, 0, :]
    last_pts = blocks[:, :, NP - 1, :]
    new_last = 0.5 * (last_pts + jnp.roll(first_pts, -1, axis=1))
    new_first = jnp.roll(new_last, 1, axis=1)
    blocks = blocks.at[:, :, 0, :].set(new_first).at[:, :, NP - 1, :].set(new_last)
    return blocks.reshape(tendency.shape)

def operator(field, speed_x, speed_y):
    deriv_table = jnp.asarray(gll_matrix())
    feats, height, breadth = field.shape
    along_x = jnp.einsum('ji,fyei->fyej', deriv_table, field.reshape(feats, height, breadth // NP, NP), precision=lax.Precision.HIGHEST).reshape(field.shape)
    along_y = jnp.einsum('ji,feix->fejx', deriv_table, field.reshape(feats, height // NP, NP, breadth), precision=lax.Precision.HIGHEST).reshape(field.shape)
    tendency = -(speed_x[:, None, None] * along_x + speed_y[:, None, None] * along_y)
    return stiff_y(stiff_x(tendency))

def advance(pieces):
    field, speed_x, speed_y = pieces
    section_one = field + operator(field, speed_x, speed_y)
    section_two = 0.75 * field + 0.25 * (section_one + operator(section_one, speed_x, speed_y))
    return field / 3.0 + 2.0 / 3.0 * (section_two + operator(section_two, speed_x, speed_y))

def column_model(inputs, w_in, b_in, w_mid, b_mid, w_top, b_top, w_out, b_out):
    hidden = jax.nn.silu(jnp.dot(w_in, inputs, preferred_element_type=jnp.float32) + b_in[:, None]).astype(jnp.bfloat16)
    hidden = jax.nn.silu(jnp.dot(w_mid, hidden, preferred_element_type=jnp.float32) + b_mid[:, None]).astype(jnp.bfloat16)
    hidden = jax.nn.silu(jnp.dot(w_top, hidden, preferred_element_type=jnp.float32) + b_top[:, None]).astype(jnp.bfloat16)
    outputs = jnp.dot(w_out, hidden, preferred_element_type=jnp.float32) + b_out[:, None]
    heating = lax.optimization_barrier(jnp.sum(outputs[:LEV], axis=0))
    return (outputs.astype(jnp.bfloat16), heating)

def reference(state, speed_x, speed_y, w_in, b_in, w_mid, b_mid, w_top, b_top, w_out, b_out, span_of):
    feature_block = math.gcd(F_IN, 48)
    groups = F_IN // feature_block
    final_state = lax.map(advance, (state.reshape(groups, feature_block, NPY, NPX), speed_x.reshape(groups, feature_block), speed_y.reshape(groups, feature_block)))
    final_state = final_state.reshape(F_IN, NPY, NPX)
    columns = final_state.reshape(F_IN, N_FACE, PY, N_ELEM, PX).transpose(1, 3, 0, 2, 4).reshape(DEVICES, F_IN, COLS_DEV).astype(jnp.bfloat16)

    def physics(inputs):
        return column_model(inputs, w_in, b_in, w_mid, b_mid, w_top, b_top, w_out, b_out)
    tend_cols, heating = lax.map(physics, columns)
    target = span_of.reshape(DEVICES * COLS_DEV).astype(jnp.int32)
    span_heating = jax.ops.segment_sum(heating.reshape(DEVICES * COLS_DEV), target, DEVICES) / COLS_DEV
    tendencies = tend_cols.reshape(N_FACE, N_ELEM, F_OUT, PY, PX).transpose(2, 0, 3, 1, 4).reshape(F_OUT, NPY, NPX)
    return (final_state, tendencies, span_heating)
```

```python
import math

import jax
import jax.numpy as jnp
import numpy as np
from jax import lax
from jax.sharding import PartitionSpec as P

NP = 4
LEV = 72


def for_sending(array):

    def short(part):
        return part.astype(jnp.bfloat16) if part.dtype == jnp.float32 else part

    return jax.tree.map(short, array)


def with_halo(block, sides, width):
    for axis, dim in sides:
        count = lax.axis_size(axis)
        forward = [(i, i + 1) for i in range(count - 1)]
        forward.append((count - 1, 0))
        backward = [(target, source) for source, target in forward]
        low = lax.ppermute(
            lax.slice_in_dim(block, block.shape[dim] - width, None, axis=dim), axis, forward
        )
        high = lax.ppermute(lax.slice_in_dim(block, 0, width, axis=dim), axis, backward)
        block = jnp.concatenate([low, block, high], axis=dim)
    return block


def gll_matrix():
    inner_node = 1.0 / math.sqrt(5.0)
    gll_nodes = np.array([-1.0, -inner_node, inner_node, 1.0])
    weights = np.array(
        [
            1.0
            / np.prod([gll_nodes[outer] - gll_nodes[other] for other in range(4) if other != outer])
            for outer in range(4)
        ]
    )
    matrix = np.zeros((4, 4))
    for outer in range(4):
        for inner in range(4):
            if inner != outer:
                matrix[outer, inner] = (
                    weights[inner] / weights[outer] / (gll_nodes[outer] - gll_nodes[inner])
                )
    for outer in range(4):
        matrix[outer, outer] = -np.sum(matrix[outer])
    return matrix.astype(np.float32)


def stiff_x(tendency, prev_cols, next_cols):
    place = lax.broadcasted_iota(jnp.int32, (1, 1, tendency.shape[2]), 2) % NP
    averaged_last = 0.5 * (tendency + next_cols)
    averaged_first = 0.5 * (prev_cols + tendency)
    return jnp.where(
        place == NP - 1, averaged_last, jnp.where(place == 0, averaged_first, tendency)
    )


def stiff_y(tendency, prev_rows, next_rows):
    place = lax.broadcasted_iota(jnp.int32, (1, tendency.shape[1], 1), 1) % NP
    averaged_last = 0.5 * (tendency + next_rows)
    averaged_first = 0.5 * (prev_rows + tendency)
    return jnp.where(
        place == NP - 1, averaged_last, jnp.where(place == 0, averaged_first, tendency)
    )


def column_model(inputs, w_in, b_in, w_mid, b_mid, w_top, b_top, w_out, b_out):
    hidden = jax.nn.silu(
        jnp.dot(w_in, inputs, preferred_element_type=jnp.float32) + b_in[:, None]
    ).astype(jnp.bfloat16)
    hidden = jax.nn.silu(
        jnp.dot(w_mid, hidden, preferred_element_type=jnp.float32) + b_mid[:, None]
    ).astype(jnp.bfloat16)
    hidden = jax.nn.silu(
        jnp.dot(w_top, hidden, preferred_element_type=jnp.float32) + b_top[:, None]
    ).astype(jnp.bfloat16)
    outputs = jnp.dot(w_out, hidden, preferred_element_type=jnp.float32) + b_out[:, None]
    heating = jnp.sum(outputs[:LEV], axis=0)
    return (outputs.astype(jnp.bfloat16), heating)


def local(state, speed_x, speed_y, w_in, b_in, w_mid, b_mid, w_top, b_top, w_out, b_out, span_of):
    feats, height, breadth = state.shape
    table = gll_matrix()
    across = jnp.asarray(np.kron(np.eye(breadth // NP, dtype=np.float32), table.T))
    downward = np.kron(np.eye(height // NP, dtype=np.float32), table)
    reach = NP - 1
    offsets = list(range(-reach, reach + 1))
    row_coefs = []
    for offset in offsets:
        column_vals = np.zeros((1, height, 1), dtype=np.float32)
        for row in range(height):
            if 0 <= row + offset < height:
                column_vals[0, row, 0] = downward[row, row + offset]
        row_coefs.append(jnp.asarray(column_vals))

    def operator(field):
        along_x = jnp.dot(
            field.reshape(feats * height, breadth), across, precision=lax.Precision.HIGHEST
        ).reshape(field.shape)
        padded_rows = jnp.pad(field, ((0, 0), (reach, reach), (0, 0)))
        along_y = jnp.zeros_like(field)
        for index, offset in enumerate(offsets):
            along_y = (
                along_y
                + row_coefs[index] * padded_rows[:, reach + offset : reach + offset + height, :]
            )
        tendency = -(speed_x[:, None, None] * along_x + speed_y[:, None, None] * along_y)
        padded = with_halo(for_sending(tendency), (("elem", 2),), 1).astype(tendency.dtype)
        tendency = stiff_x(tendency, padded[:, :, :-2], padded[:, :, 2:])
        padded = with_halo(for_sending(tendency), (("face", 1),), 1).astype(tendency.dtype)
        tendency = stiff_y(tendency, padded[:, :-2, :], padded[:, 2:, :])
        return tendency

    section_one = state + operator(state)
    section_two = 0.75 * state + 0.25 * (section_one + operator(section_one))
    final_state = state / 3.0 + 2.0 / 3.0 * (section_two + operator(section_two))
    column_count = height * breadth
    inputs = final_state.reshape(feats, column_count).astype(jnp.bfloat16)
    target = span_of.reshape(column_count)
    devices = lax.axis_size("face") * lax.axis_size("elem")
    span_ids = jnp.arange(devices, dtype=jnp.int32)
    weights = (w_in, b_in, w_mid, b_mid, w_top, b_top, w_out, b_out)
    tend_cols, heating = column_model(inputs, *weights)
    member = (target[:, None] == span_ids[None, :]).astype(jnp.float32)
    partial_sums = jnp.sum(member * heating[:, None], axis=0)
    received = lax.all_to_all(
        partial_sums.reshape(devices, 1), ("face", "elem"), 0, 1, tiled=True
    )
    span_heating = jnp.sum(received, axis=1) / column_count
    tendencies = tend_cols.reshape(-1, height, breadth)
    return (final_state, tendencies, span_heating)


def solution(mesh):
    return jax.shard_map(
        local,
        mesh=mesh,
        in_specs=(
            P(None, "face", "elem"),
            P(),
            P(),
            P(),
            P(),
            P(),
            P(),
            P(),
            P(),
            P(),
            P(),
            P("face", "elem", None, None),
        ),
        out_specs=(P(None, "face", "elem"), P(None, "face", "elem"), P(("face", "elem"))),
        check_vma=False,
    )
```

```python
import functools
import math

import jax
import jax.numpy as jnp
import numpy as np
from jax import lax
from jax.experimental import pallas as pl
from jax.experimental.pallas import tpu as pltpu
from jax.sharding import PartitionSpec as P

NP = 4
LEV = 72
CHUNK = 48
FOLD = CHUNK // 2


def gll_matrix():
    inner_node = 1.0 / math.sqrt(5.0)
    gll_nodes = np.array([-1.0, -inner_node, inner_node, 1.0])
    weights = np.array(
        [
            1.0
            / np.prod([gll_nodes[outer] - gll_nodes[other] for other in range(4) if other != outer])
            for outer in range(4)
        ]
    )
    matrix = np.zeros((4, 4))
    for outer in range(4):
        for inner in range(4):
            if inner != outer:
                matrix[outer, inner] = (
                    weights[inner] / weights[outer] / (gll_nodes[outer] - gll_nodes[inner])
                )
    for outer in range(4):
        matrix[outer, outer] = -np.sum(matrix[outer])
    return matrix.astype(np.float32)


TABLE = gll_matrix()


def lanes(shape):
    return lax.broadcasted_iota(jnp.int32, shape, len(shape) - 1)


def roll(x, shift):
    shift = shift % x.shape[-1]
    return x if shift == 0 else pltpu.roll(x, shift, x.ndim - 1)


def raw_slabs(slabs, sx, sy, ahi, alo):
    rows = slabs[0].shape[0]
    stacked = jnp.concatenate(slabs, axis=0)
    hi = stacked.astype(jnp.bfloat16)
    lo = (stacked - hi.astype(jnp.float32)).astype(jnp.bfloat16)
    along_x = (
        jnp.dot(hi, ahi, preferred_element_type=jnp.float32)
        + jnp.dot(hi, alo, preferred_element_type=jnp.float32)
        + jnp.dot(lo, ahi, preferred_element_type=jnp.float32)
    )
    out = []
    for y, _ in enumerate(slabs):
        base = (y // NP) * NP
        j = y % NP
        along_y = float(TABLE[j, 0]) * slabs[base]
        for i in range(1, NP):
            along_y = along_y + float(TABLE[j, i]) * slabs[base + i]
        dx = along_x[y * rows : (y + 1) * rows]
        out.append(-(sx * dx + sy * along_y))
    return out


def pack_edges(tend):
    rows, width = tend[0].shape
    lane = lanes((rows, width))
    acc = jnp.zeros((rows, width), jnp.float32)
    for y, t in enumerate(tend):
        acc = jnp.where(lane == 2 * y, roll(t, 2 * y), acc)
        acc = jnp.where(lane == 2 * y + 1, roll(t, 2 * y + 2), acc)
    half = rows // 2
    lane_h = lanes((half, width))
    return jnp.where(lane_h < 32, acc[:half], roll(acc[half:], 32))


def unpack_edges(block):
    return jnp.concatenate([block, roll(block, 96)], axis=0)


def stiff_x(t, right_edges, left_edges, y):
    rows, width = t.shape
    lane = lanes((rows, width))
    right = jnp.where(lane == width - 1, roll(right_edges, width - 1 - 2 * y), roll(t, width - 1))
    left = jnp.where(lane == 0, roll(left_edges, width - 1 - 2 * y), roll(t, 1))
    place = lane % NP
    return jnp.where(
        place == NP - 1, 0.5 * (t + right), jnp.where(place == 0, 0.5 * (left + t), t)
    )


def section_kernel(*refs, first, combo, edges):
    refs = list(refs)
    v0_ref = None if combo is None or combo[0] is None else refs.pop(0)
    sp_ref = refs.pop(0)
    sx_ref, sy_ref, ahi_ref, alo_ref = refs[:4]
    refs = refs[4:]
    if not first:
        exr_ref, exl_ref, dr_ref, dl_ref, eyn_ref = refs[:5]
        refs = refs[5:]
    rows = CHUNK
    height = 16
    sx = sx_ref[...]
    sy = sy_ref[...]
    ahi = ahi_ref[...]
    alo = alo_ref[...]
    slabs = [sp_ref[pl.ds(y, rows, stride=height), :] for y in range(height)]
    tend = raw_slabs(slabs, sx, sy, ahi, alo)
    if first:
        ex_ref, ey_ref = refs
        ex_ref[...] = pack_edges(tend)
        ey_ref[0] = tend[0]
        ey_ref[1] = tend[height - 1]
        return
    exr = unpack_edges(exr_ref[...])
    exl = unpack_edges(exl_ref[...])
    dr = unpack_edges(dr_ref[...])
    dl = unpack_edges(dl_ref[...])
    tx = [stiff_x(t, exr, exl, y) for y, t in enumerate(tend)]
    down = stiff_x(eyn_ref[0], dr, dl, 0)
    up = stiff_x(eyn_ref[1], dr, dl, height - 1)
    ext = [up] + tx + [down]
    new = []
    for y in range(height):
        cur = ext[y + 1]
        if y % NP == NP - 1:
            op = 0.5 * (cur + ext[y + 2])
        elif y % NP == 0:
            op = 0.5 * (ext[y] + cur)
        else:
            op = cur
        inner = slabs[y] + op
        if combo[0] is None:
            val = inner
        else:
            v0 = v0_ref[pl.ds(y, rows, stride=height), :]
            if combo[0] == "third":
                val = v0 / 3.0 + 2.0 / 3.0 * inner
            else:
                val = combo[0] * v0 + combo[1] * inner
        new.append(val)
    out_ref = refs[0]
    for y in range(height):
        out_ref[pl.ds(y, rows, stride=height), :] = new[y]
    if edges:
        ex_ref, ey_ref = refs[1:3]
        tend = raw_slabs(new, sx, sy, ahi, alo)
        ex_ref[...] = pack_edges(tend)
        ey_ref[0] = tend[0]
        ey_ref[1] = tend[height - 1]


def run_section(field_rows, v0, sx, sy, ahi, alo, halos, *, first, combo, edges):
    total, width = field_rows.shape
    feats = sx.shape[0]
    steps = feats // CHUNK
    big = pl.BlockSpec((CHUNK * 16, width), lambda i: (i, 0))
    small = pl.BlockSpec((CHUNK, width), lambda i: (i, 0))
    const = pl.BlockSpec((width, width), lambda i: (0, 0))
    edge = pl.BlockSpec((FOLD, width), lambda i: (i, 0))
    rowsb = pl.BlockSpec((2, CHUNK, width), lambda i: (0, i, 0))
    args, specs = [], []
    if combo is not None and combo[0] is not None:
        args.append(v0)
        specs.append(big)
    args += [field_rows, sx, sy, ahi, alo]
    specs += [big, small, small, const, const]
    if not first:
        args += list(halos)
        specs += [edge, edge, edge, edge, rowsb]
    out_shape, out_specs = [], []
    ex_shape = jax.ShapeDtypeStruct((feats // 2, width), jnp.float32)
    ey_shape = jax.ShapeDtypeStruct((2, feats, width), jnp.float32)
    if first:
        out_shape = [ex_shape, ey_shape]
        out_specs = [edge, rowsb]
    else:
        out_shape = [jax.ShapeDtypeStruct((total, width), jnp.float32)]
        out_specs = [big]
        if edges:
            out_shape += [ex_shape, ey_shape]
            out_specs += [edge, rowsb]
    kernel = functools.partial(section_kernel, first=first, combo=combo, edges=edges)
    return pl.pallas_call(
        kernel,
        grid=(steps,),
        in_specs=specs,
        out_specs=out_specs,
        out_shape=out_shape,
        compiler_params=pltpu.CompilerParams(vmem_limit_bytes=48 * 1024 * 1024),
    )(*args)


def exchange(ex, ey):
    n_face = lax.axis_size("face")
    n_elem = lax.axis_size("elem")
    assert n_face == 2
    from_right = [(j, (j - 1) % n_elem) for j in range(n_elem)]
    from_left = [(j, (j + 1) % n_elem) for j in range(n_elem)]
    exr = lax.ppermute(ex, "elem", from_right)
    exl = lax.ppermute(ex, "elem", from_left)
    eyn = lax.ppermute(ey, "face", [(0, 1), (1, 0)])
    diag_r, diag_l = [], []
    for f in range(n_face):
        for j in range(n_elem):
            src = f * n_elem + j
            diag_r.append((src, (1 - f) * n_elem + (j - 1) % n_elem))
            diag_l.append((src, (1 - f) * n_elem + (j + 1) % n_elem))
    dr = lax.ppermute(ex, ("face", "elem"), diag_r)
    dl = lax.ppermute(ex, ("face", "elem"), diag_l)
    return (exr, exl, dr, dl, eyn)


def column_model(inputs, w_in, b_in, w_mid, b_mid, w_top, b_top, w_out, b_out):
    hidden = jax.nn.silu(
        jnp.dot(w_in, inputs, preferred_element_type=jnp.float32) + b_in[:, None]
    ).astype(jnp.bfloat16)
    hidden = jax.nn.silu(
        jnp.dot(w_mid, hidden, preferred_element_type=jnp.float32) + b_mid[:, None]
    ).astype(jnp.bfloat16)
    hidden = jax.nn.silu(
        jnp.dot(w_top, hidden, preferred_element_type=jnp.float32) + b_top[:, None]
    ).astype(jnp.bfloat16)
    outputs = jnp.dot(w_out, hidden, preferred_element_type=jnp.float32) + b_out[:, None]
    heating = jnp.sum(outputs[:LEV], axis=0)
    return (outputs.astype(jnp.bfloat16), heating)


def local(state, speed_x, speed_y, w_in, b_in, w_mid, b_mid, w_top, b_top, w_out, b_out, span_of):
    feats, height, breadth = state.shape
    across = np.kron(np.eye(breadth // NP, dtype=np.float32), TABLE.T)
    ahi_np = across.astype(jnp.bfloat16)
    alo_np = (across - ahi_np.astype(np.float32)).astype(jnp.bfloat16)
    ahi = jnp.asarray(ahi_np)
    alo = jnp.asarray(alo_np)
    sx = jnp.broadcast_to(speed_x[:, None], (feats, breadth))
    sy = jnp.broadcast_to(speed_y[:, None], (feats, breadth))
    v0 = state.reshape(feats * height, breadth)
    ex, ey = run_section(v0, None, sx, sy, ahi, alo, None, first=True, combo=None, edges=True)
    field = v0
    combos = [(None, None), (0.75, 0.25), ("third", None)]
    for k, combo in enumerate(combos):
        halos = exchange(ex, ey)
        outs = run_section(
            field, v0, sx, sy, ahi, alo, halos, first=False, combo=combo, edges=k < 2
        )
        if k < 2:
            field, ex, ey = outs
        else:
            (field,) = outs
    final_state = field.reshape(feats, height, breadth)
    column_count = height * breadth
    inputs = final_state.reshape(feats, column_count).astype(jnp.bfloat16)
    target = span_of.reshape(column_count)
    devices = lax.axis_size("face") * lax.axis_size("elem")
    span_ids = jnp.arange(devices, dtype=jnp.int32)
    weights = (w_in, b_in, w_mid, b_mid, w_top, b_top, w_out, b_out)
    tend_cols, heating = column_model(inputs, *weights)
    member = (target[:, None] == span_ids[None, :]).astype(jnp.float32)
    partial_sums = jnp.sum(member * heating[:, None], axis=0)
    received = lax.all_to_all(
        partial_sums.reshape(devices, 1), ("face", "elem"), 0, 1, tiled=True
    )
    span_heating = jnp.sum(received, axis=1) / column_count
    tendencies = tend_cols.reshape(-1, height, breadth)
    return (final_state, tendencies, span_heating)


def solution(mesh):
    return jax.shard_map(
        local,
        mesh=mesh,
        in_specs=(
            P(None, "face", "elem"),
            P(),
            P(),
            P(),
            P(),
            P(),
            P(),
            P(),
            P(),
            P(),
            P(),
            P("face", "elem", None, None),
        ),
        out_specs=(P(None, "face", "elem"), P(None, "face", "elem"), P(("face", "elem"))),
        check_vma=False,
    )
```

```python
import functools
import math

import jax
import jax.numpy as jnp
import numpy as np
from jax import lax
from jax.experimental import pallas as pl
from jax.experimental.pallas import tpu as pltpu
from jax.sharding import PartitionSpec as P

NP = 4
LEV = 72
CHUNK = 48
PARTS = 3
FOLD = CHUNK // 2


def gll_matrix():
    inner_node = 1.0 / math.sqrt(5.0)
    gll_nodes = np.array([-1.0, -inner_node, inner_node, 1.0])
    weights = np.array(
        [
            1.0
            / np.prod([gll_nodes[outer] - gll_nodes[other] for other in range(4) if other != outer])
            for outer in range(4)
        ]
    )
    matrix = np.zeros((4, 4))
    for outer in range(4):
        for inner in range(4):
            if inner != outer:
                matrix[outer, inner] = (
                    weights[inner] / weights[outer] / (gll_nodes[outer] - gll_nodes[inner])
                )
    for outer in range(4):
        matrix[outer, outer] = -np.sum(matrix[outer])
    return matrix.astype(np.float32)


TABLE = gll_matrix()


def lanes(shape):
    return lax.broadcasted_iota(jnp.int32, shape, len(shape) - 1)


def roll(x, shift):
    shift = shift % x.shape[-1]
    return x if shift == 0 else pltpu.roll(x, shift, x.ndim - 1)


def raw_slabs(slabs, sx, sy, ahi, alo):
    rows = slabs[0].shape[0]
    stacked = jnp.concatenate(slabs, axis=0)
    hi = stacked.astype(jnp.bfloat16)
    lo = (stacked - hi.astype(jnp.float32)).astype(jnp.bfloat16)
    along_x = (
        jnp.dot(hi, ahi, preferred_element_type=jnp.float32)
        + jnp.dot(hi, alo, preferred_element_type=jnp.float32)
        + jnp.dot(lo, ahi, preferred_element_type=jnp.float32)
    )
    out = []
    for y, _ in enumerate(slabs):
        base = (y // NP) * NP
        j = y % NP
        along_y = float(TABLE[j, 0]) * slabs[base]
        for i in range(1, NP):
            along_y = along_y + float(TABLE[j, i]) * slabs[base + i]
        dx = along_x[y * rows : (y + 1) * rows]
        out.append(-(sx * dx + sy * along_y))
    return out


def pack_edges(tend):
    rows, width = tend[0].shape
    lane = lanes((rows, width))
    acc = jnp.zeros((rows, width), jnp.float32)
    for y, t in enumerate(tend):
        acc = jnp.where(lane == 2 * y, roll(t, 2 * y), acc)
        acc = jnp.where(lane == 2 * y + 1, roll(t, 2 * y + 2), acc)
    half = rows // 2
    lane_h = lanes((half, width))
    return jnp.where(lane_h < 32, acc[:half], roll(acc[half:], 32))


def unpack_edges(block):
    return jnp.concatenate([block, roll(block, 96)], axis=0)


def stiff_x(t, right_edges, left_edges, y):
    rows, width = t.shape
    lane = lanes((rows, width))
    right = jnp.where(lane == width - 1, roll(right_edges, width - 1 - 2 * y), roll(t, width - 1))
    left = jnp.where(lane == 0, roll(left_edges, width - 1 - 2 * y), roll(t, 1))
    place = lane % NP
    return jnp.where(
        place == NP - 1, 0.5 * (t + right), jnp.where(place == 0, 0.5 * (left + t), t)
    )


def section_kernel(*refs, first, combo, edges):
    refs = list(refs)
    v0_ref = None if combo is None or combo[0] is None else refs.pop(0)
    sp_ref = refs.pop(0)
    sx_ref, sy_ref, ahi_ref, alo_ref = refs[:4]
    refs = refs[4:]
    if not first:
        exr_ref, exl_ref, dr_ref, dl_ref, eyn_ref = refs[:5]
        refs = refs[5:]
    rows = CHUNK
    height = 16
    sx = sx_ref[...]
    sy = sy_ref[...]
    ahi = ahi_ref[...]
    alo = alo_ref[...]
    slabs = [sp_ref[pl.ds(y, rows, stride=height), :] for y in range(height)]
    tend = raw_slabs(slabs, sx, sy, ahi, alo)
    if first:
        ex_ref, ey_ref = refs
        ex_ref[...] = pack_edges(tend)
        ey_ref[0] = tend[0]
        ey_ref[1] = tend[height - 1]
        return
    exr = unpack_edges(exr_ref[...])
    exl = unpack_edges(exl_ref[...])
    dr = unpack_edges(dr_ref[...])
    dl = unpack_edges(dl_ref[...])
    tx = [stiff_x(t, exr, exl, y) for y, t in enumerate(tend)]
    down = stiff_x(eyn_ref[0], dr, dl, 0)
    up = stiff_x(eyn_ref[1], dr, dl, height - 1)
    ext = [up] + tx + [down]
    new = []
    for y in range(height):
        cur = ext[y + 1]
        if y % NP == NP - 1:
            op = 0.5 * (cur + ext[y + 2])
        elif y % NP == 0:
            op = 0.5 * (ext[y] + cur)
        else:
            op = cur
        inner = slabs[y] + op
        if combo[0] is None:
            val = inner
        else:
            v0 = v0_ref[pl.ds(y, rows, stride=height), :]
            if combo[0] == "third":
                val = v0 / 3.0 + 2.0 / 3.0 * inner
            else:
                val = combo[0] * v0 + combo[1] * inner
        new.append(val)
    out_ref = refs[0]
    for y in range(height):
        out_ref[pl.ds(y, rows, stride=height), :] = new[y]
    if edges:
        ex_ref, ey_ref = refs[1:3]
        tend = raw_slabs(new, sx, sy, ahi, alo)
        ex_ref[...] = pack_edges(tend)
        ey_ref[0] = tend[0]
        ey_ref[1] = tend[height - 1]


def run_section(field, field_at, v0, sx, sy, ahi, alo, halos, *, at, steps, first, combo, edges):
    width = field.shape[1]
    feats = steps * CHUNK

    def big(o):
        return pl.BlockSpec((CHUNK * 16, width), lambda i: (i + o, 0))

    small = pl.BlockSpec((CHUNK, width), lambda i: (i + at, 0))
    const = pl.BlockSpec((width, width), lambda i: (0, 0))
    edge = pl.BlockSpec((FOLD, width), lambda i: (i, 0))
    rowsb = pl.BlockSpec((2, CHUNK, width), lambda i: (0, i, 0))
    args, specs = [], []
    if combo is not None and combo[0] is not None:
        args.append(v0)
        specs.append(big(at))
    args += [field, sx, sy, ahi, alo]
    specs += [big(field_at), small, small, const, const]
    if not first:
        args += list(halos)
        specs += [edge, edge, edge, edge, rowsb]
    ex_shape = jax.ShapeDtypeStruct((feats // 2, width), jnp.float32)
    ey_shape = jax.ShapeDtypeStruct((2, feats, width), jnp.float32)
    if first:
        out_shape = [ex_shape, ey_shape]
        out_specs = [edge, rowsb]
    else:
        out_shape = [jax.ShapeDtypeStruct((feats * 16, width), jnp.float32)]
        out_specs = [big(0)]
        if edges:
            out_shape += [ex_shape, ey_shape]
            out_specs += [edge, rowsb]
    kernel = functools.partial(section_kernel, first=first, combo=combo, edges=edges)
    return pl.pallas_call(
        kernel,
        grid=(steps,),
        in_specs=specs,
        out_specs=out_specs,
        out_shape=out_shape,
        compiler_params=pltpu.CompilerParams(vmem_limit_bytes=48 * 1024 * 1024),
    )(*args)


def exchange(ex, ey):
    n_face = lax.axis_size("face")
    n_elem = lax.axis_size("elem")
    assert n_face == 2
    from_right = [(j, (j - 1) % n_elem) for j in range(n_elem)]
    from_left = [(j, (j + 1) % n_elem) for j in range(n_elem)]
    exr = lax.ppermute(ex, "elem", from_right)
    exl = lax.ppermute(ex, "elem", from_left)
    eyn = lax.ppermute(ey, "face", [(0, 1), (1, 0)])
    diag_r, diag_l = [], []
    for f in range(n_face):
        for j in range(n_elem):
            src = f * n_elem + j
            diag_r.append((src, (1 - f) * n_elem + (j - 1) % n_elem))
            diag_l.append((src, (1 - f) * n_elem + (j + 1) % n_elem))
    dr = lax.ppermute(ex, ("face", "elem"), diag_r)
    dl = lax.ppermute(ex, ("face", "elem"), diag_l)
    return (exr, exl, dr, dl, eyn)


def column_model(inputs, w_in, b_in, w_mid, b_mid, w_top, b_top, w_out, b_out):
    hidden = jax.nn.silu(
        jnp.dot(w_in, inputs, preferred_element_type=jnp.float32) + b_in[:, None]
    ).astype(jnp.bfloat16)
    hidden = jax.nn.silu(
        jnp.dot(w_mid, hidden, preferred_element_type=jnp.float32) + b_mid[:, None]
    ).astype(jnp.bfloat16)
    hidden = jax.nn.silu(
        jnp.dot(w_top, hidden, preferred_element_type=jnp.float32) + b_top[:, None]
    ).astype(jnp.bfloat16)
    outputs = jnp.dot(w_out, hidden, preferred_element_type=jnp.float32) + b_out[:, None]
    heating = jnp.sum(outputs[:LEV], axis=0)
    return (outputs.astype(jnp.bfloat16), heating)


def local(state, speed_x, speed_y, w_in, b_in, w_mid, b_mid, w_top, b_top, w_out, b_out, span_of):
    feats, height, breadth = state.shape
    across = np.kron(np.eye(breadth // NP, dtype=np.float32), TABLE.T)
    ahi_np = across.astype(jnp.bfloat16)
    alo_np = (across - ahi_np.astype(np.float32)).astype(jnp.bfloat16)
    ahi = jnp.asarray(ahi_np)
    alo = jnp.asarray(alo_np)
    sx = jnp.broadcast_to(speed_x[:, None], (feats, breadth))
    sy = jnp.broadcast_to(speed_y[:, None], (feats, breadth))
    v0 = state.reshape(feats * height, breadth)
    steps = feats // CHUNK // PARTS
    combos = [(None, None), (0.75, 0.25), ("third", None)]
    fields, edges = [], []
    for part in range(PARTS):
        at = part * steps
        edges.append(
            run_section(v0, at, None, sx, sy, ahi, alo, None, at=at, steps=steps, first=True,
                        combo=None, edges=True)
        )
        fields.append((v0, at))
    for k, combo in enumerate(combos):
        for part in range(PARTS):
            at = part * steps
            halos = exchange(*edges[part])
            field, field_at = fields[part]
            outs = run_section(
                field, field_at, v0, sx, sy, ahi, alo, halos, at=at, steps=steps, first=False,
                combo=combo, edges=k < 2,
            )
            fields[part] = (outs[0], 0)
            if k < 2:
                edges[part] = outs[1:]
    field = jnp.concatenate([f for f, _ in fields], axis=0)
    final_state = field.reshape(feats, height, breadth)
    column_count = height * breadth
    inputs = final_state.reshape(feats, column_count).astype(jnp.bfloat16)
    target = span_of.reshape(column_count)
    devices = lax.axis_size("face") * lax.axis_size("elem")
    span_ids = jnp.arange(devices, dtype=jnp.int32)
    weights = (w_in, b_in, w_mid, b_mid, w_top, b_top, w_out, b_out)
    tend_cols, heating = column_model(inputs, *weights)
    member = (target[:, None] == span_ids[None, :]).astype(jnp.float32)
    partial_sums = jnp.sum(member * heating[:, None], axis=0)
    received = lax.all_to_all(
        partial_sums.reshape(devices, 1), ("face", "elem"), 0, 1, tiled=True
    )
    span_heating = jnp.sum(received, axis=1) / column_count
    tendencies = tend_cols.reshape(-1, height, breadth)
    return (final_state, tendencies, span_heating)


def solution(mesh):
    return jax.shard_map(
        local,
        mesh=mesh,
        in_specs=(
            P(None, "face", "elem"),
            P(),
            P(),
            P(),
            P(),
            P(),
            P(),
            P(),
            P(),
            P(),
            P(),
            P("face", "elem", None, None),
        ),
        out_specs=(P(None, "face", "elem"), P(None, "face", "elem"), P(("face", "elem"))),
        check_vma=False,
    )
```

```python
import functools
import math

import jax
import jax.numpy as jnp
import numpy as np
from jax import lax
from jax.experimental import pallas as pl
from jax.experimental.pallas import tpu as pltpu
from jax.sharding import PartitionSpec as P

NP = 4
LEV = 72
CHUNK = 48
FOLD = CHUNK // 2


def gll_matrix():
    inner_node = 1.0 / math.sqrt(5.0)
    gll_nodes = np.array([-1.0, -inner_node, inner_node, 1.0])
    weights = np.array(
        [
            1.0
            / np.prod([gll_nodes[outer] - gll_nodes[other] for other in range(4) if other != outer])
            for outer in range(4)
        ]
    )
    matrix = np.zeros((4, 4))
    for outer in range(4):
        for inner in range(4):
            if inner != outer:
                matrix[outer, inner] = (
                    weights[inner] / weights[outer] / (gll_nodes[outer] - gll_nodes[inner])
                )
    for outer in range(4):
        matrix[outer, outer] = -np.sum(matrix[outer])
    return matrix.astype(np.float32)


TABLE = gll_matrix()


def lanes(shape):
    return lax.broadcasted_iota(jnp.int32, shape, len(shape) - 1)


def roll(x, shift):
    shift = shift % x.shape[-1]
    return x if shift == 0 else pltpu.roll(x, shift, x.ndim - 1)


def raw_slabs(slabs, sx, sy, ahi, alo):
    rows = slabs[0].shape[0]
    stacked = jnp.concatenate(slabs, axis=0)
    hi = stacked.astype(jnp.bfloat16)
    lo = (stacked - hi.astype(jnp.float32)).astype(jnp.bfloat16)
    along_x = (
        jnp.dot(hi, ahi, preferred_element_type=jnp.float32)
        + jnp.dot(hi, alo, preferred_element_type=jnp.float32)
        + jnp.dot(lo, ahi, preferred_element_type=jnp.float32)
    )
    out = []
    for y, _ in enumerate(slabs):
        base = (y // NP) * NP
        j = y % NP
        along_y = float(TABLE[j, 0]) * slabs[base]
        for i in range(1, NP):
            along_y = along_y + float(TABLE[j, i]) * slabs[base + i]
        dx = along_x[y * rows : (y + 1) * rows]
        out.append(-(sx * dx + sy * along_y))
    return out


def pack_edges(tend):
    rows, width = tend[0].shape
    lane = lanes((rows, width))
    acc = jnp.zeros((rows, width), jnp.float32)
    for y, t in enumerate(tend):
        acc = jnp.where(lane == 2 * y, roll(t, 2 * y), acc)
        acc = jnp.where(lane == 2 * y + 1, roll(t, 2 * y + 2), acc)
    half = rows // 2
    lane_h = lanes((half, width))
    return jnp.where(lane_h < 32, acc[:half], roll(acc[half:], 32))


def unpack_edges(block):
    return jnp.concatenate([block, roll(block, 96)], axis=0)


def stiff_x(t, right_edges, left_edges, y):
    rows, width = t.shape
    lane = lanes((rows, width))
    right = jnp.where(lane == width - 1, roll(right_edges, width - 1 - 2 * y), roll(t, width - 1))
    left = jnp.where(lane == 0, roll(left_edges, width - 1 - 2 * y), roll(t, 1))
    place = lane % NP
    return jnp.where(
        place == NP - 1, 0.5 * (t + right), jnp.where(place == 0, 0.5 * (left + t), t)
    )


def section_kernel(*refs, first, combo, edges):
    refs = list(refs)
    v0_ref = None if combo is None or combo[0] is None else refs.pop(0)
    sp_ref = refs.pop(0)
    sx_ref, sy_ref, ahi_ref, alo_ref = refs[:4]
    refs = refs[4:]
    if not first:
        exr_ref, exl_ref, dr_ref, dl_ref, eyn_ref = refs[:5]
        refs = refs[5:]
    rows = CHUNK
    height = 16
    sx = sx_ref[...]
    sy = sy_ref[...]
    ahi = ahi_ref[...]
    alo = alo_ref[...]
    slabs = [sp_ref[pl.ds(y, rows, stride=height), :] for y in range(height)]
    tend = raw_slabs(slabs, sx, sy, ahi, alo)
    if first:
        ex_ref, ey_ref = refs
        ex_ref[...] = pack_edges(tend)
        ey_ref[0] = tend[0]
        ey_ref[1] = tend[height - 1]
        return
    exr = unpack_edges(exr_ref[...])
    exl = unpack_edges(exl_ref[...])
    dr = unpack_edges(dr_ref[...])
    dl = unpack_edges(dl_ref[...])
    tx = [stiff_x(t, exr, exl, y) for y, t in enumerate(tend)]
    down = stiff_x(eyn_ref[0], dr, dl, 0)
    up = stiff_x(eyn_ref[1], dr, dl, height - 1)
    ext = [up] + tx + [down]
    new = []
    for y in range(height):
        cur = ext[y + 1]
        if y % NP == NP - 1:
            op = 0.5 * (cur + ext[y + 2])
        elif y % NP == 0:
            op = 0.5 * (ext[y] + cur)
        else:
            op = cur
        inner = slabs[y] + op
        if combo[0] is None:
            val = inner
        else:
            v0 = v0_ref[pl.ds(y, rows, stride=height), :]
            if combo[0] == "third":
                val = v0 / 3.0 + 2.0 / 3.0 * inner
            else:
                val = combo[0] * v0 + combo[1] * inner
        new.append(val)
    out_ref = refs[0]
    for y in range(height):
        out_ref[pl.ds(y, rows, stride=height), :] = new[y]
    if edges:
        ex_ref, ey_ref = refs[1:3]
        tend = raw_slabs(new, sx, sy, ahi, alo)
        ex_ref[...] = pack_edges(tend)
        ey_ref[0] = tend[0]
        ey_ref[1] = tend[height - 1]


def run_section(field_rows, v0, sx, sy, ahi, alo, halos, *, first, combo, edges):
    total, width = field_rows.shape
    feats = sx.shape[0]
    steps = feats // CHUNK
    big = pl.BlockSpec((CHUNK * 16, width), lambda i: (i, 0))
    small = pl.BlockSpec((CHUNK, width), lambda i: (i, 0))
    const = pl.BlockSpec((width, width), lambda i: (0, 0))
    edge = pl.BlockSpec((FOLD, width), lambda i: (i, 0))
    rowsb = pl.BlockSpec((2, CHUNK, width), lambda i: (0, i, 0))
    args, specs = [], []
    if combo is not None and combo[0] is not None:
        args.append(v0)
        specs.append(big)
    args += [field_rows, sx, sy, ahi, alo]
    specs += [big, small, small, const, const]
    if not first:
        args += list(halos)
        specs += [edge, edge, edge, edge, rowsb]
    out_shape, out_specs = [], []
    ex_shape = jax.ShapeDtypeStruct((feats // 2, width), jnp.float32)
    ey_shape = jax.ShapeDtypeStruct((2, feats, width), jnp.float32)
    if first:
        out_shape = [ex_shape, ey_shape]
        out_specs = [edge, rowsb]
    else:
        out_shape = [jax.ShapeDtypeStruct((total, width), jnp.float32)]
        out_specs = [big]
        if edges:
            out_shape += [ex_shape, ey_shape]
            out_specs += [edge, rowsb]
    kernel = functools.partial(section_kernel, first=first, combo=combo, edges=edges)
    return pl.pallas_call(
        kernel,
        grid=(steps,),
        in_specs=specs,
        out_specs=out_specs,
        out_shape=out_shape,
        compiler_params=pltpu.CompilerParams(vmem_limit_bytes=48 * 1024 * 1024),
    )(*args)


def exchange(ex, ey):
    n_face = lax.axis_size("face")
    n_elem = lax.axis_size("elem")
    assert n_face == 2
    from_right = [(j, (j - 1) % n_elem) for j in range(n_elem)]
    from_left = [(j, (j + 1) % n_elem) for j in range(n_elem)]
    exr = lax.ppermute(ex, "elem", from_right)
    exl = lax.ppermute(ex, "elem", from_left)
    eyn = lax.ppermute(ey, "face", [(0, 1), (1, 0)])
    diag_r, diag_l = [], []
    for f in range(n_face):
        for j in range(n_elem):
            src = f * n_elem + j
            diag_r.append((src, (1 - f) * n_elem + (j - 1) % n_elem))
            diag_l.append((src, (1 - f) * n_elem + (j + 1) % n_elem))
    dr = lax.ppermute(ex, ("face", "elem"), diag_r)
    dl = lax.ppermute(ex, ("face", "elem"), diag_l)
    return (exr, exl, dr, dl, eyn)


def column_model(inputs, w_in, b_in, w_mid, b_mid, w_top, b_top, w_out, b_out):
    hidden = jax.nn.silu(
        jnp.dot(w_in, inputs, preferred_element_type=jnp.float32) + b_in[:, None]
    ).astype(jnp.bfloat16)
    hidden = jax.nn.silu(
        jnp.dot(w_mid, hidden, preferred_element_type=jnp.float32) + b_mid[:, None]
    ).astype(jnp.bfloat16)
    hidden = jax.nn.silu(
        jnp.dot(w_top, hidden, preferred_element_type=jnp.float32) + b_top[:, None]
    ).astype(jnp.bfloat16)
    outputs = jnp.dot(w_out, hidden, preferred_element_type=jnp.float32) + b_out[:, None]
    heating = jnp.sum(outputs[:LEV], axis=0)
    return (outputs.astype(jnp.bfloat16), heating)


def mlp_kernel(fin_ref, w_in_ref, b_in_ref, w_mid_ref, b_mid_ref, w_top_ref, b_top_ref,
               w_out_ref, b_out_ref, tend_ref, heat_ref, scratch):
    feats = w_in_ref.shape[1]
    outs = w_out_ref.shape[0]
    height = heat_ref.shape[0]
    width = heat_ref.shape[1]

    def layer(w_ref, b_ref, x):
        a = jnp.dot(w_ref[...], x, preferred_element_type=jnp.float32) + b_ref[...]
        return (a / (1.0 + jnp.exp(-a))).astype(jnp.bfloat16)

    for pair in range(height // 2):
        y = 2 * pair
        x = jnp.concatenate(
            [fin_ref[pl.ds(y, feats, stride=height), :], fin_ref[pl.ds(y + 1, feats, stride=height), :]],
            axis=1,
        ).astype(jnp.bfloat16)
        h = layer(w_in_ref, b_in_ref, x)
        h = layer(w_mid_ref, b_mid_ref, h)
        h = layer(w_top_ref, b_top_ref, h)
        out = jnp.dot(w_out_ref[...], h, preferred_element_type=jnp.float32) + b_out_ref[...]
        heat = jnp.sum(out[:LEV], axis=0, keepdims=True)
        heat_ref[y : y + 1, :] = heat[:, :width]
        heat_ref[y + 1 : y + 2, :] = heat[:, width:]
        scratch[pl.ds(y, outs, stride=height), :] = out[:, :width]
        scratch[pl.ds(y + 1, outs, stride=height), :] = out[:, width:]
    tend_ref[...] = scratch[...].astype(jnp.bfloat16)


def run_mlp(fin, height, w_in, b_in, w_mid, b_mid, w_top, b_top, w_out, b_out):
    width = fin.shape[1]
    outs = w_out.shape[0]
    col = lambda b: b.reshape(-1, 1)
    return pl.pallas_call(
        mlp_kernel,
        out_shape=[
            jax.ShapeDtypeStruct((outs * height, width), jnp.bfloat16),
            jax.ShapeDtypeStruct((height, width), jnp.float32),
        ],
        scratch_shapes=[pltpu.VMEM((outs * height, width), jnp.float32)],
        compiler_params=pltpu.CompilerParams(vmem_limit_bytes=48 * 1024 * 1024),
    )(fin, w_in, col(b_in), w_mid, col(b_mid), w_top, col(b_top), w_out, col(b_out))


def local(state, speed_x, speed_y, w_in, b_in, w_mid, b_mid, w_top, b_top, w_out, b_out, span_of):
    feats, height, breadth = state.shape
    across = np.kron(np.eye(breadth // NP, dtype=np.float32), TABLE.T)
    ahi_np = across.astype(jnp.bfloat16)
    alo_np = (across - ahi_np.astype(np.float32)).astype(jnp.bfloat16)
    ahi = jnp.asarray(ahi_np)
    alo = jnp.asarray(alo_np)
    sx = jnp.broadcast_to(speed_x[:, None], (feats, breadth))
    sy = jnp.broadcast_to(speed_y[:, None], (feats, breadth))
    v0 = state.reshape(feats * height, breadth)
    ex, ey = run_section(v0, None, sx, sy, ahi, alo, None, first=True, combo=None, edges=True)
    field = v0
    combos = [(None, None), (0.75, 0.25), ("third", None)]
    for k, combo in enumerate(combos):
        halos = exchange(ex, ey)
        outs = run_section(
            field, v0, sx, sy, ahi, alo, halos, first=False, combo=combo, edges=k < 2
        )
        if k < 2:
            field, ex, ey = outs
        else:
            (field,) = outs
    final_state = field.reshape(feats, height, breadth)
    column_count = height * breadth
    target = span_of.reshape(column_count)
    devices = lax.axis_size("face") * lax.axis_size("elem")
    span_ids = jnp.arange(devices, dtype=jnp.int32)
    tend_rows, heat_rows = run_mlp(field, height, w_in, b_in, w_mid, b_mid, w_top, b_top, w_out, b_out)
    heating = heat_rows.reshape(column_count)
    member = (target[:, None] == span_ids[None, :]).astype(jnp.float32)
    partial_sums = jnp.sum(member * heating[:, None], axis=0)
    received = lax.all_to_all(
        partial_sums.reshape(devices, 1), ("face", "elem"), 0, 1, tiled=True
    )
    span_heating = jnp.sum(received, axis=1) / column_count
    tendencies = tend_rows.reshape(-1, height, breadth)
    return (final_state, tendencies, span_heating)


def solution(mesh):
    return jax.shard_map(
        local,
        mesh=mesh,
        in_specs=(
            P(None, "face", "elem"),
            P(),
            P(),
            P(),
            P(),
            P(),
            P(),
            P(),
            P(),
            P(),
            P(),
            P("face", "elem", None, None),
        ),
        out_specs=(P(None, "face", "elem"), P(None, "face", "elem"), P(("face", "elem"))),
        check_vma=False,
    )
```

```python
import functools
import math

import jax
import jax.numpy as jnp
import numpy as np
from jax import lax
from jax.experimental import pallas as pl
from jax.experimental.pallas import tpu as pltpu
from jax.sharding import PartitionSpec as P

NP = 4
LEV = 72
CHUNK = 48
FOLD = CHUNK // 2


def gll_matrix():
    inner_node = 1.0 / math.sqrt(5.0)
    gll_nodes = np.array([-1.0, -inner_node, inner_node, 1.0])
    weights = np.array(
        [
            1.0
            / np.prod([gll_nodes[outer] - gll_nodes[other] for other in range(4) if other != outer])
            for outer in range(4)
        ]
    )
    matrix = np.zeros((4, 4))
    for outer in range(4):
        for inner in range(4):
            if inner != outer:
                matrix[outer, inner] = (
                    weights[inner] / weights[outer] / (gll_nodes[outer] - gll_nodes[inner])
                )
    for outer in range(4):
        matrix[outer, outer] = -np.sum(matrix[outer])
    return matrix.astype(np.float32)


TABLE = gll_matrix()


def lanes(shape):
    return lax.broadcasted_iota(jnp.int32, shape, len(shape) - 1)


def roll(x, shift):
    shift = shift % x.shape[-1]
    return x if shift == 0 else pltpu.roll(x, shift, x.ndim - 1)


def raw_slabs(slabs, sx, sy, ahi, alo):
    rows = slabs[0].shape[0]
    stacked = jnp.concatenate(slabs, axis=0)
    hi = stacked.astype(jnp.bfloat16)
    lo = (stacked - hi.astype(jnp.float32)).astype(jnp.bfloat16)
    along_x = (
        jnp.dot(hi, ahi, preferred_element_type=jnp.float32)
        + jnp.dot(hi, alo, preferred_element_type=jnp.float32)
        + jnp.dot(lo, ahi, preferred_element_type=jnp.float32)
    )
    out = []
    for y, _ in enumerate(slabs):
        base = (y // NP) * NP
        j = y % NP
        along_y = float(TABLE[j, 0]) * slabs[base]
        for i in range(1, NP):
            along_y = along_y + float(TABLE[j, i]) * slabs[base + i]
        dx = along_x[y * rows : (y + 1) * rows]
        out.append(-(sx * dx + sy * along_y))
    return out


def pack_edges(tend):
    rows, width = tend[0].shape
    lane = lanes((rows, width))
    acc = jnp.zeros((rows, width), jnp.float32)
    for y, t in enumerate(tend):
        acc = jnp.where(lane == 2 * y, roll(t, 2 * y), acc)
        acc = jnp.where(lane == 2 * y + 1, roll(t, 2 * y + 2), acc)
    half = rows // 2
    lane_h = lanes((half, width))
    return jnp.where(lane_h < 32, acc[:half], roll(acc[half:], 32))


def unpack_edges(block):
    return jnp.concatenate([block, roll(block, 96)], axis=0)


def stiff_x(t, right_edges, left_edges, y):
    rows, width = t.shape
    lane = lanes((rows, width))
    right = jnp.where(lane == width - 1, roll(right_edges, width - 1 - 2 * y), roll(t, width - 1))
    left = jnp.where(lane == 0, roll(left_edges, width - 1 - 2 * y), roll(t, 1))
    place = lane % NP
    return jnp.where(
        place == NP - 1, 0.5 * (t + right), jnp.where(place == 0, 0.5 * (left + t), t)
    )


def section_kernel(*refs, first, combo, edges):
    refs = list(refs)
    v0_ref = None if combo is None or combo[0] is None else refs.pop(0)
    sp_ref = refs.pop(0)
    sx_ref, sy_ref, ahi_ref, alo_ref = refs[:4]
    refs = refs[4:]
    if not first:
        exr_ref, exl_ref, dr_ref, dl_ref, eyn_ref = refs[:5]
        refs = refs[5:]
    rows = CHUNK
    height = 16
    sx = sx_ref[...]
    sy = sy_ref[...]
    ahi = ahi_ref[...]
    alo = alo_ref[...]
    slabs = [sp_ref[pl.ds(y, rows, stride=height), :] for y in range(height)]
    tend = raw_slabs(slabs, sx, sy, ahi, alo)
    if first:
        ex_ref, ey_ref = refs
        ex_ref[...] = pack_edges(tend)
        ey_ref[0] = tend[0]
        ey_ref[1] = tend[height - 1]
        return
    exr = unpack_edges(exr_ref[...])
    exl = unpack_edges(exl_ref[...])
    dr = unpack_edges(dr_ref[...])
    dl = unpack_edges(dl_ref[...])
    tx = [stiff_x(t, exr, exl, y) for y, t in enumerate(tend)]
    down = stiff_x(eyn_ref[0], dr, dl, 0)
    up = stiff_x(eyn_ref[1], dr, dl, height - 1)
    ext = [up] + tx + [down]
    new = []
    for y in range(height):
        cur = ext[y + 1]
        if y % NP == NP - 1:
            op = 0.5 * (cur + ext[y + 2])
        elif y % NP == 0:
            op = 0.5 * (ext[y] + cur)
        else:
            op = cur
        inner = slabs[y] + op
        if combo[0] is None:
            val = inner
        else:
            v0 = v0_ref[pl.ds(y, rows, stride=height), :]
            if combo[0] == "third":
                val = v0 / 3.0 + 2.0 / 3.0 * inner
            else:
                val = combo[0] * v0 + combo[1] * inner
        new.append(val)
    out_ref = refs[0]
    for y in range(height):
        out_ref[pl.ds(y, rows, stride=height), :] = new[y]
    if edges:
        ex_ref, ey_ref = refs[1:3]
        tend = raw_slabs(new, sx, sy, ahi, alo)
        ex_ref[...] = pack_edges(tend)
        ey_ref[0] = tend[0]
        ey_ref[1] = tend[height - 1]


def run_section(field_rows, v0, sx, sy, ahi, alo, halos, *, first, combo, edges):
    total, width = field_rows.shape
    feats = sx.shape[0]
    steps = feats // CHUNK
    big = pl.BlockSpec((CHUNK * 16, width), lambda i: (i, 0))
    small = pl.BlockSpec((CHUNK, width), lambda i: (i, 0))
    const = pl.BlockSpec((width, width), lambda i: (0, 0))
    edge = pl.BlockSpec((FOLD, width), lambda i: (i, 0))
    rowsb = pl.BlockSpec((2, CHUNK, width), lambda i: (0, i, 0))
    args, specs = [], []
    if combo is not None and combo[0] is not None:
        args.append(v0)
        specs.append(big)
    args += [field_rows, sx, sy, ahi, alo]
    specs += [big, small, small, const, const]
    if not first:
        args += list(halos)
        specs += [edge, edge, edge, edge, rowsb]
    out_shape, out_specs = [], []
    ex_shape = jax.ShapeDtypeStruct((feats // 2, width), jnp.float32)
    ey_shape = jax.ShapeDtypeStruct((2, feats, width), jnp.float32)
    if first:
        out_shape = [ex_shape, ey_shape]
        out_specs = [edge, rowsb]
    else:
        out_shape = [jax.ShapeDtypeStruct((total, width), jnp.float32)]
        out_specs = [big]
        if edges:
            out_shape += [ex_shape, ey_shape]
            out_specs += [edge, rowsb]
    kernel = functools.partial(section_kernel, first=first, combo=combo, edges=edges)
    return pl.pallas_call(
        kernel,
        grid=(steps,),
        in_specs=specs,
        out_specs=out_specs,
        out_shape=out_shape,
        compiler_params=pltpu.CompilerParams(vmem_limit_bytes=48 * 1024 * 1024),
    )(*args)


def exchange(ex, ey):
    n_face = lax.axis_size("face")
    n_elem = lax.axis_size("elem")
    assert n_face == 2
    from_right = [(j, (j - 1) % n_elem) for j in range(n_elem)]
    from_left = [(j, (j + 1) % n_elem) for j in range(n_elem)]
    exr = lax.ppermute(ex, "elem", from_right)
    exl = lax.ppermute(ex, "elem", from_left)
    eyn = lax.ppermute(ey, "face", [(0, 1), (1, 0)])
    diag_r, diag_l = [], []
    for f in range(n_face):
        for j in range(n_elem):
            src = f * n_elem + j
            diag_r.append((src, (1 - f) * n_elem + (j - 1) % n_elem))
            diag_l.append((src, (1 - f) * n_elem + (j + 1) % n_elem))
    dr = lax.ppermute(ex, ("face", "elem"), diag_r)
    dl = lax.ppermute(ex, ("face", "elem"), diag_l)
    return (exr, exl, dr, dl, eyn)


def column_model(inputs, w_in, b_in, w_mid, b_mid, w_top, b_top, w_out, b_out):
    hidden = jax.nn.silu(
        jnp.dot(w_in, inputs, preferred_element_type=jnp.float32) + b_in[:, None]
    ).astype(jnp.bfloat16)
    hidden = jax.nn.silu(
        jnp.dot(w_mid, hidden, preferred_element_type=jnp.float32) + b_mid[:, None]
    ).astype(jnp.bfloat16)
    hidden = jax.nn.silu(
        jnp.dot(w_top, hidden, preferred_element_type=jnp.float32) + b_top[:, None]
    ).astype(jnp.bfloat16)
    outputs = jnp.dot(w_out, hidden, preferred_element_type=jnp.float32) + b_out[:, None]
    heating = jnp.sum(outputs[:LEV], axis=0)
    return (outputs.astype(jnp.bfloat16), heating)


def mlp_kernel(fin_ref, w_in_ref, b_in_ref, w_mid_ref, b_mid_ref, w_top_ref, b_top_ref,
               w_out_ref, b_out_ref, tend_ref, heat_ref, scratch):
    feats = w_in_ref.shape[1]
    outs = w_out_ref.shape[0]
    height = heat_ref.shape[0]
    width = heat_ref.shape[1]

    def layer(w_ref, b_ref, x):
        a = jnp.dot(w_ref[...], x, preferred_element_type=jnp.float32) + b_ref[...]
        return (a * (0.5 + 0.5 * jnp.tanh(0.5 * a))).astype(jnp.bfloat16)

    for pair in range(height // 2):
        y = 2 * pair
        x = jnp.concatenate(
            [fin_ref[pl.ds(y, feats, stride=height), :], fin_ref[pl.ds(y + 1, feats, stride=height), :]],
            axis=1,
        ).astype(jnp.bfloat16)
        h = layer(w_in_ref, b_in_ref, x)
        h = layer(w_mid_ref, b_mid_ref, h)
        h = layer(w_top_ref, b_top_ref, h)
        out = jnp.dot(w_out_ref[...], h, preferred_element_type=jnp.float32) + b_out_ref[...]
        heat = jnp.sum(out[:LEV], axis=0, keepdims=True)
        heat_ref[y : y + 1, :] = heat[:, :width]
        heat_ref[y + 1 : y + 2, :] = heat[:, width:]
        scratch[pl.ds(y, outs, stride=height), :] = out[:, :width]
        scratch[pl.ds(y + 1, outs, stride=height), :] = out[:, width:]
    tend_ref[...] = scratch[...].astype(jnp.bfloat16)


def run_mlp(fin, height, w_in, b_in, w_mid, b_mid, w_top, b_top, w_out, b_out):
    width = fin.shape[1]
    outs = w_out.shape[0]
    col = lambda b: b.reshape(-1, 1)
    return pl.pallas_call(
        mlp_kernel,
        out_shape=[
            jax.ShapeDtypeStruct((outs * height, width), jnp.bfloat16),
            jax.ShapeDtypeStruct((height, width), jnp.float32),
        ],
        scratch_shapes=[pltpu.VMEM((outs * height, width), jnp.float32)],
        compiler_params=pltpu.CompilerParams(vmem_limit_bytes=48 * 1024 * 1024),
    )(fin, w_in, col(b_in), w_mid, col(b_mid), w_top, col(b_top), w_out, col(b_out))


def local(state, speed_x, speed_y, w_in, b_in, w_mid, b_mid, w_top, b_top, w_out, b_out, span_of):
    feats, height, breadth = state.shape
    across = np.kron(np.eye(breadth // NP, dtype=np.float32), TABLE.T)
    ahi_np = across.astype(jnp.bfloat16)
    alo_np = (across - ahi_np.astype(np.float32)).astype(jnp.bfloat16)
    ahi = jnp.asarray(ahi_np)
    alo = jnp.asarray(alo_np)
    sx = jnp.broadcast_to(speed_x[:, None], (feats, breadth))
    sy = jnp.broadcast_to(speed_y[:, None], (feats, breadth))
    v0 = state.reshape(feats * height, breadth)
    ex, ey = run_section(v0, None, sx, sy, ahi, alo, None, first=True, combo=None, edges=True)
    field = v0
    combos = [(None, None), (0.75, 0.25), ("third", None)]
    for k, combo in enumerate(combos):
        halos = exchange(ex, ey)
        outs = run_section(
            field, v0, sx, sy, ahi, alo, halos, first=False, combo=combo, edges=k < 2
        )
        if k < 2:
            field, ex, ey = outs
        else:
            (field,) = outs
    final_state = field.reshape(feats, height, breadth)
    column_count = height * breadth
    target = span_of.reshape(column_count)
    devices = lax.axis_size("face") * lax.axis_size("elem")
    span_ids = jnp.arange(devices, dtype=jnp.int32)
    tend_rows, heat_rows = run_mlp(field, height, w_in, b_in, w_mid, b_mid, w_top, b_top, w_out, b_out)
    heating = heat_rows.reshape(column_count)
    member = (target[:, None] == span_ids[None, :]).astype(jnp.float32)
    partial_sums = jnp.sum(member * heating[:, None], axis=0)
    received = lax.all_to_all(
        partial_sums.reshape(devices, 1), ("face", "elem"), 0, 1, tiled=True
    )
    span_heating = jnp.sum(received, axis=1) / column_count
    tendencies = tend_rows.reshape(-1, height, breadth)
    return (final_state, tendencies, span_heating)


def solution(mesh):
    return jax.shard_map(
        local,
        mesh=mesh,
        in_specs=(
            P(None, "face", "elem"),
            P(),
            P(),
            P(),
            P(),
            P(),
            P(),
            P(),
            P(),
            P(),
            P(),
            P("face", "elem", None, None),
        ),
        out_specs=(P(None, "face", "elem"), P(None, "face", "elem"), P(("face", "elem"))),
        check_vma=False,
    )
```

```python
import functools
import math

import jax
import jax.numpy as jnp
import numpy as np
from jax import lax
from jax.experimental import pallas as pl
from jax.experimental.pallas import tpu as pltpu
from jax.sharding import PartitionSpec as P

NP = 4
LEV = 72
CHUNK = 48
FOLD = CHUNK // 2


def gll_matrix():
    inner_node = 1.0 / math.sqrt(5.0)
    gll_nodes = np.array([-1.0, -inner_node, inner_node, 1.0])
    weights = np.array(
        [
            1.0
            / np.prod([gll_nodes[outer] - gll_nodes[other] for other in range(4) if other != outer])
            for outer in range(4)
        ]
    )
    matrix = np.zeros((4, 4))
    for outer in range(4):
        for inner in range(4):
            if inner != outer:
                matrix[outer, inner] = (
                    weights[inner] / weights[outer] / (gll_nodes[outer] - gll_nodes[inner])
                )
    for outer in range(4):
        matrix[outer, outer] = -np.sum(matrix[outer])
    return matrix.astype(np.float32)


TABLE = gll_matrix()


def lanes(shape):
    return lax.broadcasted_iota(jnp.int32, shape, len(shape) - 1)


def roll(x, shift):
    shift = shift % x.shape[-1]
    return x if shift == 0 else pltpu.roll(x, shift, x.ndim - 1)


def raw_slabs(slabs, sx, sy, ahi, alo):
    rows = slabs[0].shape[0]
    stacked = jnp.concatenate(slabs, axis=0)
    hi = stacked.astype(jnp.bfloat16)
    lo = (stacked - hi.astype(jnp.float32)).astype(jnp.bfloat16)
    along_x = (
        jnp.dot(hi, ahi, preferred_element_type=jnp.float32)
        + jnp.dot(hi, alo, preferred_element_type=jnp.float32)
        + jnp.dot(lo, ahi, preferred_element_type=jnp.float32)
    )
    out = []
    for y, _ in enumerate(slabs):
        base = (y // NP) * NP
        j = y % NP
        along_y = float(TABLE[j, 0]) * slabs[base]
        for i in range(1, NP):
            along_y = along_y + float(TABLE[j, i]) * slabs[base + i]
        dx = along_x[y * rows : (y + 1) * rows]
        out.append(-(sx * dx + sy * along_y))
    return out


def pack_edges(tend):
    rows, width = tend[0].shape
    lane = lanes((rows, width))
    acc = jnp.zeros((rows, width), jnp.float32)
    for y, t in enumerate(tend):
        acc = jnp.where(lane == 2 * y, roll(t, 2 * y), acc)
        acc = jnp.where(lane == 2 * y + 1, roll(t, 2 * y + 2), acc)
    half = rows // 2
    lane_h = lanes((half, width))
    return jnp.where(lane_h < 32, acc[:half], roll(acc[half:], 32))


def unpack_edges(block):
    return jnp.concatenate([block, roll(block, 96)], axis=0)


def stiff_x(t, right_edges, left_edges, y):
    rows, width = t.shape
    lane = lanes((rows, width))
    right = jnp.where(lane == width - 1, roll(right_edges, width - 1 - 2 * y), roll(t, width - 1))
    left = jnp.where(lane == 0, roll(left_edges, width - 1 - 2 * y), roll(t, 1))
    place = lane % NP
    return jnp.where(
        place == NP - 1, 0.5 * (t + right), jnp.where(place == 0, 0.5 * (left + t), t)
    )


def section_kernel(*refs, first, combo, edges):
    refs = list(refs)
    v0_ref = None if combo is None or combo[0] is None else refs.pop(0)
    sp_ref = refs.pop(0)
    sx_ref, sy_ref, ahi_ref, alo_ref = refs[:4]
    refs = refs[4:]
    if not first:
        exr_ref, exl_ref, dr_ref, dl_ref, top_ref, bottom_ref = refs[:6]
        refs = refs[6:]
    rows = CHUNK
    height = 16
    sx = sx_ref[...]
    sy = sy_ref[...]
    ahi = ahi_ref[...]
    alo = alo_ref[...]
    slabs = [sp_ref[pl.ds(y, rows, stride=height), :] for y in range(height)]
    tend = raw_slabs(slabs, sx, sy, ahi, alo)
    if first:
        ex_ref, ey_ref = refs
        ex_ref[...] = pack_edges(tend)
        ey_ref[0] = tend[0]
        ey_ref[1] = tend[height - 1]
        return
    exr = unpack_edges(exr_ref[...])
    exl = unpack_edges(exl_ref[...])
    dr = unpack_edges(dr_ref[...])
    dl = unpack_edges(dl_ref[...])
    tx = [stiff_x(t, exr, exl, y) for y, t in enumerate(tend)]
    down = stiff_x(top_ref[...], dr, dl, 0)
    up = stiff_x(bottom_ref[...], dr, dl, height - 1)
    ext = [up] + tx + [down]
    new = []
    for y in range(height):
        cur = ext[y + 1]
        if y % NP == NP - 1:
            op = 0.5 * (cur + ext[y + 2])
        elif y % NP == 0:
            op = 0.5 * (ext[y] + cur)
        else:
            op = cur
        inner = slabs[y] + op
        if combo[0] is None:
            val = inner
        else:
            v0 = v0_ref[pl.ds(y, rows, stride=height), :]
            if combo[0] == "third":
                val = v0 / 3.0 + 2.0 / 3.0 * inner
            else:
                val = combo[0] * v0 + combo[1] * inner
        new.append(val)
    out_ref = refs[0]
    for y in range(height):
        out_ref[pl.ds(y, rows, stride=height), :] = new[y]
    if edges:
        ex_ref, ey_ref = refs[1:3]
        tend = raw_slabs(new, sx, sy, ahi, alo)
        ex_ref[...] = pack_edges(tend)
        ey_ref[0] = tend[0]
        ey_ref[1] = tend[height - 1]


def run_section(field_rows, v0, sx, sy, ahi, alo, halos, *, first, combo, edges):
    total, width = field_rows.shape
    feats = sx.shape[0]
    steps = feats // CHUNK
    big = pl.BlockSpec((CHUNK * 16, width), lambda i: (i, 0))
    small = pl.BlockSpec((CHUNK, width), lambda i: (i, 0))
    const = pl.BlockSpec((width, width), lambda i: (0, 0))
    edge = pl.BlockSpec((FOLD, width), lambda i: (i, 0))
    rowsb = pl.BlockSpec((2, CHUNK, width), lambda i: (0, i, 0))
    args, specs = [], []
    if combo is not None and combo[0] is not None:
        args.append(v0)
        specs.append(big)
    args += [field_rows, sx, sy, ahi, alo]
    specs += [big, small, small, const, const]
    if not first:
        exr, exl, partner = halos
        blocks = field_rows.shape[0] // (CHUNK * 16)
        args += [exr, exl, partner, partner, partner, partner]
        specs += [
            edge,
            edge,
            pl.BlockSpec((FOLD, width), lambda i: (4 * blocks + i, 0)),
            pl.BlockSpec((FOLD, width), lambda i: (5 * blocks + i, 0)),
            pl.BlockSpec((CHUNK, width), lambda i: (i, 0)),
            pl.BlockSpec((CHUNK, width), lambda i: (blocks + i, 0)),
        ]
    out_shape, out_specs = [], []
    ex_shape = jax.ShapeDtypeStruct((feats // 2, width), jnp.float32)
    ey_shape = jax.ShapeDtypeStruct((2, feats, width), jnp.float32)
    if first:
        out_shape = [ex_shape, ey_shape]
        out_specs = [edge, rowsb]
    else:
        out_shape = [jax.ShapeDtypeStruct((total, width), jnp.float32)]
        out_specs = [big]
        if edges:
            out_shape += [ex_shape, ey_shape]
            out_specs += [edge, rowsb]
    kernel = functools.partial(section_kernel, first=first, combo=combo, edges=edges)
    return pl.pallas_call(
        kernel,
        grid=(steps,),
        in_specs=specs,
        out_specs=out_specs,
        out_shape=out_shape,
        compiler_params=pltpu.CompilerParams(vmem_limit_bytes=48 * 1024 * 1024),
    )(*args)


def exchange(ex, ey):
    n_face = lax.axis_size("face")
    n_elem = lax.axis_size("elem")
    assert n_face == 2
    from_right = [(j, (j - 1) % n_elem) for j in range(n_elem)]
    from_left = [(j, (j + 1) % n_elem) for j in range(n_elem)]
    exr = lax.ppermute(ex, "elem", from_right)
    exl = lax.ppermute(ex, "elem", from_left)
    feats = ey.shape[1]
    bundle = jnp.concatenate([ey.reshape(2 * feats, ey.shape[2]), exr, exl], axis=0)
    partner = lax.ppermute(bundle, "face", [(0, 1), (1, 0)])
    return (exr, exl, partner)


def column_model(inputs, w_in, b_in, w_mid, b_mid, w_top, b_top, w_out, b_out):
    hidden = jax.nn.silu(
        jnp.dot(w_in, inputs, preferred_element_type=jnp.float32) + b_in[:, None]
    ).astype(jnp.bfloat16)
    hidden = jax.nn.silu(
        jnp.dot(w_mid, hidden, preferred_element_type=jnp.float32) + b_mid[:, None]
    ).astype(jnp.bfloat16)
    hidden = jax.nn.silu(
        jnp.dot(w_top, hidden, preferred_element_type=jnp.float32) + b_top[:, None]
    ).astype(jnp.bfloat16)
    outputs = jnp.dot(w_out, hidden, preferred_element_type=jnp.float32) + b_out[:, None]
    heating = jnp.sum(outputs[:LEV], axis=0)
    return (outputs.astype(jnp.bfloat16), heating)


def mlp_kernel(fin_ref, w_in_ref, b_in_ref, w_mid_ref, b_mid_ref, w_top_ref, b_top_ref,
               w_out_ref, b_out_ref, tend_ref, heat_ref, scratch):
    feats = w_in_ref.shape[1]
    outs = w_out_ref.shape[0]
    height = heat_ref.shape[0]
    width = heat_ref.shape[1]

    def layer(w_ref, b_ref, x):
        a = jnp.dot(w_ref[...], x, preferred_element_type=jnp.float32) + b_ref[...]
        return (a * (0.5 + 0.5 * jnp.tanh(0.5 * a))).astype(jnp.bfloat16)

    for pair in range(height // 2):
        y = 2 * pair
        x = jnp.concatenate(
            [fin_ref[pl.ds(y, feats, stride=height), :], fin_ref[pl.ds(y + 1, feats, stride=height), :]],
            axis=1,
        ).astype(jnp.bfloat16)
        h = layer(w_in_ref, b_in_ref, x)
        h = layer(w_mid_ref, b_mid_ref, h)
        h = layer(w_top_ref, b_top_ref, h)
        out = jnp.dot(w_out_ref[...], h, preferred_element_type=jnp.float32) + b_out_ref[...]
        heat = jnp.sum(out[:LEV], axis=0, keepdims=True)
        heat_ref[y : y + 1, :] = heat[:, :width]
        heat_ref[y + 1 : y + 2, :] = heat[:, width:]
        scratch[pl.ds(y, outs, stride=height), :] = out[:, :width]
        scratch[pl.ds(y + 1, outs, stride=height), :] = out[:, width:]
    tend_ref[...] = scratch[...].astype(jnp.bfloat16)


def run_mlp(fin, height, w_in, b_in, w_mid, b_mid, w_top, b_top, w_out, b_out):
    width = fin.shape[1]
    outs = w_out.shape[0]
    col = lambda b: b.reshape(-1, 1)
    return pl.pallas_call(
        mlp_kernel,
        out_shape=[
            jax.ShapeDtypeStruct((outs * height, width), jnp.bfloat16),
            jax.ShapeDtypeStruct((height, width), jnp.float32),
        ],
        scratch_shapes=[pltpu.VMEM((outs * height, width), jnp.float32)],
        compiler_params=pltpu.CompilerParams(vmem_limit_bytes=48 * 1024 * 1024),
    )(fin, w_in, col(b_in), w_mid, col(b_mid), w_top, col(b_top), w_out, col(b_out))


def local(state, speed_x, speed_y, w_in, b_in, w_mid, b_mid, w_top, b_top, w_out, b_out, span_of):
    feats, height, breadth = state.shape
    across = np.kron(np.eye(breadth // NP, dtype=np.float32), TABLE.T)
    ahi_np = across.astype(jnp.bfloat16)
    alo_np = (across - ahi_np.astype(np.float32)).astype(jnp.bfloat16)
    ahi = jnp.asarray(ahi_np)
    alo = jnp.asarray(alo_np)
    sx = jnp.broadcast_to(speed_x[:, None], (feats, breadth))
    sy = jnp.broadcast_to(speed_y[:, None], (feats, breadth))
    v0 = state.reshape(feats * height, breadth)
    ex, ey = run_section(v0, None, sx, sy, ahi, alo, None, first=True, combo=None, edges=True)
    field = v0
    combos = [(None, None), (0.75, 0.25), ("third", None)]
    for k, combo in enumerate(combos):
        halos = exchange(ex, ey)
        outs = run_section(
            field, v0, sx, sy, ahi, alo, halos, first=False, combo=combo, edges=k < 2
        )
        if k < 2:
            field, ex, ey = outs
        else:
            (field,) = outs
    final_state = field.reshape(feats, height, breadth)
    column_count = height * breadth
    target = span_of.reshape(column_count)
    devices = lax.axis_size("face") * lax.axis_size("elem")
    span_ids = jnp.arange(devices, dtype=jnp.int32)
    tend_rows, heat_rows = run_mlp(field, height, w_in, b_in, w_mid, b_mid, w_top, b_top, w_out, b_out)
    heating = heat_rows.reshape(column_count)
    member = (target[:, None] == span_ids[None, :]).astype(jnp.float32)
    partial_sums = jnp.sum(member * heating[:, None], axis=0)
    received = lax.all_to_all(
        partial_sums.reshape(devices, 1), ("face", "elem"), 0, 1, tiled=True
    )
    span_heating = jnp.sum(received, axis=1) / column_count
    tendencies = tend_rows.reshape(-1, height, breadth)
    return (final_state, tendencies, span_heating)


def solution(mesh):
    return jax.shard_map(
        local,
        mesh=mesh,
        in_specs=(
            P(None, "face", "elem"),
            P(),
            P(),
            P(),
            P(),
            P(),
            P(),
            P(),
            P(),
            P(),
            P(),
            P("face", "elem", None, None),
        ),
        out_specs=(P(None, "face", "elem"), P(None, "face", "elem"), P(("face", "elem"))),
        check_vma=False,
    )
```

```python
import functools
import math

import jax
import jax.numpy as jnp
import numpy as np
from jax import lax
from jax.experimental import pallas as pl
from jax.experimental.pallas import tpu as pltpu
from jax.sharding import PartitionSpec as P

NP = 4
LEV = 72
CHUNK = 48
FOLD = CHUNK // 2


def gll_matrix():
    inner_node = 1.0 / math.sqrt(5.0)
    gll_nodes = np.array([-1.0, -inner_node, inner_node, 1.0])
    weights = np.array(
        [
            1.0
            / np.prod([gll_nodes[outer] - gll_nodes[other] for other in range(4) if other != outer])
            for outer in range(4)
        ]
    )
    matrix = np.zeros((4, 4))
    for outer in range(4):
        for inner in range(4):
            if inner != outer:
                matrix[outer, inner] = (
                    weights[inner] / weights[outer] / (gll_nodes[outer] - gll_nodes[inner])
                )
    for outer in range(4):
        matrix[outer, outer] = -np.sum(matrix[outer])
    return matrix.astype(np.float32)


TABLE = gll_matrix()


def lanes(shape):
    return lax.broadcasted_iota(jnp.int32, shape, len(shape) - 1)


def roll(x, shift):
    shift = shift % x.shape[-1]
    return x if shift == 0 else pltpu.roll(x, shift, x.ndim - 1)


def raw_slabs(slabs, sx, sy, ahi, alo):
    rows = slabs[0].shape[0]
    stacked = jnp.concatenate(slabs, axis=0)
    hi = stacked.astype(jnp.bfloat16)
    lo = (stacked - hi.astype(jnp.float32)).astype(jnp.bfloat16)
    along_x = (
        jnp.dot(hi, ahi, preferred_element_type=jnp.float32)
        + jnp.dot(hi, alo, preferred_element_type=jnp.float32)
        + jnp.dot(lo, ahi, preferred_element_type=jnp.float32)
    )
    out = []
    for y, _ in enumerate(slabs):
        base = (y // NP) * NP
        j = y % NP
        along_y = float(TABLE[j, 0]) * slabs[base]
        for i in range(1, NP):
            along_y = along_y + float(TABLE[j, i]) * slabs[base + i]
        dx = along_x[y * rows : (y + 1) * rows]
        out.append(-(sx * dx + sy * along_y))
    return out


def pack_edges(tend):
    rows, width = tend[0].shape
    lane = lanes((rows, width))
    acc = jnp.zeros((rows, width), jnp.float32)
    for y, t in enumerate(tend):
        acc = jnp.where(lane == 2 * y, roll(t, 2 * y), acc)
        acc = jnp.where(lane == 2 * y + 1, roll(t, 2 * y + 2), acc)
    half = rows // 2
    lane_h = lanes((half, width))
    return jnp.where(lane_h < 32, acc[:half], roll(acc[half:], 32))


def unpack_edges(block):
    return jnp.concatenate([block, roll(block, 96)], axis=0)


def stiff_x(t, right_edges, left_edges, y):
    rows, width = t.shape
    lane = lanes((rows, width))
    right = jnp.where(lane == width - 1, roll(right_edges, width - 1 - 2 * y), roll(t, width - 1))
    left = jnp.where(lane == 0, roll(left_edges, width - 1 - 2 * y), roll(t, 1))
    place = lane % NP
    return jnp.where(
        place == NP - 1, 0.5 * (t + right), jnp.where(place == 0, 0.5 * (left + t), t)
    )


def section_kernel(*refs, first, combo, edges):
    refs = list(refs)
    v0_ref = None if combo is None or combo[0] is None else refs.pop(0)
    sp_ref = refs.pop(0)
    sx_ref, sy_ref, ahi_ref, alo_ref = refs[:4]
    refs = refs[4:]
    if not first:
        exr_ref, exl_ref, dr_ref, dl_ref, top_ref, bottom_ref = refs[:6]
        refs = refs[6:]
    rows = CHUNK
    height = 16
    sx = sx_ref[...]
    sy = sy_ref[...]
    ahi = ahi_ref[...]
    alo = alo_ref[...]
    slabs = [sp_ref[pl.ds(y, rows, stride=height), :] for y in range(height)]
    tend = raw_slabs(slabs, sx, sy, ahi, alo)
    if first:
        ex_ref, ey_ref = refs
        ex_ref[...] = pack_edges(tend)
        ey_ref[0] = tend[0]
        ey_ref[1] = tend[height - 1]
        return
    exr = unpack_edges(exr_ref[...])
    exl = unpack_edges(exl_ref[...])
    dr = unpack_edges(dr_ref[...])
    dl = unpack_edges(dl_ref[...])
    tx = [stiff_x(t, exr, exl, y) for y, t in enumerate(tend)]
    down = stiff_x(top_ref[...], dr, dl, 0)
    up = stiff_x(bottom_ref[...], dr, dl, height - 1)
    ext = [up] + tx + [down]
    new = []
    for y in range(height):
        cur = ext[y + 1]
        if y % NP == NP - 1:
            op = 0.5 * (cur + ext[y + 2])
        elif y % NP == 0:
            op = 0.5 * (ext[y] + cur)
        else:
            op = cur
        inner = slabs[y] + op
        if combo[0] is None:
            val = inner
        else:
            v0 = v0_ref[pl.ds(y, rows, stride=height), :]
            if combo[0] == "third":
                val = v0 / 3.0 + 2.0 / 3.0 * inner
            else:
                val = combo[0] * v0 + combo[1] * inner
        new.append(val)
    out_ref = refs[0]
    for y in range(height):
        out_ref[pl.ds(y, rows, stride=height), :] = new[y]
    if edges:
        ex_ref, ey_ref = refs[1:3]
        tend = raw_slabs(new, sx, sy, ahi, alo)
        ex_ref[...] = pack_edges(tend)
        ey_ref[0] = tend[0]
        ey_ref[1] = tend[height - 1]


def run_section(field_rows, v0, sx, sy, ahi, alo, halos, *, first, combo, edges):
    total, width = field_rows.shape
    feats = sx.shape[0]
    steps = feats // CHUNK
    big = pl.BlockSpec((CHUNK * 16, width), lambda i: (i, 0))
    small = pl.BlockSpec((CHUNK, width), lambda i: (i, 0))
    const = pl.BlockSpec((width, width), lambda i: (0, 0))
    edge = pl.BlockSpec((FOLD, width), lambda i: (i, 0))
    rowsb = pl.BlockSpec((2, CHUNK, width), lambda i: (0, i, 0))
    args, specs = [], []
    if combo is not None and combo[0] is not None:
        args.append(v0)
        specs.append(big)
    args += [field_rows, sx, sy, ahi, alo]
    specs += [big, small, small, const, const]
    if not first:
        exr, exl, partner = halos
        blocks = field_rows.shape[0] // (CHUNK * 16)
        args += [exr, exl, partner, partner, partner, partner]
        specs += [
            edge,
            edge,
            pl.BlockSpec((FOLD, width), lambda i: (4 * blocks + i, 0)),
            pl.BlockSpec((FOLD, width), lambda i: (5 * blocks + i, 0)),
            pl.BlockSpec((CHUNK, width), lambda i: (i, 0)),
            pl.BlockSpec((CHUNK, width), lambda i: (blocks + i, 0)),
        ]
    out_shape, out_specs = [], []
    ex_shape = jax.ShapeDtypeStruct((feats // 2, width), jnp.float32)
    ey_shape = jax.ShapeDtypeStruct((2, feats, width), jnp.float32)
    if first:
        out_shape = [ex_shape, ey_shape]
        out_specs = [edge, rowsb]
    else:
        out_shape = [jax.ShapeDtypeStruct((total, width), jnp.float32)]
        out_specs = [big]
        if edges:
            out_shape += [ex_shape, ey_shape]
            out_specs += [edge, rowsb]
    kernel = functools.partial(section_kernel, first=first, combo=combo, edges=edges)
    return pl.pallas_call(
        kernel,
        grid=(steps,),
        in_specs=specs,
        out_specs=out_specs,
        out_shape=out_shape,
        compiler_params=pltpu.CompilerParams(vmem_limit_bytes=48 * 1024 * 1024),
    )(*args)


def exchange(ex, ey):
    n_face = lax.axis_size("face")
    n_elem = lax.axis_size("elem")
    assert n_face == 2
    from_right = [(j, (j - 1) % n_elem) for j in range(n_elem)]
    from_left = [(j, (j + 1) % n_elem) for j in range(n_elem)]
    exr = lax.ppermute(ex, "elem", from_right)
    exl = lax.ppermute(ex, "elem", from_left)
    feats = ey.shape[1]
    bundle = jnp.concatenate([ey.reshape(2 * feats, ey.shape[2]), exr, exl], axis=0)
    partner = lax.ppermute(bundle, "face", [(0, 1), (1, 0)])
    return (exr, exl, partner)


def column_model(inputs, w_in, b_in, w_mid, b_mid, w_top, b_top, w_out, b_out):
    hidden = jax.nn.silu(
        jnp.dot(w_in, inputs, preferred_element_type=jnp.float32) + b_in[:, None]
    ).astype(jnp.bfloat16)
    hidden = jax.nn.silu(
        jnp.dot(w_mid, hidden, preferred_element_type=jnp.float32) + b_mid[:, None]
    ).astype(jnp.bfloat16)
    hidden = jax.nn.silu(
        jnp.dot(w_top, hidden, preferred_element_type=jnp.float32) + b_top[:, None]
    ).astype(jnp.bfloat16)
    outputs = jnp.dot(w_out, hidden, preferred_element_type=jnp.float32) + b_out[:, None]
    heating = jnp.sum(outputs[:LEV], axis=0)
    return (outputs.astype(jnp.bfloat16), heating)


def mlp_kernel(fin_ref, w_in_ref, w_mid_ref, w_top_ref, w_out_ref, b_ref, tend_ref, heat_ref, scratch):
    feats = w_in_ref.shape[0]
    outs = w_out_ref.shape[0]
    height = heat_ref.shape[0]
    width = heat_ref.shape[1]

    def act(a):
        return (a * (0.5 + 0.5 * jnp.tanh(0.5 * a))).astype(jnp.bfloat16)

    hid = w_mid_ref.shape[0]
    b_in = b_ref[0:hid]
    b_mid = b_ref[hid : 2 * hid]
    b_top = b_ref[2 * hid : 3 * hid]
    b_out = b_ref[3 * hid : 3 * hid + outs]

    for pair in range(height // 2):
        y = 2 * pair
        x = jnp.concatenate(
            [fin_ref[pl.ds(y, feats, stride=height), :], fin_ref[pl.ds(y + 1, feats, stride=height), :]],
            axis=1,
        ).astype(jnp.bfloat16)
        h = act(
            lax.dot_general(
                w_in_ref[...], x, (((0,), (0,)), ((), ())), preferred_element_type=jnp.float32
            )
            + b_in
        )
        h = act(jnp.dot(w_mid_ref[...], h, preferred_element_type=jnp.float32) + b_mid)
        h = act(jnp.dot(w_top_ref[...], h, preferred_element_type=jnp.float32) + b_top)
        out = jnp.dot(w_out_ref[...], h, preferred_element_type=jnp.float32) + b_out
        heat = jnp.sum(out[:LEV], axis=0, keepdims=True)
        heat_ref[y : y + 1, :] = heat[:, :width]
        heat_ref[y + 1 : y + 2, :] = heat[:, width:]
        scratch[pl.ds(y, outs, stride=height), :] = out[:, :width]
        scratch[pl.ds(y + 1, outs, stride=height), :] = out[:, width:]
    tend_ref[...] = scratch[...].astype(jnp.bfloat16)


def run_mlp(fin, height, w_in, b_in, w_mid, b_mid, w_top, b_top, w_out, b_out):
    width = fin.shape[1]
    outs = w_out.shape[0]
    biases = jnp.concatenate([b_in, b_mid, b_top, b_out]).reshape(-1, 1)
    return pl.pallas_call(
        mlp_kernel,
        out_shape=[
            jax.ShapeDtypeStruct((outs * height, width), jnp.bfloat16),
            jax.ShapeDtypeStruct((height, width), jnp.float32),
        ],
        scratch_shapes=[pltpu.VMEM((outs * height, width), jnp.float32)],
        compiler_params=pltpu.CompilerParams(vmem_limit_bytes=48 * 1024 * 1024),
    )(fin, w_in.T, w_mid, w_top, w_out, biases)


def local(state, speed_x, speed_y, w_in, b_in, w_mid, b_mid, w_top, b_top, w_out, b_out, span_of):
    feats, height, breadth = state.shape
    across = np.kron(np.eye(breadth // NP, dtype=np.float32), TABLE.T)
    ahi_np = across.astype(jnp.bfloat16)
    alo_np = (across - ahi_np.astype(np.float32)).astype(jnp.bfloat16)
    ahi = jnp.asarray(ahi_np)
    alo = jnp.asarray(alo_np)
    sx = jnp.broadcast_to(speed_x[:, None], (feats, breadth))
    sy = jnp.broadcast_to(speed_y[:, None], (feats, breadth))
    v0 = state.reshape(feats * height, breadth)
    ex, ey = run_section(v0, None, sx, sy, ahi, alo, None, first=True, combo=None, edges=True)
    field = v0
    combos = [(None, None), (0.75, 0.25), ("third", None)]
    for k, combo in enumerate(combos):
        halos = exchange(ex, ey)
        outs = run_section(
            field, v0, sx, sy, ahi, alo, halos, first=False, combo=combo, edges=k < 2
        )
        if k < 2:
            field, ex, ey = outs
        else:
            (field,) = outs
    final_state = field.reshape(feats, height, breadth)
    column_count = height * breadth
    target = span_of.reshape(column_count)
    devices = lax.axis_size("face") * lax.axis_size("elem")
    span_ids = jnp.arange(devices, dtype=jnp.int32)
    tend_rows, heat_rows = run_mlp(field, height, w_in, b_in, w_mid, b_mid, w_top, b_top, w_out, b_out)
    heating = heat_rows.reshape(column_count)
    member = (target[:, None] == span_ids[None, :]).astype(jnp.float32)
    partial_sums = jnp.sum(member * heating[:, None], axis=0)
    received = lax.all_to_all(
        partial_sums.reshape(devices, 1), ("face", "elem"), 0, 1, tiled=True
    )
    span_heating = jnp.sum(received, axis=1) / column_count
    tendencies = tend_rows.reshape(-1, height, breadth)
    return (final_state, tendencies, span_heating)


def solution(mesh):
    return jax.shard_map(
        local,
        mesh=mesh,
        in_specs=(
            P(None, "face", "elem"),
            P(),
            P(),
            P(),
            P(),
            P(),
            P(),
            P(),
            P(),
            P(),
            P(),
            P("face", "elem", None, None),
        ),
        out_specs=(P(None, "face", "elem"), P(None, "face", "elem"), P(("face", "elem"))),
        check_vma=False,
    )
```

```python
import functools
import math

import jax
import jax.numpy as jnp
import numpy as np
from jax import lax
from jax.experimental import pallas as pl
from jax.experimental.pallas import tpu as pltpu
from jax.sharding import PartitionSpec as P

NP = 4
LEV = 72
CHUNK = 48
FOLD = CHUNK // 2


def gll_matrix():
    inner_node = 1.0 / math.sqrt(5.0)
    gll_nodes = np.array([-1.0, -inner_node, inner_node, 1.0])
    weights = np.array(
        [
            1.0
            / np.prod([gll_nodes[outer] - gll_nodes[other] for other in range(4) if other != outer])
            for outer in range(4)
        ]
    )
    matrix = np.zeros((4, 4))
    for outer in range(4):
        for inner in range(4):
            if inner != outer:
                matrix[outer, inner] = (
                    weights[inner] / weights[outer] / (gll_nodes[outer] - gll_nodes[inner])
                )
    for outer in range(4):
        matrix[outer, outer] = -np.sum(matrix[outer])
    return matrix.astype(np.float32)


TABLE = gll_matrix()


def lanes(shape):
    return lax.broadcasted_iota(jnp.int32, shape, len(shape) - 1)


def roll(x, shift):
    shift = shift % x.shape[-1]
    return x if shift == 0 else pltpu.roll(x, shift, x.ndim - 1)


def raw_slabs(slabs, sx, sy, ahi, alo):
    rows = slabs[0].shape[0]
    stacked = jnp.concatenate(slabs, axis=0)
    hi = stacked.astype(jnp.bfloat16)
    lo = (stacked - hi.astype(jnp.float32)).astype(jnp.bfloat16)
    along_x = (
        jnp.dot(hi, ahi, preferred_element_type=jnp.float32)
        + jnp.dot(hi, alo, preferred_element_type=jnp.float32)
        + jnp.dot(lo, ahi, preferred_element_type=jnp.float32)
    )
    out = []
    for y, _ in enumerate(slabs):
        base = (y // NP) * NP
        j = y % NP
        along_y = float(TABLE[j, 0]) * slabs[base]
        for i in range(1, NP):
            along_y = along_y + float(TABLE[j, i]) * slabs[base + i]
        dx = along_x[y * rows : (y + 1) * rows]
        out.append(-(sx * dx + sy * along_y))
    return out


def pack_edges(tend):
    rows, width = tend[0].shape
    lane = lanes((rows, width))
    acc = jnp.zeros((rows, width), jnp.float32)
    for y, t in enumerate(tend):
        acc = jnp.where(lane == 2 * y, roll(t, 2 * y), acc)
        acc = jnp.where(lane == 2 * y + 1, roll(t, 2 * y + 2), acc)
    half = rows // 2
    lane_h = lanes((half, width))
    return jnp.where(lane_h < 32, acc[:half], roll(acc[half:], 32))


def unpack_edges(block):
    return jnp.concatenate([block, roll(block, 96)], axis=0)


def stiff_x(t, right_edges, left_edges, y):
    rows, width = t.shape
    lane = lanes((rows, width))
    right = jnp.where(lane == width - 1, roll(right_edges, width - 1 - 2 * y), roll(t, width - 1))
    left = jnp.where(lane == 0, roll(left_edges, width - 1 - 2 * y), roll(t, 1))
    place = lane % NP
    return jnp.where(
        place == NP - 1, 0.5 * (t + right), jnp.where(place == 0, 0.5 * (left + t), t)
    )


def section_kernel(*refs, first, combo, edges):
    refs = list(refs)
    v0_ref = None if combo is None or combo[0] is None else refs.pop(0)
    sp_ref = refs.pop(0)
    sx_ref, sy_ref, ahi_ref, alo_ref = refs[:4]
    refs = refs[4:]
    if not first:
        exr_ref, exl_ref, dr_ref, dl_ref, top_ref, bottom_ref = refs[:6]
        refs = refs[6:]
    rows = CHUNK
    height = 16
    sx = sx_ref[...]
    sy = sy_ref[...]
    ahi = ahi_ref[...]
    alo = alo_ref[...]
    slabs = [sp_ref[pl.ds(y, rows, stride=height), :] for y in range(height)]
    tend = raw_slabs(slabs, sx, sy, ahi, alo)
    if first:
        ex_ref, ey_ref = refs
        ex_ref[...] = pack_edges(tend)
        ey_ref[0] = tend[0]
        ey_ref[1] = tend[height - 1]
        return
    exr = unpack_edges(exr_ref[...])
    exl = unpack_edges(exl_ref[...])
    dr = unpack_edges(dr_ref[...])
    dl = unpack_edges(dl_ref[...])
    tx = [stiff_x(t, exr, exl, y) for y, t in enumerate(tend)]
    down = stiff_x(top_ref[...], dr, dl, 0)
    up = stiff_x(bottom_ref[...], dr, dl, height - 1)
    ext = [up] + tx + [down]
    new = []
    for y in range(height):
        cur = ext[y + 1]
        if y % NP == NP - 1:
            op = 0.5 * (cur + ext[y + 2])
        elif y % NP == 0:
            op = 0.5 * (ext[y] + cur)
        else:
            op = cur
        inner = slabs[y] + op
        if combo[0] is None:
            val = inner
        else:
            v0 = v0_ref[pl.ds(y, rows, stride=height), :]
            if combo[0] == "third":
                val = v0 / 3.0 + 2.0 / 3.0 * inner
            else:
                val = combo[0] * v0 + combo[1] * inner
        new.append(val)
    out_ref = refs[0]
    for y in range(height):
        out_ref[pl.ds(y, rows, stride=height), :] = new[y]
    if edges:
        ex_ref, ey_ref = refs[1:3]
        tend = raw_slabs(new, sx, sy, ahi, alo)
        ex_ref[...] = pack_edges(tend)
        ey_ref[0] = tend[0]
        ey_ref[1] = tend[height - 1]


def run_section(field_rows, v0, sx, sy, ahi, alo, halos, *, first, combo, edges):
    total, width = field_rows.shape
    feats = sx.shape[0]
    steps = feats // CHUNK
    big = pl.BlockSpec((CHUNK * 16, width), lambda i: (i, 0))
    small = pl.BlockSpec((CHUNK, width), lambda i: (i, 0))
    const = pl.BlockSpec((width, width), lambda i: (0, 0))
    edge = pl.BlockSpec((FOLD, width), lambda i: (i, 0))
    rowsb = pl.BlockSpec((2, CHUNK, width), lambda i: (0, i, 0))
    args, specs = [], []
    if combo is not None and combo[0] is not None:
        args.append(v0)
        specs.append(big)
    args += [field_rows, sx, sy, ahi, alo]
    specs += [big, small, small, const, const]
    if not first:
        exr, exl, partner = halos
        blocks = field_rows.shape[0] // (CHUNK * 16)
        args += [exr, exl, partner, partner, partner, partner]
        specs += [
            edge,
            edge,
            pl.BlockSpec((FOLD, width), lambda i: (4 * blocks + i, 0)),
            pl.BlockSpec((FOLD, width), lambda i: (5 * blocks + i, 0)),
            pl.BlockSpec((CHUNK, width), lambda i: (i, 0)),
            pl.BlockSpec((CHUNK, width), lambda i: (blocks + i, 0)),
        ]
    out_shape, out_specs = [], []
    ex_shape = jax.ShapeDtypeStruct((feats // 2, width), jnp.float32)
    ey_shape = jax.ShapeDtypeStruct((2, feats, width), jnp.float32)
    if first:
        out_shape = [ex_shape, ey_shape]
        out_specs = [edge, rowsb]
    else:
        out_shape = [jax.ShapeDtypeStruct((total, width), jnp.float32)]
        out_specs = [big]
        if edges:
            out_shape += [ex_shape, ey_shape]
            out_specs += [edge, rowsb]
    kernel = functools.partial(section_kernel, first=first, combo=combo, edges=edges)
    return pl.pallas_call(
        kernel,
        grid=(steps,),
        in_specs=specs,
        out_specs=out_specs,
        out_shape=out_shape,
        compiler_params=pltpu.CompilerParams(vmem_limit_bytes=60 * 1024 * 1024),
    )(*args)


def exchange(ex, ey):
    n_face = lax.axis_size("face")
    n_elem = lax.axis_size("elem")
    assert n_face == 2
    from_right = [(j, (j - 1) % n_elem) for j in range(n_elem)]
    from_left = [(j, (j + 1) % n_elem) for j in range(n_elem)]
    exr = lax.ppermute(ex, "elem", from_right)
    exl = lax.ppermute(ex, "elem", from_left)
    feats = ey.shape[1]
    bundle = jnp.concatenate([ey.reshape(2 * feats, ey.shape[2]), exr, exl], axis=0)
    partner = lax.ppermute(bundle, "face", [(0, 1), (1, 0)])
    return (exr, exl, partner)


def column_model(inputs, w_in, b_in, w_mid, b_mid, w_top, b_top, w_out, b_out):
    hidden = jax.nn.silu(
        jnp.dot(w_in, inputs, preferred_element_type=jnp.float32) + b_in[:, None]
    ).astype(jnp.bfloat16)
    hidden = jax.nn.silu(
        jnp.dot(w_mid, hidden, preferred_element_type=jnp.float32) + b_mid[:, None]
    ).astype(jnp.bfloat16)
    hidden = jax.nn.silu(
        jnp.dot(w_top, hidden, preferred_element_type=jnp.float32) + b_top[:, None]
    ).astype(jnp.bfloat16)
    outputs = jnp.dot(w_out, hidden, preferred_element_type=jnp.float32) + b_out[:, None]
    heating = jnp.sum(outputs[:LEV], axis=0)
    return (outputs.astype(jnp.bfloat16), heating)


def mlp_kernel(fin_ref, w_in_ref, w_mid_ref, w_top_ref, w_out_ref, b_ref, tend_ref, heat_ref, scratch):
    feats = w_in_ref.shape[0]
    outs = w_out_ref.shape[0]
    height = heat_ref.shape[0]
    width = heat_ref.shape[1]

    def act(a):
        return (a * (0.5 + 0.5 * jnp.tanh(0.5 * a))).astype(jnp.bfloat16)

    hid = w_mid_ref.shape[0]
    b_in = b_ref[0:hid]
    b_mid = b_ref[hid : 2 * hid]
    b_top = b_ref[2 * hid : 3 * hid]
    b_out = b_ref[3 * hid : 3 * hid + outs]

    for pair in range(height // 2):
        y = 2 * pair
        x = jnp.concatenate(
            [fin_ref[pl.ds(y, feats, stride=height), :], fin_ref[pl.ds(y + 1, feats, stride=height), :]],
            axis=1,
        ).astype(jnp.bfloat16)
        h = act(
            lax.dot_general(
                w_in_ref[...], x, (((0,), (0,)), ((), ())), preferred_element_type=jnp.float32
            )
            + b_in
        )
        h = act(jnp.dot(w_mid_ref[...], h, preferred_element_type=jnp.float32) + b_mid)
        h = act(jnp.dot(w_top_ref[...], h, preferred_element_type=jnp.float32) + b_top)
        out = jnp.dot(w_out_ref[...], h, preferred_element_type=jnp.float32) + b_out
        heat = jnp.sum(out[:LEV], axis=0, keepdims=True)
        heat_ref[y : y + 1, :] = heat[:, :width]
        heat_ref[y + 1 : y + 2, :] = heat[:, width:]
        scratch[pl.ds(y, outs, stride=height), :] = out[:, :width]
        scratch[pl.ds(y + 1, outs, stride=height), :] = out[:, width:]
    tend_ref[...] = scratch[...].astype(jnp.bfloat16)


def run_mlp(fin, height, w_in, b_in, w_mid, b_mid, w_top, b_top, w_out, b_out):
    width = fin.shape[1]
    outs = w_out.shape[0]
    biases = jnp.concatenate([b_in, b_mid, b_top, b_out]).reshape(-1, 1)
    return pl.pallas_call(
        mlp_kernel,
        out_shape=[
            jax.ShapeDtypeStruct((outs * height, width), jnp.bfloat16),
            jax.ShapeDtypeStruct((height, width), jnp.float32),
        ],
        scratch_shapes=[pltpu.VMEM((outs * height, width), jnp.float32)],
        compiler_params=pltpu.CompilerParams(vmem_limit_bytes=60 * 1024 * 1024),
    )(fin, w_in.T, w_mid, w_top, w_out, biases)


def local(state, speed_x, speed_y, w_in, b_in, w_mid, b_mid, w_top, b_top, w_out, b_out, span_of):
    feats, height, breadth = state.shape
    across = np.kron(np.eye(breadth // NP, dtype=np.float32), TABLE.T)
    ahi_np = across.astype(jnp.bfloat16)
    alo_np = (across - ahi_np.astype(np.float32)).astype(jnp.bfloat16)
    ahi = jnp.asarray(ahi_np)
    alo = jnp.asarray(alo_np)
    sx = jnp.broadcast_to(speed_x[:, None], (feats, breadth))
    sy = jnp.broadcast_to(speed_y[:, None], (feats, breadth))
    v0 = state.reshape(feats * height, breadth)
    ex, ey = run_section(v0, None, sx, sy, ahi, alo, None, first=True, combo=None, edges=True)
    field = v0
    combos = [(None, None), (0.75, 0.25), ("third", None)]
    for k, combo in enumerate(combos):
        halos = exchange(ex, ey)
        outs = run_section(
            field, v0, sx, sy, ahi, alo, halos, first=False, combo=combo, edges=k < 2
        )
        if k < 2:
            field, ex, ey = outs
        else:
            (field,) = outs
    final_state = field.reshape(feats, height, breadth)
    column_count = height * breadth
    target = span_of.reshape(column_count)
    devices = lax.axis_size("face") * lax.axis_size("elem")
    span_ids = jnp.arange(devices, dtype=jnp.int32)
    tend_rows, heat_rows = run_mlp(field, height, w_in, b_in, w_mid, b_mid, w_top, b_top, w_out, b_out)
    heating = heat_rows.reshape(column_count)
    member = (target[:, None] == span_ids[None, :]).astype(jnp.float32)
    partial_sums = jnp.sum(member * heating[:, None], axis=0)
    received = lax.all_to_all(
        partial_sums.reshape(devices, 1), ("face", "elem"), 0, 1, tiled=True
    )
    span_heating = jnp.sum(received, axis=1) / column_count
    tendencies = tend_rows.reshape(-1, height, breadth)
    return (final_state, tendencies, span_heating)


def solution(mesh):
    return jax.shard_map(
        local,
        mesh=mesh,
        in_specs=(
            P(None, "face", "elem"),
            P(),
            P(),
            P(),
            P(),
            P(),
            P(),
            P(),
            P(),
            P(),
            P(),
            P("face", "elem", None, None),
        ),
        out_specs=(P(None, "face", "elem"), P(None, "face", "elem"), P(("face", "elem"))),
        check_vma=False,
    )
```

```python
import functools
import math

import jax
import jax.numpy as jnp
import numpy as np
from jax import lax
from jax.experimental import pallas as pl
from jax.experimental.pallas import tpu as pltpu
from jax.sharding import PartitionSpec as P

NP = 4
LEV = 72
CHUNK = 48
FOLD = CHUNK // 2


def gll_matrix():
    inner_node = 1.0 / math.sqrt(5.0)
    gll_nodes = np.array([-1.0, -inner_node, inner_node, 1.0])
    weights = np.array(
        [
            1.0
            / np.prod([gll_nodes[outer] - gll_nodes[other] for other in range(4) if other != outer])
            for outer in range(4)
        ]
    )
    matrix = np.zeros((4, 4))
    for outer in range(4):
        for inner in range(4):
            if inner != outer:
                matrix[outer, inner] = (
                    weights[inner] / weights[outer] / (gll_nodes[outer] - gll_nodes[inner])
                )
    for outer in range(4):
        matrix[outer, outer] = -np.sum(matrix[outer])
    return matrix.astype(np.float32)


TABLE = gll_matrix()


def lanes(shape):
    return lax.broadcasted_iota(jnp.int32, shape, len(shape) - 1)


def roll(x, shift):
    shift = shift % x.shape[-1]
    return x if shift == 0 else pltpu.roll(x, shift, x.ndim - 1)


def raw_slabs(slabs, sx, sy, ahi, alo):
    rows = slabs[0].shape[0]
    stacked = jnp.concatenate(slabs, axis=0)
    hi = stacked.astype(jnp.bfloat16)
    lo = (stacked - hi.astype(jnp.float32)).astype(jnp.bfloat16)
    along_x = (
        jnp.dot(hi, ahi, preferred_element_type=jnp.float32)
        + jnp.dot(hi, alo, preferred_element_type=jnp.float32)
        + jnp.dot(lo, ahi, preferred_element_type=jnp.float32)
    )
    out = []
    for y, _ in enumerate(slabs):
        base = (y // NP) * NP
        j = y % NP
        along_y = float(TABLE[j, 0]) * slabs[base]
        for i in range(1, NP):
            along_y = along_y + float(TABLE[j, i]) * slabs[base + i]
        dx = along_x[y * rows : (y + 1) * rows]
        out.append(-(sx * dx + sy * along_y))
    return out


def pack_edges(tend):
    rows, width = tend[0].shape
    lane = lanes((rows, width))
    acc = jnp.zeros((rows, width), jnp.float32)
    for y, t in enumerate(tend):
        acc = jnp.where(lane == 2 * y, roll(t, 2 * y), acc)
        acc = jnp.where(lane == 2 * y + 1, roll(t, 2 * y + 2), acc)
    half = rows // 2
    lane_h = lanes((half, width))
    return jnp.where(lane_h < 32, acc[:half], roll(acc[half:], 32))


def unpack_edges(block):
    return jnp.concatenate([block, roll(block, 96)], axis=0)


def stiff_x(t, right_edges, left_edges, y):
    rows, width = t.shape
    lane = lanes((rows, width))
    right = jnp.where(lane == width - 1, roll(right_edges, width - 1 - 2 * y), roll(t, width - 1))
    left = jnp.where(lane == 0, roll(left_edges, width - 1 - 2 * y), roll(t, 1))
    place = lane % NP
    return jnp.where(
        place == NP - 1, 0.5 * (t + right), jnp.where(place == 0, 0.5 * (left + t), t)
    )


def section_kernel(*refs, first, combo, edges):
    refs = list(refs)
    v0_ref = None if combo is None or combo[0] is None else refs.pop(0)
    sp_ref = refs.pop(0)
    sx_ref, sy_ref, ahi_ref, alo_ref = refs[:4]
    refs = refs[4:]
    if not first:
        exr_ref, exl_ref, dr_ref, dl_ref, top_ref, bottom_ref = refs[:6]
        refs = refs[6:]
    rows = CHUNK
    height = 16
    sx = sx_ref[...]
    sy = sy_ref[...]
    ahi = ahi_ref[...]
    alo = alo_ref[...]
    slabs = [sp_ref[pl.ds(y, rows, stride=height), :] for y in range(height)]
    tend = raw_slabs(slabs, sx, sy, ahi, alo)
    if first:
        ex_ref, ey_ref = refs
        ex_ref[...] = pack_edges(tend)
        ey_ref[0] = tend[0]
        ey_ref[1] = tend[height - 1]
        return
    exr = unpack_edges(exr_ref[...])
    exl = unpack_edges(exl_ref[...])
    dr = unpack_edges(dr_ref[...])
    dl = unpack_edges(dl_ref[...])
    tx = [stiff_x(t, exr, exl, y) for y, t in enumerate(tend)]
    down = stiff_x(top_ref[...], dr, dl, 0)
    up = stiff_x(bottom_ref[...], dr, dl, height - 1)
    ext = [up] + tx + [down]
    new = []
    for y in range(height):
        cur = ext[y + 1]
        if y % NP == NP - 1:
            op = 0.5 * (cur + ext[y + 2])
        elif y % NP == 0:
            op = 0.5 * (ext[y] + cur)
        else:
            op = cur
        inner = slabs[y] + op
        if combo[0] is None:
            val = inner
        else:
            v0 = v0_ref[pl.ds(y, rows, stride=height), :]
            if combo[0] == "third":
                val = v0 / 3.0 + 2.0 / 3.0 * inner
            else:
                val = combo[0] * v0 + combo[1] * inner
        new.append(val)
    out_ref = refs[0]
    for y in range(height):
        out_ref[pl.ds(y, rows, stride=height), :] = new[y]
    if edges:
        ex_ref, ey_ref = refs[1:3]
        tend = raw_slabs(new, sx, sy, ahi, alo)
        ex_ref[...] = pack_edges(tend)
        ey_ref[0] = tend[0]
        ey_ref[1] = tend[height - 1]


def run_section(field_rows, v0, sx, sy, ahi, alo, halos, *, first, combo, edges):
    total, width = field_rows.shape
    feats = sx.shape[0]
    steps = feats // CHUNK
    big = pl.BlockSpec((CHUNK * 16, width), lambda i: (i, 0))
    small = pl.BlockSpec((CHUNK, width), lambda i: (i, 0))
    const = pl.BlockSpec((width, width), lambda i: (0, 0))
    edge = pl.BlockSpec((FOLD, width), lambda i: (i, 0))
    rowsb = pl.BlockSpec((2, CHUNK, width), lambda i: (0, i, 0))
    args, specs = [], []
    if combo is not None and combo[0] is not None:
        args.append(v0)
        specs.append(big)
    args += [field_rows, sx, sy, ahi, alo]
    specs += [big, small, small, const, const]
    if not first:
        exr, exl, partner = halos
        blocks = field_rows.shape[0] // (CHUNK * 16)
        args += [exr, exl, partner, partner, partner, partner]
        specs += [
            edge,
            edge,
            pl.BlockSpec((FOLD, width), lambda i: (4 * blocks + i, 0)),
            pl.BlockSpec((FOLD, width), lambda i: (5 * blocks + i, 0)),
            pl.BlockSpec((CHUNK, width), lambda i: (i, 0)),
            pl.BlockSpec((CHUNK, width), lambda i: (blocks + i, 0)),
        ]
    out_shape, out_specs = [], []
    ex_shape = jax.ShapeDtypeStruct((feats // 2, width), jnp.float32)
    ey_shape = jax.ShapeDtypeStruct((2, feats, width), jnp.float32)
    if first:
        out_shape = [ex_shape, ey_shape]
        out_specs = [edge, rowsb]
    else:
        out_shape = [jax.ShapeDtypeStruct((total, width), jnp.float32)]
        out_specs = [big]
        if edges:
            out_shape += [ex_shape, ey_shape]
            out_specs += [edge, rowsb]
    kernel = functools.partial(section_kernel, first=first, combo=combo, edges=edges)
    return pl.pallas_call(
        kernel,
        grid=(steps,),
        in_specs=specs,
        out_specs=out_specs,
        out_shape=out_shape,
        compiler_params=pltpu.CompilerParams(vmem_limit_bytes=16 * 1024 * 1024),
    )(*args)


def exchange(ex, ey):
    n_face = lax.axis_size("face")
    n_elem = lax.axis_size("elem")
    assert n_face == 2
    from_right = [(j, (j - 1) % n_elem) for j in range(n_elem)]
    from_left = [(j, (j + 1) % n_elem) for j in range(n_elem)]
    exr = lax.ppermute(ex, "elem", from_right)
    exl = lax.ppermute(ex, "elem", from_left)
    feats = ey.shape[1]
    bundle = jnp.concatenate([ey.reshape(2 * feats, ey.shape[2]), exr, exl], axis=0)
    partner = lax.ppermute(bundle, "face", [(0, 1), (1, 0)])
    return (exr, exl, partner)


def column_model(inputs, w_in, b_in, w_mid, b_mid, w_top, b_top, w_out, b_out):
    hidden = jax.nn.silu(
        jnp.dot(w_in, inputs, preferred_element_type=jnp.float32) + b_in[:, None]
    ).astype(jnp.bfloat16)
    hidden = jax.nn.silu(
        jnp.dot(w_mid, hidden, preferred_element_type=jnp.float32) + b_mid[:, None]
    ).astype(jnp.bfloat16)
    hidden = jax.nn.silu(
        jnp.dot(w_top, hidden, preferred_element_type=jnp.float32) + b_top[:, None]
    ).astype(jnp.bfloat16)
    outputs = jnp.dot(w_out, hidden, preferred_element_type=jnp.float32) + b_out[:, None]
    heating = jnp.sum(outputs[:LEV], axis=0)
    return (outputs.astype(jnp.bfloat16), heating)


def mlp_kernel(fin_ref, w_in_ref, w_mid_ref, w_top_ref, w_out_ref, b_ref, tend_ref, heat_ref, scratch):
    feats = w_in_ref.shape[0]
    outs = w_out_ref.shape[0]
    height = heat_ref.shape[0]
    width = heat_ref.shape[1]

    def act(a):
        return (a * (0.5 + 0.5 * jnp.tanh(0.5 * a))).astype(jnp.bfloat16)

    hid = w_mid_ref.shape[0]
    b_in = b_ref[0:hid]
    b_mid = b_ref[hid : 2 * hid]
    b_top = b_ref[2 * hid : 3 * hid]
    b_out = b_ref[3 * hid : 3 * hid + outs]

    for pair in range(height // 2):
        y = 2 * pair
        x = jnp.concatenate(
            [fin_ref[pl.ds(y, feats, stride=height), :], fin_ref[pl.ds(y + 1, feats, stride=height), :]],
            axis=1,
        ).astype(jnp.bfloat16)
        h = act(
            lax.dot_general(
                w_in_ref[...], x, (((0,), (0,)), ((), ())), preferred_element_type=jnp.float32
            )
            + b_in
        )
        h = act(jnp.dot(w_mid_ref[...], h, preferred_element_type=jnp.float32) + b_mid)
        h = act(jnp.dot(w_top_ref[...], h, preferred_element_type=jnp.float32) + b_top)
        out = jnp.dot(w_out_ref[...], h, preferred_element_type=jnp.float32) + b_out
        heat = jnp.sum(out[:LEV], axis=0, keepdims=True)
        heat_ref[y : y + 1, :] = heat[:, :width]
        heat_ref[y + 1 : y + 2, :] = heat[:, width:]
        scratch[pl.ds(y, outs, stride=height), :] = out[:, :width]
        scratch[pl.ds(y + 1, outs, stride=height), :] = out[:, width:]
    tend_ref[...] = scratch[...].astype(jnp.bfloat16)


def run_mlp(fin, height, w_in, b_in, w_mid, b_mid, w_top, b_top, w_out, b_out):
    width = fin.shape[1]
    outs = w_out.shape[0]
    biases = jnp.concatenate([b_in, b_mid, b_top, b_out]).reshape(-1, 1)
    return pl.pallas_call(
        mlp_kernel,
        out_shape=[
            jax.ShapeDtypeStruct((outs * height, width), jnp.bfloat16),
            jax.ShapeDtypeStruct((height, width), jnp.float32),
        ],
        scratch_shapes=[pltpu.VMEM((outs * height, width), jnp.float32)],
        compiler_params=pltpu.CompilerParams(vmem_limit_bytes=16 * 1024 * 1024),
    )(fin, w_in.T, w_mid, w_top, w_out, biases)


def local(state, speed_x, speed_y, w_in, b_in, w_mid, b_mid, w_top, b_top, w_out, b_out, span_of):
    feats, height, breadth = state.shape
    across = np.kron(np.eye(breadth // NP, dtype=np.float32), TABLE.T)
    ahi_np = across.astype(jnp.bfloat16)
    alo_np = (across - ahi_np.astype(np.float32)).astype(jnp.bfloat16)
    ahi = jnp.asarray(ahi_np)
    alo = jnp.asarray(alo_np)
    sx = jnp.broadcast_to(speed_x[:, None], (feats, breadth))
    sy = jnp.broadcast_to(speed_y[:, None], (feats, breadth))
    v0 = state.reshape(feats * height, breadth)
    ex, ey = run_section(v0, None, sx, sy, ahi, alo, None, first=True, combo=None, edges=True)
    field = v0
    combos = [(None, None), (0.75, 0.25), ("third", None)]
    for k, combo in enumerate(combos):
        halos = exchange(ex, ey)
        outs = run_section(
            field, v0, sx, sy, ahi, alo, halos, first=False, combo=combo, edges=k < 2
        )
        if k < 2:
            field, ex, ey = outs
        else:
            (field,) = outs
    final_state = field.reshape(feats, height, breadth)
    column_count = height * breadth
    target = span_of.reshape(column_count)
    devices = lax.axis_size("face") * lax.axis_size("elem")
    span_ids = jnp.arange(devices, dtype=jnp.int32)
    tend_rows, heat_rows = run_mlp(field, height, w_in, b_in, w_mid, b_mid, w_top, b_top, w_out, b_out)
    heating = heat_rows.reshape(column_count)
    member = (target[:, None] == span_ids[None, :]).astype(jnp.float32)
    partial_sums = jnp.sum(member * heating[:, None], axis=0)
    received = lax.all_to_all(
        partial_sums.reshape(devices, 1), ("face", "elem"), 0, 1, tiled=True
    )
    span_heating = jnp.sum(received, axis=1) / column_count
    tendencies = tend_rows.reshape(-1, height, breadth)
    return (final_state, tendencies, span_heating)


def solution(mesh):
    return jax.shard_map(
        local,
        mesh=mesh,
        in_specs=(
            P(None, "face", "elem"),
            P(),
            P(),
            P(),
            P(),
            P(),
            P(),
            P(),
            P(),
            P(),
            P(),
            P("face", "elem", None, None),
        ),
        out_specs=(P(None, "face", "elem"), P(None, "face", "elem"), P(("face", "elem"))),
        check_vma=False,
    )
```

```python
import functools
import math

import jax
import jax.numpy as jnp
import numpy as np
from jax import lax
from jax.experimental import pallas as pl
from jax.experimental.pallas import tpu as pltpu
from jax.sharding import PartitionSpec as P

NP = 4
LEV = 72
CHUNK = 48
FOLD = CHUNK // 2


def gll_matrix():
    inner_node = 1.0 / math.sqrt(5.0)
    gll_nodes = np.array([-1.0, -inner_node, inner_node, 1.0])
    weights = np.array(
        [
            1.0
            / np.prod([gll_nodes[outer] - gll_nodes[other] for other in range(4) if other != outer])
            for outer in range(4)
        ]
    )
    matrix = np.zeros((4, 4))
    for outer in range(4):
        for inner in range(4):
            if inner != outer:
                matrix[outer, inner] = (
                    weights[inner] / weights[outer] / (gll_nodes[outer] - gll_nodes[inner])
                )
    for outer in range(4):
        matrix[outer, outer] = -np.sum(matrix[outer])
    return matrix.astype(np.float32)


TABLE = gll_matrix()


def lanes(shape):
    return lax.broadcasted_iota(jnp.int32, shape, len(shape) - 1)


def roll(x, shift):
    shift = shift % x.shape[-1]
    return x if shift == 0 else pltpu.roll(x, shift, x.ndim - 1)


def raw_slabs(slabs, sx, sy, ahi, alo):
    rows = slabs[0].shape[0]
    stacked = jnp.concatenate(slabs, axis=0)
    hi = stacked.astype(jnp.bfloat16)
    lo = (stacked - hi.astype(jnp.float32)).astype(jnp.bfloat16)
    along_x = (
        jnp.dot(hi, ahi, preferred_element_type=jnp.float32)
        + jnp.dot(hi, alo, preferred_element_type=jnp.float32)
        + jnp.dot(lo, ahi, preferred_element_type=jnp.float32)
    )
    out = []
    for y, _ in enumerate(slabs):
        base = (y // NP) * NP
        j = y % NP
        along_y = float(TABLE[j, 0]) * slabs[base]
        for i in range(1, NP):
            along_y = along_y + float(TABLE[j, i]) * slabs[base + i]
        dx = along_x[y * rows : (y + 1) * rows]
        out.append(-(sx * dx + sy * along_y))
    return out


def pack_edges(tend):
    rows, width = tend[0].shape
    lane = lanes((rows, width))
    acc = jnp.zeros((rows, width), jnp.float32)
    for y, t in enumerate(tend):
        acc = jnp.where(lane == 2 * y, roll(t, 2 * y), acc)
        acc = jnp.where(lane == 2 * y + 1, roll(t, 2 * y + 2), acc)
    half = rows // 2
    lane_h = lanes((half, width))
    return jnp.where(lane_h < 32, acc[:half], roll(acc[half:], 32))


def unpack_edges(block):
    return jnp.concatenate([block, roll(block, 96)], axis=0)


def stiff_x(t, right_edges, left_edges, y):
    rows, width = t.shape
    lane = lanes((rows, width))
    right = jnp.where(lane == width - 1, roll(right_edges, width - 1 - 2 * y), roll(t, width - 1))
    left = jnp.where(lane == 0, roll(left_edges, width - 1 - 2 * y), roll(t, 1))
    place = lane % NP
    return jnp.where(
        place == NP - 1, 0.5 * (t + right), jnp.where(place == 0, 0.5 * (left + t), t)
    )


def section_kernel(*refs, first, combo, edges):
    refs = list(refs)
    v0_ref = None if combo is None or combo[0] is None else refs.pop(0)
    sp_ref = refs.pop(0)
    sx_ref, sy_ref, ahi_ref, alo_ref = refs[:4]
    refs = refs[4:]
    if not first:
        exr_ref, exl_ref, dr_ref, dl_ref, top_ref, bottom_ref = refs[:6]
        refs = refs[6:]
    rows = CHUNK
    height = 16
    sx = sx_ref[...]
    sy = sy_ref[...]
    ahi = ahi_ref[...]
    alo = alo_ref[...]
    slabs = [sp_ref[pl.ds(y, rows, stride=height), :] for y in range(height)]
    tend = raw_slabs(slabs, sx, sy, ahi, alo)
    if first:
        ex_ref, ey_ref = refs
        ex_ref[...] = pack_edges(tend)
        ey_ref[0] = tend[0]
        ey_ref[1] = tend[height - 1]
        return
    exr = unpack_edges(exr_ref[...])
    exl = unpack_edges(exl_ref[...])
    dr = unpack_edges(dr_ref[...])
    dl = unpack_edges(dl_ref[...])
    tx = [stiff_x(t, exr, exl, y) for y, t in enumerate(tend)]
    down = stiff_x(top_ref[...], dr, dl, 0)
    up = stiff_x(bottom_ref[...], dr, dl, height - 1)
    ext = [up] + tx + [down]
    new = []
    for y in range(height):
        cur = ext[y + 1]
        if y % NP == NP - 1:
            op = 0.5 * (cur + ext[y + 2])
        elif y % NP == 0:
            op = 0.5 * (ext[y] + cur)
        else:
            op = cur
        inner = slabs[y] + op
        if combo[0] is None:
            val = inner
        else:
            v0 = v0_ref[pl.ds(y, rows, stride=height), :]
            if combo[0] == "third":
                val = v0 / 3.0 + 2.0 / 3.0 * inner
            else:
                val = combo[0] * v0 + combo[1] * inner
        new.append(val)
    out_ref = refs[0]
    for y in range(height):
        out_ref[pl.ds(y, rows, stride=height), :] = new[y]
    if edges:
        ex_ref, ey_ref = refs[1:3]
        tend = raw_slabs(new, sx, sy, ahi, alo)
        ex_ref[...] = pack_edges(tend)
        ey_ref[0] = tend[0]
        ey_ref[1] = tend[height - 1]


def run_section(field_rows, v0, sx, sy, ahi, alo, halos, *, first, combo, edges):
    total, width = field_rows.shape
    feats = sx.shape[0]
    steps = feats // CHUNK
    big = pl.BlockSpec((CHUNK * 16, width), lambda i: (i, 0))
    small = pl.BlockSpec((CHUNK, width), lambda i: (i, 0))
    const = pl.BlockSpec((width, width), lambda i: (0, 0))
    edge = pl.BlockSpec((FOLD, width), lambda i: (i, 0))
    rowsb = pl.BlockSpec((2, CHUNK, width), lambda i: (0, i, 0))
    args, specs = [], []
    if combo is not None and combo[0] is not None:
        args.append(v0)
        specs.append(big)
    args += [field_rows, sx, sy, ahi, alo]
    specs += [big, small, small, const, const]
    if not first:
        exr, exl, partner = halos
        blocks = field_rows.shape[0] // (CHUNK * 16)
        args += [exr, exl, partner, partner, partner, partner]
        specs += [
            edge,
            edge,
            pl.BlockSpec((FOLD, width), lambda i: (4 * blocks + i, 0)),
            pl.BlockSpec((FOLD, width), lambda i: (5 * blocks + i, 0)),
            pl.BlockSpec((CHUNK, width), lambda i: (i, 0)),
            pl.BlockSpec((CHUNK, width), lambda i: (blocks + i, 0)),
        ]
    out_shape, out_specs = [], []
    ex_shape = jax.ShapeDtypeStruct((feats // 2, width), jnp.float32)
    ey_shape = jax.ShapeDtypeStruct((2, feats, width), jnp.float32)
    if first:
        out_shape = [ex_shape, ey_shape]
        out_specs = [edge, rowsb]
    else:
        out_shape = [jax.ShapeDtypeStruct((total, width), jnp.float32)]
        out_specs = [big]
        if edges:
            out_shape += [ex_shape, ey_shape]
            out_specs += [edge, rowsb]
    kernel = functools.partial(section_kernel, first=first, combo=combo, edges=edges)
    return pl.pallas_call(
        kernel,
        grid=(steps,),
        in_specs=specs,
        out_specs=out_specs,
        out_shape=out_shape,
        compiler_params=pltpu.CompilerParams(vmem_limit_bytes=8 * 1024 * 1024),
    )(*args)


def exchange(ex, ey):
    n_face = lax.axis_size("face")
    n_elem = lax.axis_size("elem")
    assert n_face == 2
    from_right = [(j, (j - 1) % n_elem) for j in range(n_elem)]
    from_left = [(j, (j + 1) % n_elem) for j in range(n_elem)]
    exr = lax.ppermute(ex, "elem", from_right)
    exl = lax.ppermute(ex, "elem", from_left)
    feats = ey.shape[1]
    bundle = jnp.concatenate([ey.reshape(2 * feats, ey.shape[2]), exr, exl], axis=0)
    partner = lax.ppermute(bundle, "face", [(0, 1), (1, 0)])
    return (exr, exl, partner)


def column_model(inputs, w_in, b_in, w_mid, b_mid, w_top, b_top, w_out, b_out):
    hidden = jax.nn.silu(
        jnp.dot(w_in, inputs, preferred_element_type=jnp.float32) + b_in[:, None]
    ).astype(jnp.bfloat16)
    hidden = jax.nn.silu(
        jnp.dot(w_mid, hidden, preferred_element_type=jnp.float32) + b_mid[:, None]
    ).astype(jnp.bfloat16)
    hidden = jax.nn.silu(
        jnp.dot(w_top, hidden, preferred_element_type=jnp.float32) + b_top[:, None]
    ).astype(jnp.bfloat16)
    outputs = jnp.dot(w_out, hidden, preferred_element_type=jnp.float32) + b_out[:, None]
    heating = jnp.sum(outputs[:LEV], axis=0)
    return (outputs.astype(jnp.bfloat16), heating)


def mlp_kernel(fin_ref, w_in_ref, w_mid_ref, w_top_ref, w_out_ref, b_ref, tend_ref, heat_ref, scratch):
    feats = w_in_ref.shape[0]
    outs = w_out_ref.shape[0]
    height = heat_ref.shape[0]
    width = heat_ref.shape[1]

    def act(a):
        return (a * (0.5 + 0.5 * jnp.tanh(0.5 * a))).astype(jnp.bfloat16)

    hid = w_mid_ref.shape[0]
    b_in = b_ref[0:hid]
    b_mid = b_ref[hid : 2 * hid]
    b_top = b_ref[2 * hid : 3 * hid]
    b_out = b_ref[3 * hid : 3 * hid + outs]

    for pair in range(height // 2):
        y = 2 * pair
        x = jnp.concatenate(
            [fin_ref[pl.ds(y, feats, stride=height), :], fin_ref[pl.ds(y + 1, feats, stride=height), :]],
            axis=1,
        ).astype(jnp.bfloat16)
        h = act(
            lax.dot_general(
                w_in_ref[...], x, (((0,), (0,)), ((), ())), preferred_element_type=jnp.float32
            )
            + b_in
        )
        h = act(jnp.dot(w_mid_ref[...], h, preferred_element_type=jnp.float32) + b_mid)
        h = act(jnp.dot(w_top_ref[...], h, preferred_element_type=jnp.float32) + b_top)
        out = jnp.dot(w_out_ref[...], h, preferred_element_type=jnp.float32) + b_out
        heat = jnp.sum(out[:LEV], axis=0, keepdims=True)
        heat_ref[y : y + 1, :] = heat[:, :width]
        heat_ref[y + 1 : y + 2, :] = heat[:, width:]
        scratch[pl.ds(y, outs, stride=height), :] = out[:, :width]
        scratch[pl.ds(y + 1, outs, stride=height), :] = out[:, width:]
    tend_ref[...] = scratch[...].astype(jnp.bfloat16)


def run_mlp(fin, height, w_in, b_in, w_mid, b_mid, w_top, b_top, w_out, b_out):
    width = fin.shape[1]
    outs = w_out.shape[0]
    biases = jnp.concatenate([b_in, b_mid, b_top, b_out]).reshape(-1, 1)
    return pl.pallas_call(
        mlp_kernel,
        out_shape=[
            jax.ShapeDtypeStruct((outs * height, width), jnp.bfloat16),
            jax.ShapeDtypeStruct((height, width), jnp.float32),
        ],
        scratch_shapes=[pltpu.VMEM((outs * height, width), jnp.float32)],
        compiler_params=pltpu.CompilerParams(vmem_limit_bytes=12 * 1024 * 1024),
    )(fin, w_in.T, w_mid, w_top, w_out, biases)


def local(state, speed_x, speed_y, w_in, b_in, w_mid, b_mid, w_top, b_top, w_out, b_out, span_of):
    feats, height, breadth = state.shape
    across = np.kron(np.eye(breadth // NP, dtype=np.float32), TABLE.T)
    ahi_np = across.astype(jnp.bfloat16)
    alo_np = (across - ahi_np.astype(np.float32)).astype(jnp.bfloat16)
    ahi = jnp.asarray(ahi_np)
    alo = jnp.asarray(alo_np)
    sx = jnp.broadcast_to(speed_x[:, None], (feats, breadth))
    sy = jnp.broadcast_to(speed_y[:, None], (feats, breadth))
    v0 = state.reshape(feats * height, breadth)
    ex, ey = run_section(v0, None, sx, sy, ahi, alo, None, first=True, combo=None, edges=True)
    field = v0
    combos = [(None, None), (0.75, 0.25), ("third", None)]
    for k, combo in enumerate(combos):
        halos = exchange(ex, ey)
        outs = run_section(
            field, v0, sx, sy, ahi, alo, halos, first=False, combo=combo, edges=k < 2
        )
        if k < 2:
            field, ex, ey = outs
        else:
            (field,) = outs
    final_state = field.reshape(feats, height, breadth)
    column_count = height * breadth
    target = span_of.reshape(column_count)
    devices = lax.axis_size("face") * lax.axis_size("elem")
    span_ids = jnp.arange(devices, dtype=jnp.int32)
    tend_rows, heat_rows = run_mlp(field, height, w_in, b_in, w_mid, b_mid, w_top, b_top, w_out, b_out)
    heating = heat_rows.reshape(column_count)
    member = (target[:, None] == span_ids[None, :]).astype(jnp.float32)
    partial_sums = jnp.sum(member * heating[:, None], axis=0)
    received = lax.all_to_all(
        partial_sums.reshape(devices, 1), ("face", "elem"), 0, 1, tiled=True
    )
    span_heating = jnp.sum(received, axis=1) / column_count
    tendencies = tend_rows.reshape(-1, height, breadth)
    return (final_state, tendencies, span_heating)


def solution(mesh):
    return jax.shard_map(
        local,
        mesh=mesh,
        in_specs=(
            P(None, "face", "elem"),
            P(),
            P(),
            P(),
            P(),
            P(),
            P(),
            P(),
            P(),
            P(),
            P(),
            P("face", "elem", None, None),
        ),
        out_specs=(P(None, "face", "elem"), P(None, "face", "elem"), P(("face", "elem"))),
        check_vma=False,
    )
```

```python
import functools
import math

import jax
import jax.numpy as jnp
import numpy as np
from jax import lax
from jax.experimental import pallas as pl
from jax.experimental.pallas import tpu as pltpu
from jax.sharding import PartitionSpec as P

NP = 4
LEV = 72
CHUNK = 48
FOLD = CHUNK // 2


def gll_matrix():
    inner_node = 1.0 / math.sqrt(5.0)
    gll_nodes = np.array([-1.0, -inner_node, inner_node, 1.0])
    weights = np.array(
        [
            1.0
            / np.prod([gll_nodes[outer] - gll_nodes[other] for other in range(4) if other != outer])
            for outer in range(4)
        ]
    )
    matrix = np.zeros((4, 4))
    for outer in range(4):
        for inner in range(4):
            if inner != outer:
                matrix[outer, inner] = (
                    weights[inner] / weights[outer] / (gll_nodes[outer] - gll_nodes[inner])
                )
    for outer in range(4):
        matrix[outer, outer] = -np.sum(matrix[outer])
    return matrix.astype(np.float32)


TABLE = gll_matrix()


def lanes(shape):
    return lax.broadcasted_iota(jnp.int32, shape, len(shape) - 1)


def roll(x, shift):
    shift = shift % x.shape[-1]
    return x if shift == 0 else pltpu.roll(x, shift, x.ndim - 1)


def raw_slabs(slabs, sx, sy, ahi, alo):
    rows = slabs[0].shape[0]
    stacked = jnp.concatenate(slabs, axis=0)
    hi = stacked.astype(jnp.bfloat16)
    lo = (stacked - hi.astype(jnp.float32)).astype(jnp.bfloat16)
    along_x = (
        jnp.dot(hi, ahi, preferred_element_type=jnp.float32)
        + jnp.dot(hi, alo, preferred_element_type=jnp.float32)
        + jnp.dot(lo, ahi, preferred_element_type=jnp.float32)
    )
    out = []
    for y, _ in enumerate(slabs):
        base = (y // NP) * NP
        j = y % NP
        along_y = float(TABLE[j, 0]) * slabs[base]
        for i in range(1, NP):
            along_y = along_y + float(TABLE[j, i]) * slabs[base + i]
        dx = along_x[y * rows : (y + 1) * rows]
        out.append(-(sx * dx + sy * along_y))
    return out


def pack_edges(tend):
    rows, width = tend[0].shape
    lane = lanes((rows, width))
    acc = jnp.zeros((rows, width), jnp.float32)
    for y, t in enumerate(tend):
        acc = jnp.where(lane == 2 * y, roll(t, 2 * y), acc)
        acc = jnp.where(lane == 2 * y + 1, roll(t, 2 * y + 2), acc)
    half = rows // 2
    lane_h = lanes((half, width))
    return jnp.where(lane_h < 32, acc[:half], roll(acc[half:], 32))


def unpack_edges(block):
    return jnp.concatenate([block, roll(block, 96)], axis=0)


def stiff_x(t, right_edges, left_edges, y):
    rows, width = t.shape
    lane = lanes((rows, width))
    right = jnp.where(lane == width - 1, roll(right_edges, width - 1 - 2 * y), roll(t, width - 1))
    left = jnp.where(lane == 0, roll(left_edges, width - 1 - 2 * y), roll(t, 1))
    place = lane % NP
    return jnp.where(
        place == NP - 1, 0.5 * (t + right), jnp.where(place == 0, 0.5 * (left + t), t)
    )


def section_kernel(*refs, first, combo, edges):
    refs = list(refs)
    v0_ref = None if combo is None or combo[0] is None else refs.pop(0)
    sp_ref = refs.pop(0)
    sx_ref, sy_ref, ahi_ref, alo_ref = refs[:4]
    refs = refs[4:]
    if not first:
        exr_ref, exl_ref, dr_ref, dl_ref, top_ref, bottom_ref = refs[:6]
        refs = refs[6:]
    rows = CHUNK
    height = 16
    sx = sx_ref[...]
    sy = sy_ref[...]
    ahi = ahi_ref[...]
    alo = alo_ref[...]
    slabs = [sp_ref[pl.ds(y, rows, stride=height), :] for y in range(height)]
    tend = raw_slabs(slabs, sx, sy, ahi, alo)
    if first:
        ex_ref, ey_ref = refs
        ex_ref[...] = pack_edges(tend)
        ey_ref[0] = tend[0]
        ey_ref[1] = tend[height - 1]
        return
    exr = unpack_edges(exr_ref[...])
    exl = unpack_edges(exl_ref[...])
    dr = unpack_edges(dr_ref[...])
    dl = unpack_edges(dl_ref[...])
    tx = [stiff_x(t, exr, exl, y) for y, t in enumerate(tend)]
    down = stiff_x(top_ref[...], dr, dl, 0)
    up = stiff_x(bottom_ref[...], dr, dl, height - 1)
    ext = [up] + tx + [down]
    new = []
    for y in range(height):
        cur = ext[y + 1]
        if y % NP == NP - 1:
            op = 0.5 * (cur + ext[y + 2])
        elif y % NP == 0:
            op = 0.5 * (ext[y] + cur)
        else:
            op = cur
        inner = slabs[y] + op
        if combo[0] is None:
            val = inner
        else:
            v0 = v0_ref[pl.ds(y, rows, stride=height), :]
            if combo[0] == "third":
                val = v0 / 3.0 + 2.0 / 3.0 * inner
            else:
                val = combo[0] * v0 + combo[1] * inner
        new.append(val)
    out_ref = refs[0]
    for y in range(height):
        out_ref[pl.ds(y, rows, stride=height), :] = new[y]
    if edges:
        ex_ref, ey_ref = refs[1:3]
        tend = raw_slabs(new, sx, sy, ahi, alo)
        ex_ref[...] = pack_edges(tend)
        ey_ref[0] = tend[0]
        ey_ref[1] = tend[height - 1]


def run_section(field_rows, v0, speeds, mats, halos, *, first, combo, edges):
    total, width = field_rows.shape
    feats = speeds.shape[0] // 2
    steps = feats // CHUNK
    big = pl.BlockSpec((CHUNK * 16, width), lambda i: (i, 0))
    small = pl.BlockSpec((CHUNK, width), lambda i: (i, 0))
    small_y = pl.BlockSpec((CHUNK, width), lambda i: (i + steps, 0))
    const = pl.BlockSpec((width, width), lambda i: (0, 0))
    const_lo = pl.BlockSpec((width, width), lambda i: (1, 0))
    edge = pl.BlockSpec((FOLD, width), lambda i: (i, 0))
    rowsb = pl.BlockSpec((2, CHUNK, width), lambda i: (0, i, 0))
    args, specs = [], []
    if combo is not None and combo[0] is not None:
        args.append(v0)
        specs.append(big)
    args += [field_rows, speeds, speeds, mats, mats]
    specs += [big, small, small_y, const, const_lo]
    if not first:
        exr, exl, partner = halos
        blocks = field_rows.shape[0] // (CHUNK * 16)
        args += [exr, exl, partner, partner, partner, partner]
        specs += [
            edge,
            edge,
            pl.BlockSpec((FOLD, width), lambda i: (4 * blocks + i, 0)),
            pl.BlockSpec((FOLD, width), lambda i: (5 * blocks + i, 0)),
            pl.BlockSpec((CHUNK, width), lambda i: (i, 0)),
            pl.BlockSpec((CHUNK, width), lambda i: (blocks + i, 0)),
        ]
    out_shape, out_specs = [], []
    ex_shape = jax.ShapeDtypeStruct((feats // 2, width), jnp.float32)
    ey_shape = jax.ShapeDtypeStruct((2, feats, width), jnp.float32)
    if first:
        out_shape = [ex_shape, ey_shape]
        out_specs = [edge, rowsb]
    else:
        out_shape = [jax.ShapeDtypeStruct((total, width), jnp.float32)]
        out_specs = [big]
        if edges:
            out_shape += [ex_shape, ey_shape]
            out_specs += [edge, rowsb]
    kernel = functools.partial(section_kernel, first=first, combo=combo, edges=edges)
    return pl.pallas_call(
        kernel,
        grid=(steps,),
        in_specs=specs,
        out_specs=out_specs,
        out_shape=out_shape,
        compiler_params=pltpu.CompilerParams(vmem_limit_bytes=16 * 1024 * 1024),
    )(*args)


def exchange(ex, ey):
    n_face = lax.axis_size("face")
    n_elem = lax.axis_size("elem")
    assert n_face == 2
    from_right = [(j, (j - 1) % n_elem) for j in range(n_elem)]
    from_left = [(j, (j + 1) % n_elem) for j in range(n_elem)]
    exr = lax.ppermute(ex, "elem", from_right)
    exl = lax.ppermute(ex, "elem", from_left)
    feats = ey.shape[1]
    bundle = jnp.concatenate([ey.reshape(2 * feats, ey.shape[2]), exr, exl], axis=0)
    partner = lax.ppermute(bundle, "face", [(0, 1), (1, 0)])
    return (exr, exl, partner)


def column_model(inputs, w_in, b_in, w_mid, b_mid, w_top, b_top, w_out, b_out):
    hidden = jax.nn.silu(
        jnp.dot(w_in, inputs, preferred_element_type=jnp.float32) + b_in[:, None]
    ).astype(jnp.bfloat16)
    hidden = jax.nn.silu(
        jnp.dot(w_mid, hidden, preferred_element_type=jnp.float32) + b_mid[:, None]
    ).astype(jnp.bfloat16)
    hidden = jax.nn.silu(
        jnp.dot(w_top, hidden, preferred_element_type=jnp.float32) + b_top[:, None]
    ).astype(jnp.bfloat16)
    outputs = jnp.dot(w_out, hidden, preferred_element_type=jnp.float32) + b_out[:, None]
    heating = jnp.sum(outputs[:LEV], axis=0)
    return (outputs.astype(jnp.bfloat16), heating)


def mlp_kernel(fin_ref, w_in_ref, w_mid_ref, w_top_ref, w_out_ref, b_ref, tend_ref, heat_ref, scratch):
    feats = w_in_ref.shape[0]
    outs = w_out_ref.shape[0]
    height = heat_ref.shape[0]
    width = heat_ref.shape[1]

    def act(a):
        return (a * (0.5 + 0.5 * jnp.tanh(0.5 * a))).astype(jnp.bfloat16)

    hid = w_mid_ref.shape[0]
    b_in = b_ref[0:hid]
    b_mid = b_ref[hid : 2 * hid]
    b_top = b_ref[2 * hid : 3 * hid]
    b_out = b_ref[3 * hid : 3 * hid + outs]

    for pair in range(height // 2):
        y = 2 * pair
        x = jnp.concatenate(
            [fin_ref[pl.ds(y, feats, stride=height), :], fin_ref[pl.ds(y + 1, feats, stride=height), :]],
            axis=1,
        ).astype(jnp.bfloat16)
        h = act(
            lax.dot_general(
                w_in_ref[...], x, (((0,), (0,)), ((), ())), preferred_element_type=jnp.float32
            )
            + b_in
        )
        h = act(jnp.dot(w_mid_ref[...], h, preferred_element_type=jnp.float32) + b_mid)
        h = act(jnp.dot(w_top_ref[...], h, preferred_element_type=jnp.float32) + b_top)
        out = jnp.dot(w_out_ref[...], h, preferred_element_type=jnp.float32) + b_out
        heat = jnp.sum(out[:LEV], axis=0, keepdims=True)
        heat_ref[y : y + 1, :] = heat[:, :width]
        heat_ref[y + 1 : y + 2, :] = heat[:, width:]
        scratch[pl.ds(y, outs, stride=height), :] = out[:, :width]
        scratch[pl.ds(y + 1, outs, stride=height), :] = out[:, width:]
    tend_ref[...] = scratch[...].astype(jnp.bfloat16)


def run_mlp(fin, height, w_in, b_in, w_mid, b_mid, w_top, b_top, w_out, b_out):
    width = fin.shape[1]
    outs = w_out.shape[0]
    biases = jnp.concatenate([b_in, b_mid, b_top, b_out]).reshape(-1, 1)
    return pl.pallas_call(
        mlp_kernel,
        out_shape=[
            jax.ShapeDtypeStruct((outs * height, width), jnp.bfloat16),
            jax.ShapeDtypeStruct((height, width), jnp.float32),
        ],
        scratch_shapes=[pltpu.VMEM((outs * height, width), jnp.float32)],
        compiler_params=pltpu.CompilerParams(vmem_limit_bytes=16 * 1024 * 1024),
    )(fin, w_in.T, w_mid, w_top, w_out, biases)


def local(state, speed_x, speed_y, w_in, b_in, w_mid, b_mid, w_top, b_top, w_out, b_out, span_of):
    feats, height, breadth = state.shape
    across = np.kron(np.eye(breadth // NP, dtype=np.float32), TABLE.T)
    ahi_np = across.astype(jnp.bfloat16)
    alo_np = (across - ahi_np.astype(np.float32)).astype(jnp.bfloat16)
    mats = jnp.asarray(np.concatenate([ahi_np, alo_np], axis=0))
    speeds = jnp.broadcast_to(jnp.concatenate([speed_x, speed_y])[:, None], (2 * feats, breadth))
    v0 = state.reshape(feats * height, breadth)
    ex, ey = run_section(v0, None, speeds, mats, None, first=True, combo=None, edges=True)
    field = v0
    combos = [(None, None), (0.75, 0.25), ("third", None)]
    for k, combo in enumerate(combos):
        halos = exchange(ex, ey)
        outs = run_section(
            field, v0, speeds, mats, halos, first=False, combo=combo, edges=k < 2
        )
        if k < 2:
            field, ex, ey = outs
        else:
            (field,) = outs
    final_state = field.reshape(feats, height, breadth)
    column_count = height * breadth
    target = span_of.reshape(column_count)
    devices = lax.axis_size("face") * lax.axis_size("elem")
    span_ids = jnp.arange(devices, dtype=jnp.int32)
    tend_rows, heat_rows = run_mlp(field, height, w_in, b_in, w_mid, b_mid, w_top, b_top, w_out, b_out)
    heating = heat_rows.reshape(column_count)
    member = (target[:, None] == span_ids[None, :]).astype(jnp.float32)
    partial_sums = jnp.sum(member * heating[:, None], axis=0)
    received = lax.all_to_all(
        partial_sums.reshape(devices, 1), ("face", "elem"), 0, 1, tiled=True
    )
    span_heating = jnp.sum(received, axis=1) / column_count
    tendencies = tend_rows.reshape(-1, height, breadth)
    return (final_state, tendencies, span_heating)


def solution(mesh):
    return jax.shard_map(
        local,
        mesh=mesh,
        in_specs=(
            P(None, "face", "elem"),
            P(),
            P(),
            P(),
            P(),
            P(),
            P(),
            P(),
            P(),
            P(),
            P(),
            P("face", "elem", None, None),
        ),
        out_specs=(P(None, "face", "elem"), P(None, "face", "elem"), P(("face", "elem"))),
        check_vma=False,
    )
```

```python
import functools
import math

import jax
import jax.numpy as jnp
import numpy as np
from jax import lax
from jax.experimental import pallas as pl
from jax.experimental.pallas import tpu as pltpu
from jax.sharding import PartitionSpec as P

NP = 4
LEV = 72
CHUNK = 48
FOLD = CHUNK // 2


def gll_matrix():
    inner_node = 1.0 / math.sqrt(5.0)
    gll_nodes = np.array([-1.0, -inner_node, inner_node, 1.0])
    weights = np.array(
        [
            1.0
            / np.prod([gll_nodes[outer] - gll_nodes[other] for other in range(4) if other != outer])
            for outer in range(4)
        ]
    )
    matrix = np.zeros((4, 4))
    for outer in range(4):
        for inner in range(4):
            if inner != outer:
                matrix[outer, inner] = (
                    weights[inner] / weights[outer] / (gll_nodes[outer] - gll_nodes[inner])
                )
    for outer in range(4):
        matrix[outer, outer] = -np.sum(matrix[outer])
    return matrix.astype(np.float32)


TABLE = gll_matrix()


def lanes(shape):
    return lax.broadcasted_iota(jnp.int32, shape, len(shape) - 1)


def roll(x, shift):
    shift = shift % x.shape[-1]
    return x if shift == 0 else pltpu.roll(x, shift, x.ndim - 1)


def raw_slabs(slabs, sx, sy, ahi, alo):
    rows = slabs[0].shape[0]
    stacked = jnp.concatenate(slabs, axis=0)
    hi = stacked.astype(jnp.bfloat16)
    lo = (stacked - hi.astype(jnp.float32)).astype(jnp.bfloat16)
    along_x = (
        jnp.dot(hi, ahi, preferred_element_type=jnp.float32)
        + jnp.dot(hi, alo, preferred_element_type=jnp.float32)
        + jnp.dot(lo, ahi, preferred_element_type=jnp.float32)
    )
    out = []
    for y, _ in enumerate(slabs):
        base = (y // NP) * NP
        j = y % NP
        along_y = float(TABLE[j, 0]) * slabs[base]
        for i in range(1, NP):
            along_y = along_y + float(TABLE[j, i]) * slabs[base + i]
        dx = along_x[y * rows : (y + 1) * rows]
        out.append(-(sx * dx + sy * along_y))
    return out


def raw_stiff_x(slabs, sx, sy, fhi, flo, smat, right_edges, left_edges):
    rows, width = slabs[0].shape
    stacked = jnp.concatenate(slabs, axis=0)
    hi = stacked.astype(jnp.bfloat16)
    lo = (stacked - hi.astype(jnp.float32)).astype(jnp.bfloat16)
    along_x = (
        jnp.dot(hi, fhi, preferred_element_type=jnp.float32)
        + jnp.dot(hi, flo, preferred_element_type=jnp.float32)
        + jnp.dot(lo, fhi, preferred_element_type=jnp.float32)
    )
    averaged = jnp.dot(hi, smat, preferred_element_type=jnp.float32) + jnp.dot(
        lo, smat, preferred_element_type=jnp.float32
    )
    lane = lanes((rows, width))
    out = []
    for y in range(len(slabs)):
        base = (y // NP) * NP
        j = y % NP
        part = lambda k: averaged[k * rows : (k + 1) * rows]
        along_y = float(TABLE[j, 0]) * part(base)
        for i in range(1, NP):
            along_y = along_y + float(TABLE[j, i]) * part(base + i)
        dx = along_x[y * rows : (y + 1) * rows]
        halo = jnp.where(
            lane == width - 1,
            roll(right_edges, width - 1 - 2 * y),
            jnp.where(lane == 0, roll(left_edges, width - 1 - 2 * y), 0.0),
        )
        out.append(-(sx * dx + sy * along_y) + 0.5 * halo)
    return out


def pack_edges(tend):
    rows, width = tend[0].shape
    lane = lanes((rows, width))
    acc = jnp.zeros((rows, width), jnp.float32)
    for y, t in enumerate(tend):
        acc = jnp.where(lane == 2 * y, roll(t, 2 * y), acc)
        acc = jnp.where(lane == 2 * y + 1, roll(t, 2 * y + 2), acc)
    half = rows // 2
    lane_h = lanes((half, width))
    return jnp.where(lane_h < 32, acc[:half], roll(acc[half:], 32))


def unpack_edges(block):
    return jnp.concatenate([block, roll(block, 96)], axis=0)


def stiff_x(t, right_edges, left_edges, y):
    rows, width = t.shape
    lane = lanes((rows, width))
    right = jnp.where(lane == width - 1, roll(right_edges, width - 1 - 2 * y), roll(t, width - 1))
    left = jnp.where(lane == 0, roll(left_edges, width - 1 - 2 * y), roll(t, 1))
    place = lane % NP
    return jnp.where(
        place == NP - 1, 0.5 * (t + right), jnp.where(place == 0, 0.5 * (left + t), t)
    )


def section_kernel(*refs, first, combo, edges):
    refs = list(refs)
    v0_ref = None if combo is None or combo[0] is None else refs.pop(0)
    sp_ref = refs.pop(0)
    sx_ref, sy_ref, ahi_ref, alo_ref = refs[:4]
    refs = refs[4:]
    if not first:
        fhi_ref, flo_ref, smat_ref = refs[:3]
        exr_ref, exl_ref, dr_ref, dl_ref, top_ref, bottom_ref = refs[3:9]
        refs = refs[9:]
    rows = CHUNK
    height = 16
    sx = sx_ref[...]
    sy = sy_ref[...]
    ahi = ahi_ref[...]
    alo = alo_ref[...]
    slabs = [sp_ref[pl.ds(y, rows, stride=height), :] for y in range(height)]
    if first:
        tend = raw_slabs(slabs, sx, sy, ahi, alo)
        ex_ref, ey_ref = refs
        ex_ref[...] = pack_edges(tend)
        ey_ref[0] = tend[0]
        ey_ref[1] = tend[height - 1]
        return
    exr = unpack_edges(exr_ref[...])
    exl = unpack_edges(exl_ref[...])
    dr = unpack_edges(dr_ref[...])
    dl = unpack_edges(dl_ref[...])
    tx = raw_stiff_x(slabs, sx, sy, fhi_ref[...], flo_ref[...], smat_ref[...], exr, exl)
    down = stiff_x(top_ref[...], dr, dl, 0)
    up = stiff_x(bottom_ref[...], dr, dl, height - 1)
    ext = [up] + tx + [down]
    new = []
    for y in range(height):
        cur = ext[y + 1]
        if y % NP == NP - 1:
            op = 0.5 * (cur + ext[y + 2])
        elif y % NP == 0:
            op = 0.5 * (ext[y] + cur)
        else:
            op = cur
        inner = slabs[y] + op
        if combo[0] is None:
            val = inner
        else:
            v0 = v0_ref[pl.ds(y, rows, stride=height), :]
            if combo[0] == "third":
                val = v0 / 3.0 + 2.0 / 3.0 * inner
            else:
                val = combo[0] * v0 + combo[1] * inner
        new.append(val)
    out_ref = refs[0]
    for y in range(height):
        out_ref[pl.ds(y, rows, stride=height), :] = new[y]
    if edges:
        ex_ref, ey_ref = refs[1:3]
        tend = raw_slabs(new, sx, sy, ahi, alo)
        ex_ref[...] = pack_edges(tend)
        ey_ref[0] = tend[0]
        ey_ref[1] = tend[height - 1]


def run_section(field_rows, v0, speeds, mats, halos, *, first, combo, edges):
    total, width = field_rows.shape
    feats = speeds.shape[0] // 2
    steps = feats // CHUNK
    big = pl.BlockSpec((CHUNK * 16, width), lambda i: (i, 0))
    small = pl.BlockSpec((CHUNK, width), lambda i: (i, 0))
    small_y = pl.BlockSpec((CHUNK, width), lambda i: (i + steps, 0))
    const = pl.BlockSpec((width, width), lambda i: (0, 0))
    const_lo = pl.BlockSpec((width, width), lambda i: (1, 0))
    const_fhi = pl.BlockSpec((width, width), lambda i: (2, 0))
    const_flo = pl.BlockSpec((width, width), lambda i: (3, 0))
    const_s = pl.BlockSpec((width, width), lambda i: (4, 0))
    edge = pl.BlockSpec((FOLD, width), lambda i: (i, 0))
    rowsb = pl.BlockSpec((2, CHUNK, width), lambda i: (0, i, 0))
    args, specs = [], []
    if combo is not None and combo[0] is not None:
        args.append(v0)
        specs.append(big)
    args += [field_rows, speeds, speeds, mats, mats]
    specs += [big, small, small_y, const, const_lo]
    if not first:
        args += [mats, mats, mats]
        specs += [const_fhi, const_flo, const_s]
    if not first:
        exr, exl, partner = halos
        blocks = field_rows.shape[0] // (CHUNK * 16)
        args += [exr, exl, partner, partner, partner, partner]
        specs += [
            edge,
            edge,
            pl.BlockSpec((FOLD, width), lambda i: (4 * blocks + i, 0)),
            pl.BlockSpec((FOLD, width), lambda i: (5 * blocks + i, 0)),
            pl.BlockSpec((CHUNK, width), lambda i: (i, 0)),
            pl.BlockSpec((CHUNK, width), lambda i: (blocks + i, 0)),
        ]
    out_shape, out_specs = [], []
    ex_shape = jax.ShapeDtypeStruct((feats // 2, width), jnp.float32)
    ey_shape = jax.ShapeDtypeStruct((2, feats, width), jnp.float32)
    if first:
        out_shape = [ex_shape, ey_shape]
        out_specs = [edge, rowsb]
    else:
        out_shape = [jax.ShapeDtypeStruct((total, width), jnp.float32)]
        out_specs = [big]
        if edges:
            out_shape += [ex_shape, ey_shape]
            out_specs += [edge, rowsb]
    kernel = functools.partial(section_kernel, first=first, combo=combo, edges=edges)
    return pl.pallas_call(
        kernel,
        grid=(steps,),
        in_specs=specs,
        out_specs=out_specs,
        out_shape=out_shape,
        compiler_params=pltpu.CompilerParams(vmem_limit_bytes=16 * 1024 * 1024),
    )(*args)


def exchange(ex, ey):
    n_face = lax.axis_size("face")
    n_elem = lax.axis_size("elem")
    assert n_face == 2
    from_right = [(j, (j - 1) % n_elem) for j in range(n_elem)]
    from_left = [(j, (j + 1) % n_elem) for j in range(n_elem)]
    exr = lax.ppermute(ex, "elem", from_right)
    exl = lax.ppermute(ex, "elem", from_left)
    feats = ey.shape[1]
    bundle = jnp.concatenate([ey.reshape(2 * feats, ey.shape[2]), exr, exl], axis=0)
    partner = lax.ppermute(bundle, "face", [(0, 1), (1, 0)])
    return (exr, exl, partner)


def column_model(inputs, w_in, b_in, w_mid, b_mid, w_top, b_top, w_out, b_out):
    hidden = jax.nn.silu(
        jnp.dot(w_in, inputs, preferred_element_type=jnp.float32) + b_in[:, None]
    ).astype(jnp.bfloat16)
    hidden = jax.nn.silu(
        jnp.dot(w_mid, hidden, preferred_element_type=jnp.float32) + b_mid[:, None]
    ).astype(jnp.bfloat16)
    hidden = jax.nn.silu(
        jnp.dot(w_top, hidden, preferred_element_type=jnp.float32) + b_top[:, None]
    ).astype(jnp.bfloat16)
    outputs = jnp.dot(w_out, hidden, preferred_element_type=jnp.float32) + b_out[:, None]
    heating = jnp.sum(outputs[:LEV], axis=0)
    return (outputs.astype(jnp.bfloat16), heating)


def mlp_kernel(fin_ref, w_in_ref, w_mid_ref, w_top_ref, w_out_ref, b_ref, tend_ref, heat_ref, scratch):
    feats = w_in_ref.shape[0]
    outs = w_out_ref.shape[0]
    height = heat_ref.shape[0]
    width = heat_ref.shape[1]

    def act(a):
        return (a * (0.5 + 0.5 * jnp.tanh(0.5 * a))).astype(jnp.bfloat16)

    hid = w_mid_ref.shape[0]
    b_in = b_ref[0:hid]
    b_mid = b_ref[hid : 2 * hid]
    b_top = b_ref[2 * hid : 3 * hid]
    b_out = b_ref[3 * hid : 3 * hid + outs]

    for pair in range(height // 2):
        y = 2 * pair
        x = jnp.concatenate(
            [fin_ref[pl.ds(y, feats, stride=height), :], fin_ref[pl.ds(y + 1, feats, stride=height), :]],
            axis=1,
        ).astype(jnp.bfloat16)
        h = act(
            lax.dot_general(
                w_in_ref[...], x, (((0,), (0,)), ((), ())), preferred_element_type=jnp.float32
            )
            + b_in
        )
        h = act(jnp.dot(w_mid_ref[...], h, preferred_element_type=jnp.float32) + b_mid)
        h = act(jnp.dot(w_top_ref[...], h, preferred_element_type=jnp.float32) + b_top)
        out = jnp.dot(w_out_ref[...], h, preferred_element_type=jnp.float32) + b_out
        heat = jnp.sum(out[:LEV], axis=0, keepdims=True)
        heat_ref[y : y + 1, :] = heat[:, :width]
        heat_ref[y + 1 : y + 2, :] = heat[:, width:]
        scratch[pl.ds(y, outs, stride=height), :] = out[:, :width]
        scratch[pl.ds(y + 1, outs, stride=height), :] = out[:, width:]
    tend_ref[...] = scratch[...].astype(jnp.bfloat16)


def run_mlp(fin, height, w_in, b_in, w_mid, b_mid, w_top, b_top, w_out, b_out):
    width = fin.shape[1]
    outs = w_out.shape[0]
    biases = jnp.concatenate([b_in, b_mid, b_top, b_out]).reshape(-1, 1)
    return pl.pallas_call(
        mlp_kernel,
        out_shape=[
            jax.ShapeDtypeStruct((outs * height, width), jnp.bfloat16),
            jax.ShapeDtypeStruct((height, width), jnp.float32),
        ],
        scratch_shapes=[pltpu.VMEM((outs * height, width), jnp.float32)],
        compiler_params=pltpu.CompilerParams(vmem_limit_bytes=16 * 1024 * 1024),
    )(fin, w_in.T, w_mid, w_top, w_out, biases)


def local(state, speed_x, speed_y, w_in, b_in, w_mid, b_mid, w_top, b_top, w_out, b_out, span_of):
    feats, height, breadth = state.shape
    across = np.kron(np.eye(breadth // NP, dtype=np.float32), TABLE.T)
    ahi_np = across.astype(jnp.bfloat16)
    alo_np = (across - ahi_np.astype(np.float32)).astype(jnp.bfloat16)
    smat = np.zeros((breadth, breadth), np.float64)
    for lane in range(breadth):
        if lane % NP == NP - 1:
            smat[lane, lane] = 0.5
            if lane + 1 < breadth:
                smat[lane + 1, lane] = 0.5
        elif lane % NP == 0:
            smat[lane, lane] = 0.5
            if lane > 0:
                smat[lane - 1, lane] = 0.5
        else:
            smat[lane, lane] = 1.0
    fused = (across.astype(np.float64) @ smat).astype(np.float32)
    fhi_np = fused.astype(jnp.bfloat16)
    flo_np = (fused - fhi_np.astype(np.float32)).astype(jnp.bfloat16)
    mats = jnp.asarray(
        np.concatenate([ahi_np, alo_np, fhi_np, flo_np, smat.astype(jnp.bfloat16)], axis=0)
    )
    speeds = jnp.broadcast_to(jnp.concatenate([speed_x, speed_y])[:, None], (2 * feats, breadth))
    v0 = state.reshape(feats * height, breadth)
    ex, ey = run_section(v0, None, speeds, mats, None, first=True, combo=None, edges=True)
    field = v0
    combos = [(None, None), (0.75, 0.25), ("third", None)]
    for k, combo in enumerate(combos):
        halos = exchange(ex, ey)
        outs = run_section(
            field, v0, speeds, mats, halos, first=False, combo=combo, edges=k < 2
        )
        if k < 2:
            field, ex, ey = outs
        else:
            (field,) = outs
    final_state = field.reshape(feats, height, breadth)
    column_count = height * breadth
    target = span_of.reshape(column_count)
    devices = lax.axis_size("face") * lax.axis_size("elem")
    span_ids = jnp.arange(devices, dtype=jnp.int32)
    tend_rows, heat_rows = run_mlp(field, height, w_in, b_in, w_mid, b_mid, w_top, b_top, w_out, b_out)
    heating = heat_rows.reshape(column_count)
    member = (target[:, None] == span_ids[None, :]).astype(jnp.float32)
    partial_sums = jnp.sum(member * heating[:, None], axis=0)
    received = lax.all_to_all(
        partial_sums.reshape(devices, 1), ("face", "elem"), 0, 1, tiled=True
    )
    span_heating = jnp.sum(received, axis=1) / column_count
    tendencies = tend_rows.reshape(-1, height, breadth)
    return (final_state, tendencies, span_heating)


def solution(mesh):
    return jax.shard_map(
        local,
        mesh=mesh,
        in_specs=(
            P(None, "face", "elem"),
            P(),
            P(),
            P(),
            P(),
            P(),
            P(),
            P(),
            P(),
            P(),
            P(),
            P("face", "elem", None, None),
        ),
        out_specs=(P(None, "face", "elem"), P(None, "face", "elem"), P(("face", "elem"))),
        check_vma=False,
    )
```

```python
import functools
import math

import jax
import jax.numpy as jnp
import numpy as np
from jax import lax
from jax.experimental import pallas as pl
from jax.experimental.pallas import tpu as pltpu
from jax.sharding import PartitionSpec as P

NP = 4
LEV = 72
CHUNK = 48
FOLD = CHUNK // 2


def gll_matrix():
    inner_node = 1.0 / math.sqrt(5.0)
    gll_nodes = np.array([-1.0, -inner_node, inner_node, 1.0])
    weights = np.array(
        [
            1.0
            / np.prod([gll_nodes[outer] - gll_nodes[other] for other in range(4) if other != outer])
            for outer in range(4)
        ]
    )
    matrix = np.zeros((4, 4))
    for outer in range(4):
        for inner in range(4):
            if inner != outer:
                matrix[outer, inner] = (
                    weights[inner] / weights[outer] / (gll_nodes[outer] - gll_nodes[inner])
                )
    for outer in range(4):
        matrix[outer, outer] = -np.sum(matrix[outer])
    return matrix.astype(np.float32)


TABLE = gll_matrix()


def lanes(shape):
    return lax.broadcasted_iota(jnp.int32, shape, len(shape) - 1)


def roll(x, shift):
    shift = shift % x.shape[-1]
    return x if shift == 0 else pltpu.roll(x, shift, x.ndim - 1)


def raw_slabs(slabs, sx, sy, ahi, alo):
    rows = slabs[0].shape[0]
    stacked = jnp.concatenate(slabs, axis=0)
    hi = stacked.astype(jnp.bfloat16)
    lo = (stacked - hi.astype(jnp.float32)).astype(jnp.bfloat16)
    along_x = (
        jnp.dot(hi, ahi, preferred_element_type=jnp.float32)
        + jnp.dot(hi, alo, preferred_element_type=jnp.float32)
        + jnp.dot(lo, ahi, preferred_element_type=jnp.float32)
    )
    out = []
    for y, _ in enumerate(slabs):
        base = (y // NP) * NP
        j = y % NP
        along_y = float(TABLE[j, 0]) * slabs[base]
        for i in range(1, NP):
            along_y = along_y + float(TABLE[j, i]) * slabs[base + i]
        dx = along_x[y * rows : (y + 1) * rows]
        out.append(-(sx * dx + sy * along_y))
    return out


def pack_edges(tend):
    rows, width = tend[0].shape
    lane = lanes((rows, width))
    acc = jnp.zeros((rows, width), jnp.float32)
    for y, t in enumerate(tend):
        acc = jnp.where(lane == 2 * y, roll(t, 2 * y), acc)
        acc = jnp.where(lane == 2 * y + 1, roll(t, 2 * y + 2), acc)
    half = rows // 2
    lane_h = lanes((half, width))
    return jnp.where(lane_h < 32, acc[:half], roll(acc[half:], 32))


def unpack_edges(block):
    return jnp.concatenate([block, roll(block, 96)], axis=0)


def stiff_x(t, right_edges, left_edges, y):
    rows, width = t.shape
    lane = lanes((rows, width))
    right = jnp.where(lane == width - 1, roll(right_edges, width - 1 - 2 * y), roll(t, width - 1))
    left = jnp.where(lane == 0, roll(left_edges, width - 1 - 2 * y), roll(t, 1))
    place = lane % NP
    return jnp.where(
        place == NP - 1, 0.5 * (t + right), jnp.where(place == 0, 0.5 * (left + t), t)
    )


def section_kernel(*refs, first, combo, edges, mlp):
    refs = list(refs)
    v0_ref = None if combo is None or combo[0] is None else refs.pop(0)
    sp_ref = refs.pop(0)
    sx_ref, sy_ref, ahi_ref, alo_ref = refs[:4]
    refs = refs[4:]
    if not first:
        exr_ref, exl_ref, dr_ref, dl_ref, top_ref, bottom_ref = refs[:6]
        refs = refs[6:]
    if mlp:
        mlp_in = refs[:5]
        refs = refs[5:]
    rows = CHUNK
    height = 16
    sx = sx_ref[...]
    sy = sy_ref[...]
    ahi = ahi_ref[...]
    alo = alo_ref[...]
    slabs = [sp_ref[pl.ds(y, rows, stride=height), :] for y in range(height)]
    tend = raw_slabs(slabs, sx, sy, ahi, alo)
    if first:
        ex_ref, ey_ref = refs
        ex_ref[...] = pack_edges(tend)
        ey_ref[0] = tend[0]
        ey_ref[1] = tend[height - 1]
        return
    exr = unpack_edges(exr_ref[...])
    exl = unpack_edges(exl_ref[...])
    dr = unpack_edges(dr_ref[...])
    dl = unpack_edges(dl_ref[...])
    tx = [stiff_x(t, exr, exl, y) for y, t in enumerate(tend)]
    down = stiff_x(top_ref[...], dr, dl, 0)
    up = stiff_x(bottom_ref[...], dr, dl, height - 1)
    ext = [up] + tx + [down]
    new = []
    for y in range(height):
        cur = ext[y + 1]
        if y % NP == NP - 1:
            op = 0.5 * (cur + ext[y + 2])
        elif y % NP == 0:
            op = 0.5 * (ext[y] + cur)
        else:
            op = cur
        inner = slabs[y] + op
        if combo[0] is None:
            val = inner
        else:
            v0 = v0_ref[pl.ds(y, rows, stride=height), :]
            if combo[0] == "third":
                val = v0 / 3.0 + 2.0 / 3.0 * inner
            else:
                val = combo[0] * v0 + combo[1] * inner
        new.append(val)
    out_ref = refs[0]
    for y in range(height):
        out_ref[pl.ds(y, rows, stride=height), :] = new[y]
    if mlp:
        tend_ref, heat_ref, held, scratch = refs[1:5]
        step = pl.program_id(0)
        start = pl.multiple_of(step * rows, rows)
        for y in range(height):
            held[y, pl.ds(start, rows), :] = new[y]

        @pl.when(step == pl.num_programs(0) - 1)
        def _():
            mlp_body(lambda y: held[y], *mlp_in, tend_ref, heat_ref, scratch)
    if edges:
        ex_ref, ey_ref = refs[1:3]
        tend = raw_slabs(new, sx, sy, ahi, alo)
        ex_ref[...] = pack_edges(tend)
        ey_ref[0] = tend[0]
        ey_ref[1] = tend[height - 1]


def run_section(field_rows, v0, speeds, mats, halos, *, first, combo, edges, mlp=None):
    total, width = field_rows.shape
    feats = speeds.shape[0] // 2
    steps = feats // CHUNK
    big = pl.BlockSpec((CHUNK * 16, width), lambda i: (i, 0))
    small = pl.BlockSpec((CHUNK, width), lambda i: (i, 0))
    small_y = pl.BlockSpec((CHUNK, width), lambda i: (i + steps, 0))
    const = pl.BlockSpec((width, width), lambda i: (0, 0))
    const_lo = pl.BlockSpec((width, width), lambda i: (1, 0))
    edge = pl.BlockSpec((FOLD, width), lambda i: (i, 0))
    rowsb = pl.BlockSpec((2, CHUNK, width), lambda i: (0, i, 0))
    args, specs = [], []
    if combo is not None and combo[0] is not None:
        args.append(v0)
        specs.append(big)
    args += [field_rows, speeds, speeds, mats, mats]
    specs += [big, small, small_y, const, const_lo]
    if not first:
        exr, exl, partner = halos
        blocks = field_rows.shape[0] // (CHUNK * 16)
        args += [exr, exl, partner, partner, partner, partner]
        specs += [
            edge,
            edge,
            pl.BlockSpec((FOLD, width), lambda i: (4 * blocks + i, 0)),
            pl.BlockSpec((FOLD, width), lambda i: (5 * blocks + i, 0)),
            pl.BlockSpec((CHUNK, width), lambda i: (i, 0)),
            pl.BlockSpec((CHUNK, width), lambda i: (blocks + i, 0)),
        ]
    out_shape, out_specs = [], []
    ex_shape = jax.ShapeDtypeStruct((feats // 2, width), jnp.float32)
    ey_shape = jax.ShapeDtypeStruct((2, feats, width), jnp.float32)
    if first:
        out_shape = [ex_shape, ey_shape]
        out_specs = [edge, rowsb]
    else:
        out_shape = [jax.ShapeDtypeStruct((total, width), jnp.float32)]
        out_specs = [big]
        if edges:
            out_shape += [ex_shape, ey_shape]
            out_specs += [edge, rowsb]
    scratch_shapes = []
    limit = 16
    if mlp is not None:
        height = field_rows.shape[0] // feats
        outs = mlp[3].shape[0]
        whole = lambda a: pl.BlockSpec(a.shape, lambda i: (0,) * a.ndim)
        args += list(mlp)
        specs += [whole(a) for a in mlp]
        out_shape += [
            jax.ShapeDtypeStruct((outs * height, width), jnp.bfloat16),
            jax.ShapeDtypeStruct((height, width), jnp.float32),
        ]
        out_specs += [whole(out_shape[-2]), whole(out_shape[-1])]
        scratch_shapes = [
            pltpu.VMEM((height, feats, width), jnp.float32),
            pltpu.VMEM((outs * height, width), jnp.float32),
        ]
        limit = 32
    kernel = functools.partial(section_kernel, first=first, combo=combo, edges=edges, mlp=mlp is not None)
    return pl.pallas_call(
        kernel,
        grid=(steps,),
        in_specs=specs,
        out_specs=out_specs,
        out_shape=out_shape,
        scratch_shapes=scratch_shapes,
        compiler_params=pltpu.CompilerParams(vmem_limit_bytes=limit * 1024 * 1024),
    )(*args)


def exchange(ex, ey):
    n_face = lax.axis_size("face")
    n_elem = lax.axis_size("elem")
    assert n_face == 2
    from_right = [(j, (j - 1) % n_elem) for j in range(n_elem)]
    from_left = [(j, (j + 1) % n_elem) for j in range(n_elem)]
    exr = lax.ppermute(ex, "elem", from_right)
    exl = lax.ppermute(ex, "elem", from_left)
    feats = ey.shape[1]
    bundle = jnp.concatenate([ey.reshape(2 * feats, ey.shape[2]), exr, exl], axis=0)
    partner = lax.ppermute(bundle, "face", [(0, 1), (1, 0)])
    return (exr, exl, partner)


def column_model(inputs, w_in, b_in, w_mid, b_mid, w_top, b_top, w_out, b_out):
    hidden = jax.nn.silu(
        jnp.dot(w_in, inputs, preferred_element_type=jnp.float32) + b_in[:, None]
    ).astype(jnp.bfloat16)
    hidden = jax.nn.silu(
        jnp.dot(w_mid, hidden, preferred_element_type=jnp.float32) + b_mid[:, None]
    ).astype(jnp.bfloat16)
    hidden = jax.nn.silu(
        jnp.dot(w_top, hidden, preferred_element_type=jnp.float32) + b_top[:, None]
    ).astype(jnp.bfloat16)
    outputs = jnp.dot(w_out, hidden, preferred_element_type=jnp.float32) + b_out[:, None]
    heating = jnp.sum(outputs[:LEV], axis=0)
    return (outputs.astype(jnp.bfloat16), heating)


def mlp_kernel(fin_ref, w_in_ref, w_mid_ref, w_top_ref, w_out_ref, b_ref, tend_ref, heat_ref, scratch):
    feats = w_in_ref.shape[0]
    height = heat_ref.shape[0]
    mlp_body(
        lambda y: fin_ref[pl.ds(y, feats, stride=height), :],
        w_in_ref, w_mid_ref, w_top_ref, w_out_ref, b_ref, tend_ref, heat_ref, scratch,
    )


def mlp_body(slab, w_in_ref, w_mid_ref, w_top_ref, w_out_ref, b_ref, tend_ref, heat_ref, scratch):
    outs = w_out_ref.shape[0]
    height = heat_ref.shape[0]
    width = heat_ref.shape[1]

    def act(a):
        return (a * (0.5 + 0.5 * jnp.tanh(0.5 * a))).astype(jnp.bfloat16)

    hid = w_mid_ref.shape[0]
    b_in = b_ref[0:hid]
    b_mid = b_ref[hid : 2 * hid]
    b_top = b_ref[2 * hid : 3 * hid]
    b_out = b_ref[3 * hid : 3 * hid + outs]

    for pair in range(height // 2):
        y = 2 * pair
        x = jnp.concatenate([slab(y), slab(y + 1)], axis=1).astype(jnp.bfloat16)
        h = act(
            lax.dot_general(
                w_in_ref[...], x, (((0,), (0,)), ((), ())), preferred_element_type=jnp.float32
            )
            + b_in
        )
        h = act(jnp.dot(w_mid_ref[...], h, preferred_element_type=jnp.float32) + b_mid)
        h = act(jnp.dot(w_top_ref[...], h, preferred_element_type=jnp.float32) + b_top)
        out = jnp.dot(w_out_ref[...], h, preferred_element_type=jnp.float32) + b_out
        heat = jnp.sum(out[:LEV], axis=0, keepdims=True)
        heat_ref[y : y + 1, :] = heat[:, :width]
        heat_ref[y + 1 : y + 2, :] = heat[:, width:]
        scratch[pl.ds(y, outs, stride=height), :] = out[:, :width]
        scratch[pl.ds(y + 1, outs, stride=height), :] = out[:, width:]
    tend_ref[...] = scratch[...].astype(jnp.bfloat16)


def run_mlp(fin, height, w_in, b_in, w_mid, b_mid, w_top, b_top, w_out, b_out):
    width = fin.shape[1]
    outs = w_out.shape[0]
    biases = jnp.concatenate([b_in, b_mid, b_top, b_out]).reshape(-1, 1)
    return pl.pallas_call(
        mlp_kernel,
        out_shape=[
            jax.ShapeDtypeStruct((outs * height, width), jnp.bfloat16),
            jax.ShapeDtypeStruct((height, width), jnp.float32),
        ],
        scratch_shapes=[pltpu.VMEM((outs * height, width), jnp.float32)],
        compiler_params=pltpu.CompilerParams(vmem_limit_bytes=16 * 1024 * 1024),
    )(fin, w_in.T, w_mid, w_top, w_out, biases)


def local(state, speed_x, speed_y, w_in, b_in, w_mid, b_mid, w_top, b_top, w_out, b_out, span_of):
    feats, height, breadth = state.shape
    across = np.kron(np.eye(breadth // NP, dtype=np.float32), TABLE.T)
    ahi_np = across.astype(jnp.bfloat16)
    alo_np = (across - ahi_np.astype(np.float32)).astype(jnp.bfloat16)
    mats = jnp.asarray(np.concatenate([ahi_np, alo_np], axis=0))
    speeds = jnp.broadcast_to(jnp.concatenate([speed_x, speed_y])[:, None], (2 * feats, breadth))
    v0 = state.reshape(feats * height, breadth)
    ex, ey = run_section(v0, None, speeds, mats, None, first=True, combo=None, edges=True)
    field = v0
    combos = [(None, None), (0.75, 0.25), ("third", None)]
    for k, combo in enumerate(combos):
        halos = exchange(ex, ey)
        extra = None
        if k == 2:
            biases = jnp.concatenate([b_in, b_mid, b_top, b_out]).reshape(-1, 1)
            extra = (w_in.T, w_mid, w_top, w_out, biases)
        outs = run_section(
            field, v0, speeds, mats, halos, first=False, combo=combo, edges=k < 2, mlp=extra
        )
        if k < 2:
            field, ex, ey = outs
        else:
            field, tend_rows, heat_rows = outs
    final_state = field.reshape(feats, height, breadth)
    column_count = height * breadth
    target = span_of.reshape(column_count)
    devices = lax.axis_size("face") * lax.axis_size("elem")
    span_ids = jnp.arange(devices, dtype=jnp.int32)
    heating = heat_rows.reshape(column_count)
    member = (target[:, None] == span_ids[None, :]).astype(jnp.float32)
    partial_sums = jnp.sum(member * heating[:, None], axis=0)
    received = lax.all_to_all(
        partial_sums.reshape(devices, 1), ("face", "elem"), 0, 1, tiled=True
    )
    span_heating = jnp.sum(received, axis=1) / column_count
    tendencies = tend_rows.reshape(-1, height, breadth)
    return (final_state, tendencies, span_heating)


def solution(mesh):
    return jax.shard_map(
        local,
        mesh=mesh,
        in_specs=(
            P(None, "face", "elem"),
            P(),
            P(),
            P(),
            P(),
            P(),
            P(),
            P(),
            P(),
            P(),
            P(),
            P("face", "elem", None, None),
        ),
        out_specs=(P(None, "face", "elem"), P(None, "face", "elem"), P(("face", "elem"))),
        check_vma=False,
    )
```

```python
import functools
import math

import jax
import jax.numpy as jnp
import numpy as np
from jax import lax
from jax.experimental import pallas as pl
from jax.experimental.pallas import tpu as pltpu
from jax.sharding import PartitionSpec as P

NP = 4
LEV = 72
CHUNK = 48
FOLD = CHUNK // 2


def gll_matrix():
    inner_node = 1.0 / math.sqrt(5.0)
    gll_nodes = np.array([-1.0, -inner_node, inner_node, 1.0])
    weights = np.array(
        [
            1.0
            / np.prod([gll_nodes[outer] - gll_nodes[other] for other in range(4) if other != outer])
            for outer in range(4)
        ]
    )
    matrix = np.zeros((4, 4))
    for outer in range(4):
        for inner in range(4):
            if inner != outer:
                matrix[outer, inner] = (
                    weights[inner] / weights[outer] / (gll_nodes[outer] - gll_nodes[inner])
                )
    for outer in range(4):
        matrix[outer, outer] = -np.sum(matrix[outer])
    return matrix.astype(np.float32)


TABLE = gll_matrix()


def lanes(shape):
    return lax.broadcasted_iota(jnp.int32, shape, len(shape) - 1)


def roll(x, shift):
    shift = shift % x.shape[-1]
    return x if shift == 0 else pltpu.roll(x, shift, x.ndim - 1)


def raw_slabs(slabs, sx, sy, ahi, alo):
    rows = slabs[0].shape[0]
    stacked = jnp.concatenate(slabs, axis=0)
    hi = stacked.astype(jnp.bfloat16)
    lo = (stacked - hi.astype(jnp.float32)).astype(jnp.bfloat16)
    along_x = (
        jnp.dot(hi, ahi, preferred_element_type=jnp.float32)
        + jnp.dot(hi, alo, preferred_element_type=jnp.float32)
        + jnp.dot(lo, ahi, preferred_element_type=jnp.float32)
    )
    out = []
    for y, _ in enumerate(slabs):
        base = (y // NP) * NP
        j = y % NP
        along_y = float(TABLE[j, 0]) * slabs[base]
        for i in range(1, NP):
            along_y = along_y + float(TABLE[j, i]) * slabs[base + i]
        dx = along_x[y * rows : (y + 1) * rows]
        out.append(-(sx * dx + sy * along_y))
    return out


def pack_edges(tend):
    rows, width = tend[0].shape
    lane = lanes((rows, width))
    acc = jnp.zeros((rows, width), jnp.float32)
    for y, t in enumerate(tend):
        acc = jnp.where(lane == 2 * y, roll(t, 2 * y), acc)
        acc = jnp.where(lane == 2 * y + 1, roll(t, 2 * y + 2), acc)
    half = rows // 2
    lane_h = lanes((half, width))
    return jnp.where(lane_h < 32, acc[:half], roll(acc[half:], 32))


def unpack_edges(block):
    return jnp.concatenate([block, roll(block, 96)], axis=0)


def stiff_x(t, right_edges, left_edges, y):
    rows, width = t.shape
    lane = lanes((rows, width))
    right = jnp.where(lane == width - 1, roll(right_edges, width - 1 - 2 * y), roll(t, width - 1))
    left = jnp.where(lane == 0, roll(left_edges, width - 1 - 2 * y), roll(t, 1))
    place = lane % NP
    return jnp.where(
        place == NP - 1, 0.5 * (t + right), jnp.where(place == 0, 0.5 * (left + t), t)
    )


def section_kernel(*refs, first, combo, edges, mlp):
    refs = list(refs)
    v0_ref = None if combo is None or combo[0] is None else refs.pop(0)
    sp_ref = refs.pop(0)
    sx_ref, sy_ref, ahi_ref, alo_ref = refs[:4]
    refs = refs[4:]
    if not first:
        exr_ref, exl_ref, dr_ref, dl_ref, top_ref, bottom_ref = refs[:6]
        refs = refs[6:]
    if mlp:
        mlp_in = refs[:5]
        refs = refs[5:]
    rows = CHUNK
    height = 16
    sx = sx_ref[...]
    sy = sy_ref[...]
    ahi = ahi_ref[...]
    alo = alo_ref[...]
    slabs = [sp_ref[pl.ds(y, rows, stride=height), :] for y in range(height)]
    tend = raw_slabs(slabs, sx, sy, ahi, alo)
    if first:
        ex_ref, ey_ref = refs
        ex_ref[...] = pack_edges(tend)
        ey_ref[0] = tend[0]
        ey_ref[1] = tend[height - 1]
        return
    exr = unpack_edges(exr_ref[...])
    exl = unpack_edges(exl_ref[...])
    dr = unpack_edges(dr_ref[...])
    dl = unpack_edges(dl_ref[...])
    tx = [stiff_x(t, exr, exl, y) for y, t in enumerate(tend)]
    down = stiff_x(top_ref[...], dr, dl, 0)
    up = stiff_x(bottom_ref[...], dr, dl, height - 1)
    ext = [up] + tx + [down]
    new = []
    for y in range(height):
        cur = ext[y + 1]
        if y % NP == NP - 1:
            op = 0.5 * (cur + ext[y + 2])
        elif y % NP == 0:
            op = 0.5 * (ext[y] + cur)
        else:
            op = cur
        inner = slabs[y] + op
        if combo[0] is None:
            val = inner
        else:
            v0 = v0_ref[pl.ds(y, rows, stride=height), :]
            if combo[0] == "third":
                val = v0 / 3.0 + 2.0 / 3.0 * inner
            else:
                val = combo[0] * v0 + combo[1] * inner
        new.append(val)
    out_ref = refs[0]
    for y in range(height):
        out_ref[pl.ds(y, rows, stride=height), :] = new[y]
    if mlp:
        tend_ref, heat_ref, held, scratch = refs[1:5]
        step = pl.program_id(0)
        start = pl.multiple_of(step * rows, rows)
        for y in range(height):
            held[y, pl.ds(start, rows), :] = new[y]

        @pl.when(step == pl.num_programs(0) - 1)
        def _():
            mlp_body(lambda y: held[y], *mlp_in, tend_ref, heat_ref, scratch)
    if edges:
        ex_ref, ey_ref = refs[1:3]
        tend = raw_slabs(new, sx, sy, ahi, alo)
        ex_ref[...] = pack_edges(tend)
        ey_ref[0] = tend[0]
        ey_ref[1] = tend[height - 1]


def run_section(field_rows, v0, speeds, mats, halos, *, first, combo, edges, mlp=None):
    total, width = field_rows.shape
    feats = speeds.shape[0] // 2
    steps = feats // CHUNK
    big = pl.BlockSpec((CHUNK * 16, width), lambda i: (i, 0))
    small = pl.BlockSpec((CHUNK, width), lambda i: (i, 0))
    small_y = pl.BlockSpec((CHUNK, width), lambda i: (i + steps, 0))
    const = pl.BlockSpec((width, width), lambda i: (0, 0))
    const_lo = pl.BlockSpec((width, width), lambda i: (1, 0))
    edge = pl.BlockSpec((FOLD, width), lambda i: (i, 0))
    rowsb = pl.BlockSpec((2, CHUNK, width), lambda i: (0, i, 0))
    args, specs = [], []
    if combo is not None and combo[0] is not None:
        args.append(v0)
        specs.append(big)
    args += [field_rows, speeds, speeds, mats, mats]
    specs += [big, small, small_y, const, const_lo]
    if not first:
        exr, exl, corners, rows = halos
        blocks = field_rows.shape[0] // (CHUNK * 16)
        args += [exr, exl, corners, corners, rows, rows]
        specs += [
            edge,
            edge,
            pl.BlockSpec((FOLD, width), lambda i: (i, 0)),
            pl.BlockSpec((FOLD, width), lambda i: (blocks + i, 0)),
            pl.BlockSpec((CHUNK, width), lambda i: (i, 0)),
            pl.BlockSpec((CHUNK, width), lambda i: (blocks + i, 0)),
        ]
    out_shape, out_specs = [], []
    ex_shape = jax.ShapeDtypeStruct((feats // 2, width), jnp.float32)
    ey_shape = jax.ShapeDtypeStruct((2, feats, width), jnp.float32)
    if first:
        out_shape = [ex_shape, ey_shape]
        out_specs = [edge, rowsb]
    else:
        out_shape = [jax.ShapeDtypeStruct((total, width), jnp.float32)]
        out_specs = [big]
        if edges:
            out_shape += [ex_shape, ey_shape]
            out_specs += [edge, rowsb]
    scratch_shapes = []
    limit = 16
    if mlp is not None:
        height = field_rows.shape[0] // feats
        outs = mlp[3].shape[0]
        whole = lambda a: pl.BlockSpec(a.shape, lambda i: (0,) * a.ndim)
        args += list(mlp)
        specs += [whole(a) for a in mlp]
        out_shape += [
            jax.ShapeDtypeStruct((outs * height, width), jnp.bfloat16),
            jax.ShapeDtypeStruct((height, width), jnp.float32),
        ]
        out_specs += [whole(out_shape[-2]), whole(out_shape[-1])]
        scratch_shapes = [
            pltpu.VMEM((height, feats, width), jnp.float32),
            pltpu.VMEM((outs * height, width), jnp.float32),
        ]
        limit = 32
    kernel = functools.partial(section_kernel, first=first, combo=combo, edges=edges, mlp=mlp is not None)
    return pl.pallas_call(
        kernel,
        grid=(steps,),
        in_specs=specs,
        out_specs=out_specs,
        out_shape=out_shape,
        scratch_shapes=scratch_shapes,
        compiler_params=pltpu.CompilerParams(vmem_limit_bytes=limit * 1024 * 1024),
    )(*args)


def exchange(ex, ey):
    n_face = lax.axis_size("face")
    n_elem = lax.axis_size("elem")
    assert n_face == 2
    from_right = [(j, (j - 1) % n_elem) for j in range(n_elem)]
    from_left = [(j, (j + 1) % n_elem) for j in range(n_elem)]
    exr = lax.ppermute(ex, "elem", from_right)
    exl = lax.ppermute(ex, "elem", from_left)
    feats = ey.shape[1]
    swap = [(0, 1), (1, 0)]
    rows = lax.ppermute(ey.reshape(2 * feats, ey.shape[2]), "face", swap)
    corners = lax.ppermute(jnp.concatenate([exr, exl], axis=0), "face", swap)
    return (exr, exl, corners, rows)


def column_model(inputs, w_in, b_in, w_mid, b_mid, w_top, b_top, w_out, b_out):
    hidden = jax.nn.silu(
        jnp.dot(w_in, inputs, preferred_element_type=jnp.float32) + b_in[:, None]
    ).astype(jnp.bfloat16)
    hidden = jax.nn.silu(
        jnp.dot(w_mid, hidden, preferred_element_type=jnp.float32) + b_mid[:, None]
    ).astype(jnp.bfloat16)
    hidden = jax.nn.silu(
        jnp.dot(w_top, hidden, preferred_element_type=jnp.float32) + b_top[:, None]
    ).astype(jnp.bfloat16)
    outputs = jnp.dot(w_out, hidden, preferred_element_type=jnp.float32) + b_out[:, None]
    heating = jnp.sum(outputs[:LEV], axis=0)
    return (outputs.astype(jnp.bfloat16), heating)


def mlp_kernel(fin_ref, w_in_ref, w_mid_ref, w_top_ref, w_out_ref, b_ref, tend_ref, heat_ref, scratch):
    feats = w_in_ref.shape[0]
    height = heat_ref.shape[0]
    mlp_body(
        lambda y: fin_ref[pl.ds(y, feats, stride=height), :],
        w_in_ref, w_mid_ref, w_top_ref, w_out_ref, b_ref, tend_ref, heat_ref, scratch,
    )


def mlp_body(slab, w_in_ref, w_mid_ref, w_top_ref, w_out_ref, b_ref, tend_ref, heat_ref, scratch):
    outs = w_out_ref.shape[0]
    height = heat_ref.shape[0]
    width = heat_ref.shape[1]

    def act(a):
        return (a * (0.5 + 0.5 * jnp.tanh(0.5 * a))).astype(jnp.bfloat16)

    hid = w_mid_ref.shape[0]
    b_in = b_ref[0:hid]
    b_mid = b_ref[hid : 2 * hid]
    b_top = b_ref[2 * hid : 3 * hid]
    b_out = b_ref[3 * hid : 3 * hid + outs]

    for pair in range(height // 2):
        y = 2 * pair
        x = jnp.concatenate([slab(y), slab(y + 1)], axis=1).astype(jnp.bfloat16)
        h = act(
            lax.dot_general(
                w_in_ref[...], x, (((0,), (0,)), ((), ())), preferred_element_type=jnp.float32
            )
            + b_in
        )
        h = act(jnp.dot(w_mid_ref[...], h, preferred_element_type=jnp.float32) + b_mid)
        h = act(jnp.dot(w_top_ref[...], h, preferred_element_type=jnp.float32) + b_top)
        out = jnp.dot(w_out_ref[...], h, preferred_element_type=jnp.float32) + b_out
        heat = jnp.sum(out[:LEV], axis=0, keepdims=True)
        heat_ref[y : y + 1, :] = heat[:, :width]
        heat_ref[y + 1 : y + 2, :] = heat[:, width:]
        scratch[pl.ds(y, outs, stride=height), :] = out[:, :width]
        scratch[pl.ds(y + 1, outs, stride=height), :] = out[:, width:]
    tend_ref[...] = scratch[...].astype(jnp.bfloat16)


def run_mlp(fin, height, w_in, b_in, w_mid, b_mid, w_top, b_top, w_out, b_out):
    width = fin.shape[1]
    outs = w_out.shape[0]
    biases = jnp.concatenate([b_in, b_mid, b_top, b_out]).reshape(-1, 1)
    return pl.pallas_call(
        mlp_kernel,
        out_shape=[
            jax.ShapeDtypeStruct((outs * height, width), jnp.bfloat16),
            jax.ShapeDtypeStruct((height, width), jnp.float32),
        ],
        scratch_shapes=[pltpu.VMEM((outs * height, width), jnp.float32)],
        compiler_params=pltpu.CompilerParams(vmem_limit_bytes=16 * 1024 * 1024),
    )(fin, w_in.T, w_mid, w_top, w_out, biases)


def local(state, speed_x, speed_y, w_in, b_in, w_mid, b_mid, w_top, b_top, w_out, b_out, span_of):
    feats, height, breadth = state.shape
    across = np.kron(np.eye(breadth // NP, dtype=np.float32), TABLE.T)
    ahi_np = across.astype(jnp.bfloat16)
    alo_np = (across - ahi_np.astype(np.float32)).astype(jnp.bfloat16)
    mats = jnp.asarray(np.concatenate([ahi_np, alo_np], axis=0))
    speeds = jnp.broadcast_to(jnp.concatenate([speed_x, speed_y])[:, None], (2 * feats, breadth))
    v0 = state.reshape(feats * height, breadth)
    ex, ey = run_section(v0, None, speeds, mats, None, first=True, combo=None, edges=True)
    field = v0
    combos = [(None, None), (0.75, 0.25), ("third", None)]
    for k, combo in enumerate(combos):
        halos = exchange(ex, ey)
        extra = None
        if k == 2:
            biases = jnp.concatenate([b_in, b_mid, b_top, b_out]).reshape(-1, 1)
            extra = (w_in.T, w_mid, w_top, w_out, biases)
        outs = run_section(
            field, v0, speeds, mats, halos, first=False, combo=combo, edges=k < 2, mlp=extra
        )
        if k < 2:
            field, ex, ey = outs
        else:
            field, tend_rows, heat_rows = outs
    final_state = field.reshape(feats, height, breadth)
    column_count = height * breadth
    target = span_of.reshape(column_count)
    devices = lax.axis_size("face") * lax.axis_size("elem")
    span_ids = jnp.arange(devices, dtype=jnp.int32)
    heating = heat_rows.reshape(column_count)
    member = (target[:, None] == span_ids[None, :]).astype(jnp.float32)
    partial_sums = jnp.sum(member * heating[:, None], axis=0)
    received = lax.all_to_all(
        partial_sums.reshape(devices, 1), ("face", "elem"), 0, 1, tiled=True
    )
    span_heating = jnp.sum(received, axis=1) / column_count
    tendencies = tend_rows.reshape(-1, height, breadth)
    return (final_state, tendencies, span_heating)


def solution(mesh):
    return jax.shard_map(
        local,
        mesh=mesh,
        in_specs=(
            P(None, "face", "elem"),
            P(),
            P(),
            P(),
            P(),
            P(),
            P(),
            P(),
            P(),
            P(),
            P(),
            P("face", "elem", None, None),
        ),
        out_specs=(P(None, "face", "elem"), P(None, "face", "elem"), P(("face", "elem"))),
        check_vma=False,
    )
```

```python
import functools
import math

import jax
import jax.numpy as jnp
import numpy as np
from jax import lax
from jax.experimental import pallas as pl
from jax.experimental.pallas import tpu as pltpu
from jax.sharding import PartitionSpec as P

NP = 4
LEV = 72
CHUNK = 48
FOLD = CHUNK // 2


def gll_matrix():
    inner_node = 1.0 / math.sqrt(5.0)
    gll_nodes = np.array([-1.0, -inner_node, inner_node, 1.0])
    weights = np.array(
        [
            1.0
            / np.prod([gll_nodes[outer] - gll_nodes[other] for other in range(4) if other != outer])
            for outer in range(4)
        ]
    )
    matrix = np.zeros((4, 4))
    for outer in range(4):
        for inner in range(4):
            if inner != outer:
                matrix[outer, inner] = (
                    weights[inner] / weights[outer] / (gll_nodes[outer] - gll_nodes[inner])
                )
    for outer in range(4):
        matrix[outer, outer] = -np.sum(matrix[outer])
    return matrix.astype(np.float32)


TABLE = gll_matrix()


def lanes(shape):
    return lax.broadcasted_iota(jnp.int32, shape, len(shape) - 1)


def roll(x, shift):
    shift = shift % x.shape[-1]
    return x if shift == 0 else pltpu.roll(x, shift, x.ndim - 1)


def raw_slabs(slabs, sx, sy, ahi, alo):
    rows = slabs[0].shape[0]
    stacked = jnp.concatenate(slabs, axis=0)
    hi = stacked.astype(jnp.bfloat16)
    lo = (stacked - hi.astype(jnp.float32)).astype(jnp.bfloat16)
    along_x = (
        jnp.dot(hi, ahi, preferred_element_type=jnp.float32)
        + jnp.dot(hi, alo, preferred_element_type=jnp.float32)
        + jnp.dot(lo, ahi, preferred_element_type=jnp.float32)
    )
    out = []
    for y, _ in enumerate(slabs):
        base = (y // NP) * NP
        j = y % NP
        along_y = float(TABLE[j, 0]) * slabs[base]
        for i in range(1, NP):
            along_y = along_y + float(TABLE[j, i]) * slabs[base + i]
        dx = along_x[y * rows : (y + 1) * rows]
        out.append(-(sx * dx + sy * along_y))
    return out


def pack_edges(tend):
    rows, width = tend[0].shape
    lane = lanes((rows, width))
    acc = jnp.zeros((rows, width), jnp.float32)
    for y, t in enumerate(tend):
        acc = jnp.where(lane == 2 * y, roll(t, 2 * y), acc)
        acc = jnp.where(lane == 2 * y + 1, roll(t, 2 * y + 2), acc)
    half = rows // 2
    lane_h = lanes((half, width))
    return jnp.where(lane_h < 32, acc[:half], roll(acc[half:], 32))


def unpack_edges(block):
    return jnp.concatenate([block, roll(block, 96)], axis=0)


def stiff_x(t, right_edges, left_edges, y):
    rows, width = t.shape
    lane = lanes((rows, width))
    right = jnp.where(lane == width - 1, roll(right_edges, width - 1 - 2 * y), roll(t, width - 1))
    left = jnp.where(lane == 0, roll(left_edges, width - 1 - 2 * y), roll(t, 1))
    place = lane % NP
    return jnp.where(
        place == NP - 1, 0.5 * (t + right), jnp.where(place == 0, 0.5 * (left + t), t)
    )


def section_kernel(*refs, first, combo, edges, mlp):
    refs = list(refs)
    v0_ref = None if combo is None or combo[0] is None else refs.pop(0)
    sp_ref = refs.pop(0)
    sx_ref, sy_ref, ahi_ref, alo_ref = refs[:4]
    refs = refs[4:]
    if not first:
        exr_ref, exl_ref, dr_ref, dl_ref, top_ref, bottom_ref = refs[:6]
        refs = refs[6:]
    if mlp:
        mlp_in = refs[:5]
        refs = refs[5:]
    rows = CHUNK
    height = 16
    sx = sx_ref[...]
    sy = sy_ref[...]
    ahi = ahi_ref[...]
    alo = alo_ref[...]
    slabs = [sp_ref[pl.ds(y, rows, stride=height), :] for y in range(height)]
    tend = raw_slabs(slabs, sx, sy, ahi, alo)
    if first:
        ex_ref, ey_ref = refs
        ex_ref[...] = pack_edges(tend)
        ey_ref[0] = tend[0]
        ey_ref[1] = tend[height - 1]
        return
    exr = unpack_edges(exr_ref[...])
    exl = unpack_edges(exl_ref[...])
    dr = unpack_edges(dr_ref[...])
    dl = unpack_edges(dl_ref[...])
    tx = [stiff_x(t, exr, exl, y) for y, t in enumerate(tend)]
    down = stiff_x(top_ref[...], dr, dl, 0)
    up = stiff_x(bottom_ref[...], dr, dl, height - 1)
    ext = [up] + tx + [down]
    new = []
    for y in range(height):
        cur = ext[y + 1]
        if y % NP == NP - 1:
            op = 0.5 * (cur + ext[y + 2])
        elif y % NP == 0:
            op = 0.5 * (ext[y] + cur)
        else:
            op = cur
        inner = slabs[y] + op
        if combo[0] is None:
            val = inner
        else:
            v0 = v0_ref[pl.ds(y, rows, stride=height), :]
            if combo[0] == "third":
                val = v0 / 3.0 + 2.0 / 3.0 * inner
            else:
                val = combo[0] * v0 + combo[1] * inner
        new.append(val)
    out_ref = refs[0]
    for y in range(height):
        out_ref[pl.ds(y, rows, stride=height), :] = new[y]
    if mlp:
        tend_ref, heat_ref, held, scratch = refs[1:5]
        step = pl.program_id(0)
        start = pl.multiple_of(step * rows, rows)
        for y in range(height):
            held[y, pl.ds(start, rows), :] = new[y]

        @pl.when(step == pl.num_programs(0) - 1)
        def _():
            mlp_body(lambda y: held[y], *mlp_in, tend_ref, heat_ref, scratch)
    if edges:
        ex_ref, ey_ref = refs[1:3]
        tend = raw_slabs(new, sx, sy, ahi, alo)
        ex_ref[...] = pack_edges(tend)
        ey_ref[0] = tend[0]
        ey_ref[1] = tend[height - 1]


def run_section(field_rows, v0, speeds, mats, halos, *, first, combo, edges, mlp=None):
    total, width = field_rows.shape
    feats = speeds.shape[0] // 2
    steps = feats // CHUNK
    big = pl.BlockSpec((CHUNK * 16, width), lambda i: (i, 0))
    small = pl.BlockSpec((CHUNK, width), lambda i: (i, 0))
    small_y = pl.BlockSpec((CHUNK, width), lambda i: (i + steps, 0))
    const = pl.BlockSpec((width, width), lambda i: (0, 0))
    const_lo = pl.BlockSpec((width, width), lambda i: (1, 0))
    edge = pl.BlockSpec((FOLD, width), lambda i: (i, 0))
    rowsb = pl.BlockSpec((2, CHUNK, width), lambda i: (0, i, 0))
    args, specs = [], []
    if combo is not None and combo[0] is not None:
        args.append(v0)
        specs.append(big)
    args += [field_rows, speeds, speeds, mats, mats]
    specs += [big, small, small_y, const, const_lo]
    if not first:
        exr, exl, corner_r, corner_l, rows = halos
        blocks = field_rows.shape[0] // (CHUNK * 16)
        args += [exr, exl, corner_r, corner_l, rows, rows]
        specs += [
            edge,
            edge,
            edge,
            edge,
            pl.BlockSpec((CHUNK, width), lambda i: (i, 0)),
            pl.BlockSpec((CHUNK, width), lambda i: (blocks + i, 0)),
        ]
    out_shape, out_specs = [], []
    ex_shape = jax.ShapeDtypeStruct((feats // 2, width), jnp.float32)
    ey_shape = jax.ShapeDtypeStruct((2, feats, width), jnp.float32)
    if first:
        out_shape = [ex_shape, ey_shape]
        out_specs = [edge, rowsb]
    else:
        out_shape = [jax.ShapeDtypeStruct((total, width), jnp.float32)]
        out_specs = [big]
        if edges:
            out_shape += [ex_shape, ey_shape]
            out_specs += [edge, rowsb]
    scratch_shapes = []
    limit = 16
    if mlp is not None:
        height = field_rows.shape[0] // feats
        outs = mlp[3].shape[0]
        whole = lambda a: pl.BlockSpec(a.shape, lambda i: (0,) * a.ndim)
        args += list(mlp)
        specs += [whole(a) for a in mlp]
        out_shape += [
            jax.ShapeDtypeStruct((outs * height, width), jnp.bfloat16),
            jax.ShapeDtypeStruct((height, width), jnp.float32),
        ]
        out_specs += [whole(out_shape[-2]), whole(out_shape[-1])]
        scratch_shapes = [
            pltpu.VMEM((height, feats, width), jnp.float32),
            pltpu.VMEM((outs * height, width), jnp.float32),
        ]
        limit = 32
    kernel = functools.partial(section_kernel, first=first, combo=combo, edges=edges, mlp=mlp is not None)
    return pl.pallas_call(
        kernel,
        grid=(steps,),
        in_specs=specs,
        out_specs=out_specs,
        out_shape=out_shape,
        scratch_shapes=scratch_shapes,
        compiler_params=pltpu.CompilerParams(vmem_limit_bytes=limit * 1024 * 1024),
    )(*args)


def exchange(ex, ey):
    n_face = lax.axis_size("face")
    n_elem = lax.axis_size("elem")
    assert n_face == 2
    from_right = [(j, (j - 1) % n_elem) for j in range(n_elem)]
    from_left = [(j, (j + 1) % n_elem) for j in range(n_elem)]
    exr = lax.ppermute(ex, "elem", from_right)
    exl = lax.ppermute(ex, "elem", from_left)
    feats = ey.shape[1]
    swap = [(0, 1), (1, 0)]
    rows = lax.ppermute(ey.reshape(2 * feats, ey.shape[2]), "face", swap)
    corner_r = lax.ppermute(exr, "face", swap)
    corner_l = lax.ppermute(exl, "face", swap)
    return (exr, exl, corner_r, corner_l, rows)


def column_model(inputs, w_in, b_in, w_mid, b_mid, w_top, b_top, w_out, b_out):
    hidden = jax.nn.silu(
        jnp.dot(w_in, inputs, preferred_element_type=jnp.float32) + b_in[:, None]
    ).astype(jnp.bfloat16)
    hidden = jax.nn.silu(
        jnp.dot(w_mid, hidden, preferred_element_type=jnp.float32) + b_mid[:, None]
    ).astype(jnp.bfloat16)
    hidden = jax.nn.silu(
        jnp.dot(w_top, hidden, preferred_element_type=jnp.float32) + b_top[:, None]
    ).astype(jnp.bfloat16)
    outputs = jnp.dot(w_out, hidden, preferred_element_type=jnp.float32) + b_out[:, None]
    heating = jnp.sum(outputs[:LEV], axis=0)
    return (outputs.astype(jnp.bfloat16), heating)


def mlp_kernel(fin_ref, w_in_ref, w_mid_ref, w_top_ref, w_out_ref, b_ref, tend_ref, heat_ref, scratch):
    feats = w_in_ref.shape[0]
    height = heat_ref.shape[0]
    mlp_body(
        lambda y: fin_ref[pl.ds(y, feats, stride=height), :],
        w_in_ref, w_mid_ref, w_top_ref, w_out_ref, b_ref, tend_ref, heat_ref, scratch,
    )


def mlp_body(slab, w_in_ref, w_mid_ref, w_top_ref, w_out_ref, b_ref, tend_ref, heat_ref, scratch):
    outs = w_out_ref.shape[0]
    height = heat_ref.shape[0]
    width = heat_ref.shape[1]

    def act(a):
        return (a * (0.5 + 0.5 * jnp.tanh(0.5 * a))).astype(jnp.bfloat16)

    hid = w_mid_ref.shape[0]
    b_in = b_ref[0:hid]
    b_mid = b_ref[hid : 2 * hid]
    b_top = b_ref[2 * hid : 3 * hid]
    b_out = b_ref[3 * hid : 3 * hid + outs]

    for pair in range(height // 2):
        y = 2 * pair
        x = jnp.concatenate([slab(y), slab(y + 1)], axis=1).astype(jnp.bfloat16)
        h = act(
            lax.dot_general(
                w_in_ref[...], x, (((0,), (0,)), ((), ())), preferred_element_type=jnp.float32
            )
            + b_in
        )
        h = act(jnp.dot(w_mid_ref[...], h, preferred_element_type=jnp.float32) + b_mid)
        h = act(jnp.dot(w_top_ref[...], h, preferred_element_type=jnp.float32) + b_top)
        out = jnp.dot(w_out_ref[...], h, preferred_element_type=jnp.float32) + b_out
        heat = jnp.sum(out[:LEV], axis=0, keepdims=True)
        heat_ref[y : y + 1, :] = heat[:, :width]
        heat_ref[y + 1 : y + 2, :] = heat[:, width:]
        scratch[pl.ds(y, outs, stride=height), :] = out[:, :width]
        scratch[pl.ds(y + 1, outs, stride=height), :] = out[:, width:]
    tend_ref[...] = scratch[...].astype(jnp.bfloat16)


def run_mlp(fin, height, w_in, b_in, w_mid, b_mid, w_top, b_top, w_out, b_out):
    width = fin.shape[1]
    outs = w_out.shape[0]
    biases = jnp.concatenate([b_in, b_mid, b_top, b_out]).reshape(-1, 1)
    return pl.pallas_call(
        mlp_kernel,
        out_shape=[
            jax.ShapeDtypeStruct((outs * height, width), jnp.bfloat16),
            jax.ShapeDtypeStruct((height, width), jnp.float32),
        ],
        scratch_shapes=[pltpu.VMEM((outs * height, width), jnp.float32)],
        compiler_params=pltpu.CompilerParams(vmem_limit_bytes=16 * 1024 * 1024),
    )(fin, w_in.T, w_mid, w_top, w_out, biases)


def local(state, speed_x, speed_y, w_in, b_in, w_mid, b_mid, w_top, b_top, w_out, b_out, span_of):
    feats, height, breadth = state.shape
    across = np.kron(np.eye(breadth // NP, dtype=np.float32), TABLE.T)
    ahi_np = across.astype(jnp.bfloat16)
    alo_np = (across - ahi_np.astype(np.float32)).astype(jnp.bfloat16)
    mats = jnp.asarray(np.concatenate([ahi_np, alo_np], axis=0))
    speeds = jnp.broadcast_to(jnp.concatenate([speed_x, speed_y])[:, None], (2 * feats, breadth))
    v0 = state.reshape(feats * height, breadth)
    ex, ey = run_section(v0, None, speeds, mats, None, first=True, combo=None, edges=True)
    field = v0
    combos = [(None, None), (0.75, 0.25), ("third", None)]
    for k, combo in enumerate(combos):
        halos = exchange(ex, ey)
        extra = None
        if k == 2:
            biases = jnp.concatenate([b_in, b_mid, b_top, b_out]).reshape(-1, 1)
            extra = (w_in.T, w_mid, w_top, w_out, biases)
        outs = run_section(
            field, v0, speeds, mats, halos, first=False, combo=combo, edges=k < 2, mlp=extra
        )
        if k < 2:
            field, ex, ey = outs
        else:
            field, tend_rows, heat_rows = outs
    final_state = field.reshape(feats, height, breadth)
    column_count = height * breadth
    target = span_of.reshape(column_count)
    devices = lax.axis_size("face") * lax.axis_size("elem")
    span_ids = jnp.arange(devices, dtype=jnp.int32)
    heating = heat_rows.reshape(column_count)
    member = (target[:, None] == span_ids[None, :]).astype(jnp.float32)
    partial_sums = jnp.sum(member * heating[:, None], axis=0)
    received = lax.all_to_all(
        partial_sums.reshape(devices, 1), ("face", "elem"), 0, 1, tiled=True
    )
    span_heating = jnp.sum(received, axis=1) / column_count
    tendencies = tend_rows.reshape(-1, height, breadth)
    return (final_state, tendencies, span_heating)


def solution(mesh):
    return jax.shard_map(
        local,
        mesh=mesh,
        in_specs=(
            P(None, "face", "elem"),
            P(),
            P(),
            P(),
            P(),
            P(),
            P(),
            P(),
            P(),
            P(),
            P(),
            P("face", "elem", None, None),
        ),
        out_specs=(P(None, "face", "elem"), P(None, "face", "elem"), P(("face", "elem"))),
        check_vma=False,
    )
```

```python
import functools
import math

import jax
import jax.numpy as jnp
import numpy as np
from jax import lax
from jax.experimental import pallas as pl
from jax.experimental.pallas import tpu as pltpu
from jax.sharding import PartitionSpec as P

NP = 4
LEV = 72
CHUNK = 48
FOLD = CHUNK // 2


def gll_matrix():
    inner_node = 1.0 / math.sqrt(5.0)
    gll_nodes = np.array([-1.0, -inner_node, inner_node, 1.0])
    weights = np.array(
        [
            1.0
            / np.prod([gll_nodes[outer] - gll_nodes[other] for other in range(4) if other != outer])
            for outer in range(4)
        ]
    )
    matrix = np.zeros((4, 4))
    for outer in range(4):
        for inner in range(4):
            if inner != outer:
                matrix[outer, inner] = (
                    weights[inner] / weights[outer] / (gll_nodes[outer] - gll_nodes[inner])
                )
    for outer in range(4):
        matrix[outer, outer] = -np.sum(matrix[outer])
    return matrix.astype(np.float32)


TABLE = gll_matrix()


def lanes(shape):
    return lax.broadcasted_iota(jnp.int32, shape, len(shape) - 1)


def roll(x, shift):
    shift = shift % x.shape[-1]
    return x if shift == 0 else pltpu.roll(x, shift, x.ndim - 1)


def raw_slabs(slabs, sx, sy, ahi, alo):
    rows = slabs[0].shape[0]
    stacked = jnp.concatenate(slabs, axis=0)
    hi = stacked.astype(jnp.bfloat16)
    lo = (stacked - hi.astype(jnp.float32)).astype(jnp.bfloat16)
    along_x = (
        jnp.dot(hi, ahi, preferred_element_type=jnp.float32)
        + jnp.dot(hi, alo, preferred_element_type=jnp.float32)
        + jnp.dot(lo, ahi, preferred_element_type=jnp.float32)
    )
    out = []
    for y, _ in enumerate(slabs):
        base = (y // NP) * NP
        j = y % NP
        along_y = float(TABLE[j, 0]) * slabs[base]
        for i in range(1, NP):
            along_y = along_y + float(TABLE[j, i]) * slabs[base + i]
        dx = along_x[y * rows : (y + 1) * rows]
        out.append(-(sx * dx + sy * along_y))
    return out


def pack_edges(tend):
    rows, width = tend[0].shape
    lane = lanes((rows, width))
    acc = jnp.zeros((rows, width), jnp.float32)
    for y, t in enumerate(tend):
        acc = jnp.where(lane == 2 * y, roll(t, 2 * y), acc)
        acc = jnp.where(lane == 2 * y + 1, roll(t, 2 * y + 2), acc)
    half = rows // 2
    lane_h = lanes((half, width))
    return jnp.where(lane_h < 32, acc[:half], roll(acc[half:], 32))


def unpack_edges(block):
    return jnp.concatenate([block, roll(block, 96)], axis=0)


def stiff_x(t, right_edges, left_edges, y):
    rows, width = t.shape
    lane = lanes((rows, width))
    right = jnp.where(lane == width - 1, roll(right_edges, width - 1 - 2 * y), roll(t, width - 1))
    left = jnp.where(lane == 0, roll(left_edges, width - 1 - 2 * y), roll(t, 1))
    place = lane % NP
    return jnp.where(
        place == NP - 1, 0.5 * (t + right), jnp.where(place == 0, 0.5 * (left + t), t)
    )


def section_kernel(*refs, first, combo, edges, mlp, given):
    refs = list(refs)
    v0_ref = None if combo is None or combo[0] is None else refs.pop(0)
    sp_ref = refs.pop(0)
    sx_ref, sy_ref, ahi_ref, alo_ref = refs[:4]
    refs = refs[4:]
    if not first:
        exr_ref, exl_ref, dr_ref, dl_ref, top_ref, bottom_ref = refs[:6]
        refs = refs[6:]
    if given:
        t_in_ref = refs.pop(0)
    if mlp:
        mlp_in = refs[:5]
        refs = refs[5:]
    rows = CHUNK
    height = 16
    sx = sx_ref[...]
    sy = sy_ref[...]
    ahi = ahi_ref[...]
    alo = alo_ref[...]
    slabs = [sp_ref[pl.ds(y, rows, stride=height), :] for y in range(height)]
    if given:
        tend = [t_in_ref[pl.ds(y, rows, stride=height), :] for y in range(height)]
    else:
        tend = raw_slabs(slabs, sx, sy, ahi, alo)
    if first:
        ex_ref, ey_ref, t_out_ref = refs
        for y in range(height):
            t_out_ref[pl.ds(y, rows, stride=height), :] = tend[y]
        ex_ref[...] = pack_edges(tend)
        ey_ref[0] = tend[0]
        ey_ref[1] = tend[height - 1]
        return
    exr = unpack_edges(exr_ref[...])
    exl = unpack_edges(exl_ref[...])
    dr = unpack_edges(dr_ref[...])
    dl = unpack_edges(dl_ref[...])
    tx = [stiff_x(t, exr, exl, y) for y, t in enumerate(tend)]
    down = stiff_x(top_ref[...], dr, dl, 0)
    up = stiff_x(bottom_ref[...], dr, dl, height - 1)
    ext = [up] + tx + [down]
    new = []
    for y in range(height):
        cur = ext[y + 1]
        if y % NP == NP - 1:
            op = 0.5 * (cur + ext[y + 2])
        elif y % NP == 0:
            op = 0.5 * (ext[y] + cur)
        else:
            op = cur
        inner = slabs[y] + op
        if combo[0] is None:
            val = inner
        else:
            v0 = v0_ref[pl.ds(y, rows, stride=height), :]
            if combo[0] == "third":
                val = v0 / 3.0 + 2.0 / 3.0 * inner
            else:
                val = combo[0] * v0 + combo[1] * inner
        new.append(val)
    out_ref = refs[0]
    for y in range(height):
        out_ref[pl.ds(y, rows, stride=height), :] = new[y]
    if mlp:
        tend_ref, heat_ref, held, scratch = refs[1:5]
        step = pl.program_id(0)
        start = pl.multiple_of(step * rows, rows)
        for y in range(height):
            held[y, pl.ds(start, rows), :] = new[y]

        @pl.when(step == pl.num_programs(0) - 1)
        def _():
            mlp_body(lambda y: held[y], *mlp_in, tend_ref, heat_ref, scratch)
    if edges:
        ex_ref, ey_ref = refs[1:3]
        tend = raw_slabs(new, sx, sy, ahi, alo)
        ex_ref[...] = pack_edges(tend)
        ey_ref[0] = tend[0]
        ey_ref[1] = tend[height - 1]


def run_section(field_rows, v0, speeds, mats, halos, *, first, combo, edges, mlp=None, given=None):
    total, width = field_rows.shape
    feats = speeds.shape[0] // 2
    steps = feats // CHUNK
    big = pl.BlockSpec((CHUNK * 16, width), lambda i: (i, 0))
    small = pl.BlockSpec((CHUNK, width), lambda i: (i, 0))
    small_y = pl.BlockSpec((CHUNK, width), lambda i: (i + steps, 0))
    const = pl.BlockSpec((width, width), lambda i: (0, 0))
    const_lo = pl.BlockSpec((width, width), lambda i: (1, 0))
    edge = pl.BlockSpec((FOLD, width), lambda i: (i, 0))
    rowsb = pl.BlockSpec((2, CHUNK, width), lambda i: (0, i, 0))
    args, specs = [], []
    if combo is not None and combo[0] is not None:
        args.append(v0)
        specs.append(big)
    args += [field_rows, speeds, speeds, mats, mats]
    specs += [big, small, small_y, const, const_lo]
    if not first:
        exr, exl, corner_r, corner_l, rows = halos
        blocks = field_rows.shape[0] // (CHUNK * 16)
        args += [exr, exl, corner_r, corner_l, rows, rows]
        specs += [
            edge,
            edge,
            edge,
            edge,
            pl.BlockSpec((CHUNK, width), lambda i: (i, 0)),
            pl.BlockSpec((CHUNK, width), lambda i: (blocks + i, 0)),
        ]
    if given is not None:
        args.append(given)
        specs.append(big)
    out_shape, out_specs = [], []
    ex_shape = jax.ShapeDtypeStruct((feats // 2, width), jnp.float32)
    ey_shape = jax.ShapeDtypeStruct((2, feats, width), jnp.float32)
    if first:
        out_shape = [ex_shape, ey_shape, jax.ShapeDtypeStruct((total, width), jnp.float32)]
        out_specs = [edge, rowsb, big]
    else:
        out_shape = [jax.ShapeDtypeStruct((total, width), jnp.float32)]
        out_specs = [big]
        if edges:
            out_shape += [ex_shape, ey_shape]
            out_specs += [edge, rowsb]
    scratch_shapes = []
    limit = 16
    if mlp is not None:
        height = field_rows.shape[0] // feats
        outs = mlp[3].shape[0]
        whole = lambda a: pl.BlockSpec(a.shape, lambda i: (0,) * a.ndim)
        args += list(mlp)
        specs += [whole(a) for a in mlp]
        out_shape += [
            jax.ShapeDtypeStruct((outs * height, width), jnp.bfloat16),
            jax.ShapeDtypeStruct((height, width), jnp.float32),
        ]
        out_specs += [whole(out_shape[-2]), whole(out_shape[-1])]
        scratch_shapes = [
            pltpu.VMEM((height, feats, width), jnp.float32),
            pltpu.VMEM((outs * height, width), jnp.float32),
        ]
        limit = 32
    kernel = functools.partial(section_kernel, first=first, combo=combo, edges=edges, mlp=mlp is not None,
                               given=given is not None)
    return pl.pallas_call(
        kernel,
        grid=(steps,),
        in_specs=specs,
        out_specs=out_specs,
        out_shape=out_shape,
        scratch_shapes=scratch_shapes,
        compiler_params=pltpu.CompilerParams(vmem_limit_bytes=limit * 1024 * 1024),
    )(*args)


def exchange(ex, ey):
    n_face = lax.axis_size("face")
    n_elem = lax.axis_size("elem")
    assert n_face == 2
    from_right = [(j, (j - 1) % n_elem) for j in range(n_elem)]
    from_left = [(j, (j + 1) % n_elem) for j in range(n_elem)]
    exr = lax.ppermute(ex, "elem", from_right)
    exl = lax.ppermute(ex, "elem", from_left)
    feats = ey.shape[1]
    swap = [(0, 1), (1, 0)]
    rows = lax.ppermute(ey.reshape(2 * feats, ey.shape[2]), "face", swap)
    corner_r = lax.ppermute(exr, "face", swap)
    corner_l = lax.ppermute(exl, "face", swap)
    return (exr, exl, corner_r, corner_l, rows)


def column_model(inputs, w_in, b_in, w_mid, b_mid, w_top, b_top, w_out, b_out):
    hidden = jax.nn.silu(
        jnp.dot(w_in, inputs, preferred_element_type=jnp.float32) + b_in[:, None]
    ).astype(jnp.bfloat16)
    hidden = jax.nn.silu(
        jnp.dot(w_mid, hidden, preferred_element_type=jnp.float32) + b_mid[:, None]
    ).astype(jnp.bfloat16)
    hidden = jax.nn.silu(
        jnp.dot(w_top, hidden, preferred_element_type=jnp.float32) + b_top[:, None]
    ).astype(jnp.bfloat16)
    outputs = jnp.dot(w_out, hidden, preferred_element_type=jnp.float32) + b_out[:, None]
    heating = jnp.sum(outputs[:LEV], axis=0)
    return (outputs.astype(jnp.bfloat16), heating)


def mlp_kernel(fin_ref, w_in_ref, w_mid_ref, w_top_ref, w_out_ref, b_ref, tend_ref, heat_ref, scratch):
    feats = w_in_ref.shape[0]
    height = heat_ref.shape[0]
    mlp_body(
        lambda y: fin_ref[pl.ds(y, feats, stride=height), :],
        w_in_ref, w_mid_ref, w_top_ref, w_out_ref, b_ref, tend_ref, heat_ref, scratch,
    )


def mlp_body(slab, w_in_ref, w_mid_ref, w_top_ref, w_out_ref, b_ref, tend_ref, heat_ref, scratch):
    outs = w_out_ref.shape[0]
    height = heat_ref.shape[0]
    width = heat_ref.shape[1]

    def act(a):
        return (a * (0.5 + 0.5 * jnp.tanh(0.5 * a))).astype(jnp.bfloat16)

    hid = w_mid_ref.shape[0]
    b_in = b_ref[0:hid]
    b_mid = b_ref[hid : 2 * hid]
    b_top = b_ref[2 * hid : 3 * hid]
    b_out = b_ref[3 * hid : 3 * hid + outs]

    for pair in range(height // 2):
        y = 2 * pair
        x = jnp.concatenate([slab(y), slab(y + 1)], axis=1).astype(jnp.bfloat16)
        h = act(
            lax.dot_general(
                w_in_ref[...], x, (((0,), (0,)), ((), ())), preferred_element_type=jnp.float32
            )
            + b_in
        )
        h = act(jnp.dot(w_mid_ref[...], h, preferred_element_type=jnp.float32) + b_mid)
        h = act(jnp.dot(w_top_ref[...], h, preferred_element_type=jnp.float32) + b_top)
        out = jnp.dot(w_out_ref[...], h, preferred_element_type=jnp.float32) + b_out
        heat = jnp.sum(out[:LEV], axis=0, keepdims=True)
        heat_ref[y : y + 1, :] = heat[:, :width]
        heat_ref[y + 1 : y + 2, :] = heat[:, width:]
        scratch[pl.ds(y, outs, stride=height), :] = out[:, :width]
        scratch[pl.ds(y + 1, outs, stride=height), :] = out[:, width:]
    tend_ref[...] = scratch[...].astype(jnp.bfloat16)


def run_mlp(fin, height, w_in, b_in, w_mid, b_mid, w_top, b_top, w_out, b_out):
    width = fin.shape[1]
    outs = w_out.shape[0]
    biases = jnp.concatenate([b_in, b_mid, b_top, b_out]).reshape(-1, 1)
    return pl.pallas_call(
        mlp_kernel,
        out_shape=[
            jax.ShapeDtypeStruct((outs * height, width), jnp.bfloat16),
            jax.ShapeDtypeStruct((height, width), jnp.float32),
        ],
        scratch_shapes=[pltpu.VMEM((outs * height, width), jnp.float32)],
        compiler_params=pltpu.CompilerParams(vmem_limit_bytes=16 * 1024 * 1024),
    )(fin, w_in.T, w_mid, w_top, w_out, biases)


def local(state, speed_x, speed_y, w_in, b_in, w_mid, b_mid, w_top, b_top, w_out, b_out, span_of):
    feats, height, breadth = state.shape
    across = np.kron(np.eye(breadth // NP, dtype=np.float32), TABLE.T)
    ahi_np = across.astype(jnp.bfloat16)
    alo_np = (across - ahi_np.astype(np.float32)).astype(jnp.bfloat16)
    mats = jnp.asarray(np.concatenate([ahi_np, alo_np], axis=0))
    speeds = jnp.broadcast_to(jnp.concatenate([speed_x, speed_y])[:, None], (2 * feats, breadth))
    v0 = state.reshape(feats * height, breadth)
    ex, ey, tend0 = run_section(v0, None, speeds, mats, None, first=True, combo=None, edges=True)
    field = v0
    combos = [(None, None), (0.75, 0.25), ("third", None)]
    for k, combo in enumerate(combos):
        halos = exchange(ex, ey)
        extra = None
        if k == 2:
            biases = jnp.concatenate([b_in, b_mid, b_top, b_out]).reshape(-1, 1)
            extra = (w_in.T, w_mid, w_top, w_out, biases)
        outs = run_section(
            field, v0, speeds, mats, halos, first=False, combo=combo, edges=k < 2, mlp=extra,
            given=tend0 if k == 0 else None,
        )
        if k < 2:
            field, ex, ey = outs
        else:
            field, tend_rows, heat_rows = outs
    final_state = field.reshape(feats, height, breadth)
    column_count = height * breadth
    target = span_of.reshape(column_count)
    devices = lax.axis_size("face") * lax.axis_size("elem")
    span_ids = jnp.arange(devices, dtype=jnp.int32)
    heating = heat_rows.reshape(column_count)
    member = (target[:, None] == span_ids[None, :]).astype(jnp.float32)
    partial_sums = jnp.sum(member * heating[:, None], axis=0)
    received = lax.all_to_all(
        partial_sums.reshape(devices, 1), ("face", "elem"), 0, 1, tiled=True
    )
    span_heating = jnp.sum(received, axis=1) / column_count
    tendencies = tend_rows.reshape(-1, height, breadth)
    return (final_state, tendencies, span_heating)


def solution(mesh):
    return jax.shard_map(
        local,
        mesh=mesh,
        in_specs=(
            P(None, "face", "elem"),
            P(),
            P(),
            P(),
            P(),
            P(),
            P(),
            P(),
            P(),
            P(),
            P(),
            P("face", "elem", None, None),
        ),
        out_specs=(P(None, "face", "elem"), P(None, "face", "elem"), P(("face", "elem"))),
        check_vma=False,
    )
```
